32 devices in a mesh: group: 2 (over y), ctx: 4 (over z), chan: 4 (over x, core).
Axes of the slice: x: 2, y: 2, z: 4, core: 2. Of those that a mesh axis runs over, the one named last changes fastest.
Arguments:
- short_proj: bfloat16 [3, 1024, 4096], P(None, ('group', 'ctx'), 'chan'), parts along dimension 1, may hold values from -6 to 6
- medium_proj: bfloat16 [3, 1024, 4096], P(None, ('group', 'ctx'), 'chan'), parts along dimension 1, may hold values from -6 to 6
- long_proj: bfloat16 [3, 1024, 4096], P(None, ('group', 'ctx'), 'chan'), parts along dimension 1, may hold values from -6 to 6
- feature_taps: bfloat16 [3, 3, 3, 4096], P(None, None, None, 'chan'), may hold values from -3.5 to 3.5
- short_taps: bfloat16 [7, 256], P(None, 'chan'), may hold values from -2 to 2
- medium_taps: bfloat16 [256, 128], P('chan'), may hold values from -0.5 to 0.5
- long_rates: float32 [256, 16], P('chan'), may hold values from 0 to 0.035, as said below
- long_residues: float32 [256, 16], P('chan'), may hold values from -1.5 to 1.5
Outputs:
- short_mixed: bfloat16 [1024, 4096], P(('group', 'ctx'), 'chan'), parts along dimension 0
- medium_mixed: bfloat16 [1024, 4096], P(('group', 'ctx'), 'chan'), parts along dimension 0
- long_mixed: bfloat16 [1024, 4096], P(('group', 'ctx'), 'chan'), parts along dimension 0
The draws below stay inside these ranges and needn't reach their ends.
There are 2 independent parts, one for each index of `group`. The reference program is written for one: setup_inputs(seed, part) draws one part's arguments, and reference() takes and returns one part's arrays. A program takes and returns all parts, laid end to end along the dimension named above; an argument that names none is the same for every part. Nothing has to cross between parts.
Inputs may be any that keep to these rules, and one draw needn't show every extreme that they name: `long_rates`: every rate is positive.
All inputs are finite; a program needn't handle non-finite values.
Results may differ from the reference program's by a relative error of at most 0.0054.
Values may be sent and summed in bfloat16 or wider, within the bound.
No kernel may reach another device: no remote copies, remote signals or barrier semaphores. Data moves between devices by JAX's collectives and lax.ppermute only.
A program may use at most 192 MiB of HBM per device.

```python
import jax
import jax.numpy as jnp
from jax import lax

CHANNELS = 4096
GROUP_SIZE = 16
MODES = 16
FEAT_TAPS = 3
SHORT_TAPS = 7
MEDIUM_TAPS = 128
GROUPS = 256
LOOP = 512


def draw_long_rates(key, part):
    pick_key, slow_key, fast_key = jax.random.split(key, 3)
    slow_share = 0.5
    slow_mask = jax.random.bernoulli(pick_key, slow_share, (GROUPS, MODES))
    slow_rates = jax.random.uniform(slow_key, (GROUPS, MODES), jnp.float32, 0.1, 2.0) / LOOP
    fast_rates = jax.random.uniform(fast_key, (GROUPS, MODES), jnp.float32, 1.0 / 50.0, 1.0 / 30.0)
    return jnp.where(slow_mask, slow_rates, fast_rates)


def levels(key, extent, shards, least, high):
    def one(axis_at, parts):
        draws = jax.random.uniform(jax.random.fold_in(jax.random.fold_in(key, 6), axis_at), (parts,), jnp.float32, least / len(shards), high / len(shards))
        return jnp.repeat(jnp.exp(draws), extent[axis_at] // parts).reshape((-1,) + (1,) * (len(extent) - axis_at - 1))

    factor_of = one(*shards[0])
    for cut in shards[1:]:
        factor_of = factor_of * one(*cut)
    return factor_of


def normal_values(key, shape, width, limit, shards=(), dtype=jnp.bfloat16):
    values = jax.random.normal(key, shape, jnp.float32) * width
    if len(shards) > 0:
        values = levels(key, shape, shards, -0.22, 0.18) * values
    return jnp.clip(values, min=-limit, max=limit).astype(dtype)


def setup_inputs(seed: int = 0, part: int = 0) -> dict:
    seeds = jax.random.split(jax.random.key(seed), 9)
    part_splits = jax.random.split(jax.random.fold_in(seeds[8], part), 9)
    return {
        "short_proj": normal_values(part_splits[0], (3, LOOP, CHANNELS), 1.0, 6.0, ((1, 4), (2, 4))),
        "medium_proj": normal_values(part_splits[1], (3, LOOP, CHANNELS), 1.0, 6.0, ((1, 4), (2, 4))),
        "long_proj": normal_values(part_splits[2], (3, LOOP, CHANNELS), 1.0, 6.0, ((1, 4), (2, 4))),
        "feature_taps": normal_values(seeds[3], (3, 3, FEAT_TAPS, CHANNELS), FEAT_TAPS ** -0.5, 3.5, ((3, 4),)),
        "short_taps": normal_values(seeds[4], (SHORT_TAPS, GROUPS), SHORT_TAPS ** -0.5, 2.0, ((1, 4),)),
        "medium_taps": normal_values(seeds[5], (GROUPS, MEDIUM_TAPS), MEDIUM_TAPS ** -0.5, 0.5, ((0, 4),)),
        "long_rates": draw_long_rates(jax.random.fold_in(seeds[8], 71), part),
        "long_residues": normal_values(seeds[7], (GROUPS, MODES), 0.25, 1.5, ((0, 4),), jnp.float32),
    }


def featurize(projected, filter_taps):
    source = projected.astype(jnp.float32)
    weights = filter_taps.astype(jnp.float32)
    result = weights[:, 0][:, None, :] * source
    for offset in range(1, FEAT_TAPS):
        result = result + weights[:, offset][:, None, :] * jnp.roll(source, offset, axis=1)
    return result

def short_filter(product, group_taps):
    columns = jnp.repeat(group_taps.astype(jnp.float32), GROUP_SIZE, axis=1)
    source = product.astype(jnp.float32)
    result = columns[0] * source
    for offset in range(1, SHORT_TAPS):
        result = result + columns[offset] * jnp.roll(source, offset, axis=0)
    return result

def medium_filter(product, group_taps):
    columns = jnp.repeat(group_taps.astype(jnp.float32), GROUP_SIZE, axis=0)
    source = product.astype(jnp.float32)

    def accumulate(offset, running):
        weight_row = lax.dynamic_index_in_dim(columns, offset, 1, keepdims=False)
        return running + weight_row * jnp.roll(source, offset, axis=0)
    return lax.fori_loop(0, MEDIUM_TAPS, accumulate, jnp.zeros_like(source))

def long_filter(product, long_rates, long_residues):
    channel_rates = jnp.repeat(long_rates, GROUP_SIZE, axis=0)
    residues = jnp.repeat(long_residues, GROUP_SIZE, axis=0)
    wrap_scale = -jnp.expm1(-channel_rates * LOOP)
    mode_gains = residues * jnp.sqrt(-jnp.expm1(-2.0 * channel_rates) * wrap_scale / (1.0 + jnp.exp(-channel_rates * LOOP)))
    step_decay = jnp.exp(-channel_rates)
    source = product.astype(jnp.float32)

    def advance(current, column):
        current = step_decay * current + column[:, None]
        return (current, lax.optimization_barrier(jnp.sum(mode_gains * current, axis=1)))
    final_state, unused = lax.scan(advance, jnp.zeros_like(channel_rates), source)
    steady, outputs = lax.scan(advance, final_state / wrap_scale, source)
    return outputs

def reference(short_proj, medium_proj, long_proj, feature_taps, short_taps, medium_taps, long_rates, long_residues):
    short_feat = featurize(short_proj, feature_taps[0])
    short_product = (short_feat[1] * short_feat[2]).astype(jnp.bfloat16)
    short_mixed = (short_feat[0] * short_filter(short_product, short_taps)).astype(jnp.bfloat16)
    medium_feat = featurize(medium_proj, feature_taps[1])
    medium_product = (medium_feat[1] * medium_feat[2]).astype(jnp.bfloat16)
    medium_mixed = (medium_feat[0] * medium_filter(medium_product, medium_taps)).astype(jnp.bfloat16)
    long_feat = featurize(long_proj, feature_taps[2])
    long_product = (long_feat[1] * long_feat[2]).astype(jnp.bfloat16)
    long_mixed = (long_feat[0] * long_filter(long_product, long_rates, long_residues)).astype(jnp.bfloat16)
    return (short_mixed, medium_mixed, long_mixed)
```

```python
import functools

import jax
import jax.numpy as jnp
from jax import lax
from jax.experimental import pallas as pl
from jax.experimental.pallas import tpu as pltpu
from jax.sharding import PartitionSpec as P

f32 = jnp.float32
bf16 = jnp.bfloat16
TILE = 128


def shifted(block, axis, distance):
    size = lax.axis_size(axis)
    route = [((i - distance) % size, i) for i in range(size)]
    return lax.ppermute(block, axis, route)


def split_bf16(x):
    hi = x.astype(bf16)
    return hi, (x - hi.astype(f32)).astype(bf16)


def feature_rows(proj_ref, rim_ref, ft_ref, operator, branch, index, lookback):
    src = proj_ref[index].astype(f32)
    number = operator * 3 + branch
    row = lax.broadcasted_iota(jnp.int32, src.shape, 0)
    result = ft_ref[pl.ds(number * (lookback + 1), 1), :] * src
    for back in range(1, lookback + 1):
        moved = pltpu.roll(src, back, 0)
        for t in range(back):
            rim_row = rim_ref[pl.ds(number * lookback + lookback + t - back, 1), :].astype(f32)
            moved = jnp.where(row == t, rim_row, moved)
        result = result + ft_ref[pl.ds(number * (lookback + 1) + back, 1), :] * moved
    return result


def toeplitz_kernel(bm_ref, bl_ref, tm_ref, tlh_ref, tll_ref):
    per = bm_ref.shape[0]
    rows = tm_ref.shape[1]
    width = bm_ref.shape[1]
    for gl in range(per):
        base = jnp.broadcast_to(bm_ref[pl.ds(gl, 1), :], (rows, width))
        tm_ref[gl] = pltpu.roll(base, 0, 1, stride=1, stride_axis=0).astype(bf16)
        base = jnp.broadcast_to(bl_ref[pl.ds(gl, 1), :], (rows, width))
        full = pltpu.roll(base, 0, 1, stride=1, stride_axis=0)[:, :rows]
        hi, lo = split_bf16(full)
        tlh_ref[gl] = hi
        tll_ref[gl] = lo


def features_kernel(sp_ref, mp_ref, lp_ref, rim_ref, ft_ref, wsh_ref, wsl_ref,
                    zs_ref, zm_ref, zl_ref, tail_ref, state_ref, *, lookback, modes, group_width):
    products = []
    for operator, proj_ref in enumerate((sp_ref, mp_ref, lp_ref)):
        k_feat = feature_rows(proj_ref, rim_ref, ft_ref, operator, 1, 1, lookback)
        v_feat = feature_rows(proj_ref, rim_ref, ft_ref, operator, 2, 2, lookback)
        products.append((k_feat * v_feat).astype(bf16))
    zs, zm, zl = products
    length = zs.shape[0]
    zs_ref[...] = zs
    zm_ref[...] = zm
    zl_ref[...] = zl
    tail_ref[pl.ds(0, length), :] = zm
    tail_ref[pl.ds(length, 16), :] = zs[length - 16:, :]
    full = jnp.dot(wsh_ref[...], zl, preferred_element_type=f32) + jnp.dot(
        wsl_ref[...], zl, preferred_element_type=f32
    )
    rows = lax.broadcasted_iota(jnp.int32, full.shape, 0) // modes
    lanes = lax.broadcasted_iota(jnp.int32, full.shape, 1) // group_width
    full = jnp.where(rows == lanes, full, 0.0)
    state = full[0:modes, :]
    for gl in range(1, full.shape[0] // modes):
        state = state + full[gl * modes:(gl + 1) * modes, :]
    state_ref[...] = state


def mix_kernel(sq_ref, mq_ref, lq_ref, rim_ref, ft_ref, zs_ref, zm_ref, zl_ref, tail_ref, st_ref,
               tm_ref, tlh_ref, tll_ref, ech_ref, ecl_ref, inc_ref,
               so_ref, mo_ref, lo_ref, y_scr, zext_scr, *, lookback, modes, group_width):
    length, lanes_n = zs_ref.shape
    per = lanes_n // group_width
    row = lax.broadcasted_iota(jnp.int32, (length, lanes_n), 0)
    lane_group = lax.broadcasted_iota(jnp.int32, (length, lanes_n), 1) // group_width
    queries = [
        feature_rows(ref, rim_ref, ft_ref, operator, 0, 0, lookback)
        for operator, ref in enumerate((sq_ref, mq_ref, lq_ref))
    ]

    zs = zs_ref[...].astype(f32)
    y_scr[...] = zs
    y_scr[pl.ds(length - 16, 16), :] = tail_ref[pl.ds(length, 16), :].astype(f32)
    wrapped = y_scr[...]
    conv = st_ref[pl.ds(0, 1), :] * zs
    for j in range(1, st_ref.shape[0]):
        back = jnp.where(row < j, pltpu.roll(wrapped, j, 0), pltpu.roll(zs, j, 0))
        conv = conv + st_ref[pl.ds(j, 1), :] * back
    so_ref[...] = (queries[0] * conv).astype(so_ref.dtype)

    zext_scr[pl.ds(0, length), :] = tail_ref[pl.ds(0, length), :]
    zext_scr[pl.ds(length, length), :] = zm_ref[...]
    zext = zext_scr[...]
    acc = jnp.zeros((length, lanes_n), f32)
    for gl in range(per):
        part = jnp.dot(tm_ref[gl], zext, preferred_element_type=f32)
        acc = jnp.where(lane_group == gl, part, acc)
    mo_ref[...] = (queries[1] * acc).astype(mo_ref.dtype)

    zl = zl_ref[...]
    acc = jnp.zeros((length, lanes_n), f32)
    for gl in range(per):
        part = jnp.dot(tlh_ref[gl], zl, preferred_element_type=f32) + jnp.dot(
            tll_ref[gl], zl, preferred_element_type=f32
        )
        acc = jnp.where(lane_group == gl, part, acc)
    incoming = inc_ref[...]
    stacked = jnp.concatenate([incoming] * per, axis=0)
    srow = lax.broadcasted_iota(jnp.int32, stacked.shape, 0) // modes
    slane = lax.broadcasted_iota(jnp.int32, stacked.shape, 1) // group_width
    stacked = jnp.where(srow == slane, stacked, 0.0)
    ih, il = split_bf16(stacked)
    eh = ech_ref[...]
    el = ecl_ref[...]
    carried = (
        jnp.dot(eh, ih, preferred_element_type=f32)
        + jnp.dot(eh, il, preferred_element_type=f32)
        + jnp.dot(el, ih, preferred_element_type=f32)
    )
    lo_ref[...] = (queries[2] * (acc + carried)).astype(lo_ref.dtype)


def on_device(short_proj, medium_proj, long_proj, feature_taps, short_taps, medium_taps,
              long_rates, long_residues):
    _, length, channels = short_proj.shape
    groups, modes = long_rates.shape
    group_width = channels // groups
    lookback = feature_taps.shape[2] - 1
    reach = medium_taps.shape[1]
    short_count = short_taps.shape[0]
    assert reach <= length and short_count <= 17 and lookback < length
    blocks = lax.axis_size("ctx")
    position = lax.axis_index("ctx")
    per = TILE // group_width
    tiles = channels // TILE
    projs = (short_proj, medium_proj, long_proj)

    rims = jnp.concatenate(
        [p[:, length - lookback:].reshape(3 * lookback, channels) for p in projs], axis=0
    )
    arrived = shifted(rims, "ctx", 1)

    ft = feature_taps.astype(f32).reshape(-1, channels)
    st = jnp.repeat(short_taps.astype(f32), group_width, axis=1)
    bm = jnp.concatenate(
        [
            jnp.zeros((groups, length - reach + 1), f32),
            medium_taps.astype(f32)[:, ::-1],
            jnp.zeros((groups, length - 1), f32),
        ],
        axis=1,
    )
    rates = long_rates
    loop_length = length * blocks
    wrap_scale = -jnp.expm1(-rates * loop_length)
    gains = long_residues * jnp.sqrt(
        -jnp.expm1(-2.0 * rates) * wrap_scale / (1.0 + jnp.exp(-rates * loop_length))
    )
    offsets = jnp.arange(length, dtype=f32)
    profile = jnp.sum(gains[:, :, None] * jnp.exp(-rates[:, :, None] * offsets), axis=1)
    bl = jnp.concatenate(
        [profile[:, :1], jnp.zeros((groups, length), f32), profile[:, :0:-1]], axis=1
    )
    to_end = jnp.exp(-rates[:, :, None] * (length - 1.0 - offsets)).reshape(groups * modes, length)
    wsh, wsl = split_bf16(to_end)
    starts = (gains[None] * jnp.exp(-rates[None] * (offsets + 1.0)[:, None, None])).reshape(
        length, groups * modes
    )
    ech, ecl = split_bf16(starts)

    tm, tlh, tll = pl.pallas_call(
        toeplitz_kernel,
        grid=(tiles,),
        in_specs=[pl.BlockSpec((per, 2 * length), lambda j: (j, 0))] * 2,
        out_specs=[
            pl.BlockSpec((per, length, 2 * length), lambda j: (j, 0, 0)),
            pl.BlockSpec((per, length, length), lambda j: (j, 0, 0)),
            pl.BlockSpec((per, length, length), lambda j: (j, 0, 0)),
        ],
        out_shape=[
            jax.ShapeDtypeStruct((groups, length, 2 * length), bf16),
            jax.ShapeDtypeStruct((groups, length, length), bf16),
            jax.ShapeDtypeStruct((groups, length, length), bf16),
        ],
    )(bm, bl)

    lane_block = lambda rows: pl.BlockSpec((rows, TILE), lambda j: (0, j))
    proj_block = pl.BlockSpec((3, length, TILE), lambda j: (0, 0, j))
    zs, zm, zl, tail, state = pl.pallas_call(
        functools.partial(
            features_kernel, lookback=lookback, modes=modes, group_width=group_width
        ),
        grid=(tiles,),
        in_specs=[
            proj_block,
            proj_block,
            proj_block,
            lane_block(rims.shape[0]),
            lane_block(ft.shape[0]),
            pl.BlockSpec((per * modes, length), lambda j: (j, 0)),
            pl.BlockSpec((per * modes, length), lambda j: (j, 0)),
        ],
        out_specs=[
            lane_block(length),
            lane_block(length),
            lane_block(length),
            lane_block(length + 16),
            lane_block(modes),
        ],
        out_shape=[
            jax.ShapeDtypeStruct((length, channels), bf16),
            jax.ShapeDtypeStruct((length, channels), bf16),
            jax.ShapeDtypeStruct((length, channels), bf16),
            jax.ShapeDtypeStruct((length + 16, channels), bf16),
            jax.ShapeDtypeStruct((modes, channels), f32),
        ],
    )(short_proj, medium_proj, long_proj, arrived, ft, wsh, wsl)

    tail_in = shifted(tail, "ctx", 1)
    if blocks <= 8:
        stack = jnp.stack([shifted(state, "ctx", k) for k in range(1, blocks)] + [state])
        powers = jnp.arange(blocks, dtype=f32)
    else:
        stack = lax.all_gather(state, "ctx")
        powers = ((position - 1 - jnp.arange(blocks)) % blocks).astype(f32)
    rate_c = jnp.repeat(rates.T, group_width, axis=1)
    wrap_c = jnp.repeat(wrap_scale.T, group_width, axis=1)
    incoming = (
        jnp.sum(jnp.exp(-rate_c[None] * (length * powers)[:, None, None]) * stack, axis=0)
        / wrap_c
    )

    query_block = pl.BlockSpec((1, length, TILE), lambda j: (0, 0, j))
    outs = pl.pallas_call(
        functools.partial(mix_kernel, lookback=lookback, modes=modes, group_width=group_width),
        grid=(tiles,),
        in_specs=[
            query_block,
            query_block,
            query_block,
            lane_block(rims.shape[0]),
            lane_block(ft.shape[0]),
            lane_block(length),
            lane_block(length),
            lane_block(length),
            lane_block(length + 16),
            lane_block(short_count),
            pl.BlockSpec((per, length, 2 * length), lambda j: (j, 0, 0)),
            pl.BlockSpec((per, length, length), lambda j: (j, 0, 0)),
            pl.BlockSpec((per, length, length), lambda j: (j, 0, 0)),
            pl.BlockSpec((length, per * modes), lambda j: (0, j)),
            pl.BlockSpec((length, per * modes), lambda j: (0, j)),
            lane_block(modes),
        ],
        out_specs=[lane_block(length)] * 3,
        out_shape=[jax.ShapeDtypeStruct((length, channels), bf16)] * 3,
        scratch_shapes=[
            pltpu.VMEM((length, TILE), f32),
            pltpu.VMEM((2 * length, TILE), bf16),
        ],
    )(short_proj, medium_proj, long_proj, arrived, ft, zs, zm, zl, tail_in, st,
      tm, tlh, tll, ech, ecl, incoming)
    return tuple(outs)


def solution(mesh):
    return jax.shard_map(
        on_device,
        mesh=mesh,
        in_specs=(
            P(None, ("group", "ctx"), "chan"),
            P(None, ("group", "ctx"), "chan"),
            P(None, ("group", "ctx"), "chan"),
            P(None, None, None, "chan"),
            P(None, "chan"),
            P("chan", None),
            P("chan", None),
            P("chan", None),
        ),
        out_specs=(
            P(("group", "ctx"), "chan"),
            P(("group", "ctx"), "chan"),
            P(("group", "ctx"), "chan"),
        ),
        check_vma=False,
    )
```

```python
import functools

import jax
import jax.numpy as jnp
from jax import lax
from jax.experimental import pallas as pl
from jax.experimental.pallas import tpu as pltpu
from jax.sharding import PartitionSpec as P

f32 = jnp.float32
bf16 = jnp.bfloat16
TILE = 128
BLOCK = 512


def shifted(block, axis, distance):
    size = lax.axis_size(axis)
    route = [((i - distance) % size, i) for i in range(size)]
    return lax.ppermute(block, axis, route)


def split_bf16(x):
    hi = x.astype(bf16)
    return hi, (x - hi.astype(f32)).astype(bf16)


def split_glue(x):
    hi = lax.reduce_precision(x, exponent_bits=8, mantissa_bits=7)
    return hi.astype(bf16), (x - hi).astype(bf16)


def feature_rows(proj_ref, rim_ref, ft_ref, lanes, operator, branch, index, lookback):
    src = proj_ref[index, :, lanes].astype(f32)
    number = operator * 3 + branch
    row = lax.broadcasted_iota(jnp.int32, src.shape, 0)
    result = ft_ref[pl.ds(number * (lookback + 1), 1), lanes] * src
    for back in range(1, lookback + 1):
        moved = pltpu.roll(src, back, 0)
        for t in range(back):
            rim_row = rim_ref[pl.ds(number * lookback + lookback + t - back, 1), lanes]
            moved = jnp.where(row == t, rim_row.astype(f32), moved)
        result = result + ft_ref[pl.ds(number * (lookback + 1) + back, 1), lanes] * moved
    return result


def toeplitz_kernel(bm_ref, bl_ref, after_ref, tm_ref, tlh_ref, tll_ref):
    per = bm_ref.shape[0]
    rows = tm_ref.shape[1]
    width = bm_ref.shape[1]
    for gl in range(per):
        base = jnp.broadcast_to(bm_ref[pl.ds(gl, 1), :], (rows, width))
        tm_ref[gl] = pltpu.roll(base, 0, 1, stride=1, stride_axis=0).astype(bf16)
        base = jnp.broadcast_to(bl_ref[pl.ds(gl, 1), :], (rows, width))
        full = pltpu.roll(base, 0, 1, stride=1, stride_axis=0)[:, :rows]
        hi, lo = split_bf16(full)
        tlh_ref[gl] = hi
        tll_ref[gl] = lo


def features_kernel(sp_ref, mp_ref, lp_ref, rim_ref, ft_ref, wsh_ref, wsl_ref,
                    zs_ref, zm_ref, zl_ref, tail_ref, state_ref, *, lookback, modes, group_width):
    length = zs_ref.shape[0]
    rows_per = TILE // group_width * modes
    for sub in range(zs_ref.shape[1] // TILE):
        lanes = pl.ds(sub * TILE, TILE)
        products = []
        for operator, proj_ref in enumerate((sp_ref, mp_ref, lp_ref)):
            k_feat = feature_rows(proj_ref, rim_ref, ft_ref, lanes, operator, 1, 1, lookback)
            v_feat = feature_rows(proj_ref, rim_ref, ft_ref, lanes, operator, 2, 2, lookback)
            products.append((k_feat * v_feat).astype(bf16))
        zs, zm, zl = products
        zs_ref[:, lanes] = zs
        zm_ref[:, lanes] = zm
        zl_ref[:, lanes] = zl
        tail_ref[pl.ds(0, length), lanes] = zm
        tail_ref[pl.ds(length, 16), lanes] = zs[length - 16:, :]
        weights = pl.ds(sub * rows_per, rows_per)
        full = jnp.dot(wsh_ref[weights, :], zl, preferred_element_type=f32) + jnp.dot(
            wsl_ref[weights, :], zl, preferred_element_type=f32
        )
        rows = lax.broadcasted_iota(jnp.int32, full.shape, 0) // modes
        lane_group = lax.broadcasted_iota(jnp.int32, full.shape, 1) // group_width
        full = jnp.where(rows == lane_group, full, 0.0)
        state = full[0:modes, :]
        for gl in range(1, rows_per // modes):
            state = state + full[gl * modes:(gl + 1) * modes, :]
        state_ref[:, lanes] = state
        hi, lo = split_bf16(state)
        tail_ref[pl.ds(length + 16, modes), lanes] = hi
        tail_ref[pl.ds(length + 16 + modes, modes), lanes] = lo


def mix_kernel(sq_ref, mq_ref, lq_ref, rim_ref, ft_ref, zs_ref, zm_ref, zl_ref, tail_ref, st_ref,
               tm_ref, tlh_ref, tll_ref, ech_ref, ecl_ref, inc_ref,
               so_ref, mo_ref, lo_ref, y_scr, zext_scr, *, lookback, modes, group_width):
    length = zs_ref.shape[0]
    per = TILE // group_width
    row = lax.broadcasted_iota(jnp.int32, (length, TILE), 0)
    lane_group = lax.broadcasted_iota(jnp.int32, (length, TILE), 1) // group_width
    for sub in range(zs_ref.shape[1] // TILE):
        lanes = pl.ds(sub * TILE, TILE)
        queries = [
            feature_rows(ref, rim_ref, ft_ref, lanes, operator, 0, 0, lookback)
            for operator, ref in enumerate((sq_ref, mq_ref, lq_ref))
        ]

        zs = zs_ref[:, lanes].astype(f32)
        y_scr[...] = zs
        y_scr[pl.ds(length - 16, 16), :] = tail_ref[pl.ds(length, 16), lanes].astype(f32)
        wrapped = y_scr[...]
        conv = st_ref[pl.ds(0, 1), lanes] * zs
        for j in range(1, st_ref.shape[0]):
            back = jnp.where(row < j, pltpu.roll(wrapped, j, 0), pltpu.roll(zs, j, 0))
            conv = conv + st_ref[pl.ds(j, 1), lanes] * back
        so_ref[:, lanes] = (queries[0] * conv).astype(so_ref.dtype)

        zext_scr[pl.ds(0, length), :] = tail_ref[pl.ds(0, length), lanes]
        zext_scr[pl.ds(length, length), :] = zm_ref[:, lanes]
        zext = zext_scr[...]
        acc = jnp.zeros((length, TILE), f32)
        for gl in range(per):
            part = jnp.dot(tm_ref[sub * per + gl], zext, preferred_element_type=f32)
            acc = jnp.where(lane_group == gl, part, acc)
        mo_ref[:, lanes] = (queries[1] * acc).astype(mo_ref.dtype)

        zl = zl_ref[:, lanes]
        acc = jnp.zeros((length, TILE), f32)
        for gl in range(per):
            part = jnp.dot(tlh_ref[sub * per + gl], zl, preferred_element_type=f32) + jnp.dot(
                tll_ref[sub * per + gl], zl, preferred_element_type=f32
            )
            acc = jnp.where(lane_group == gl, part, acc)
        incoming = inc_ref[:, lanes]
        stacked = jnp.concatenate([incoming] * per, axis=0)
        srow = lax.broadcasted_iota(jnp.int32, stacked.shape, 0) // modes
        slane = lax.broadcasted_iota(jnp.int32, stacked.shape, 1) // group_width
        stacked = jnp.where(srow == slane, stacked, 0.0)
        ih, il = split_bf16(stacked)
        eh = ech_ref[:, lanes]
        el = ecl_ref[:, lanes]
        carried = (
            jnp.dot(eh, ih, preferred_element_type=f32)
            + jnp.dot(eh, il, preferred_element_type=f32)
            + jnp.dot(el, ih, preferred_element_type=f32)
        )
        lo_ref[:, lanes] = (queries[2] * (acc + carried)).astype(lo_ref.dtype)


def on_device(short_proj, medium_proj, long_proj, feature_taps, short_taps, medium_taps,
              long_rates, long_residues):
    _, length, channels = short_proj.shape
    groups, modes = long_rates.shape
    group_width = channels // groups
    lookback = feature_taps.shape[2] - 1
    reach = medium_taps.shape[1]
    short_count = short_taps.shape[0]
    assert reach <= length and short_count <= 17 and lookback < length
    blocks = lax.axis_size("ctx")
    position = lax.axis_index("ctx")
    width = min(BLOCK, channels)
    steps = channels // width
    gpb = width // group_width
    projs = (short_proj, medium_proj, long_proj)

    rims = jnp.concatenate(
        [p[:, length - lookback:].reshape(3 * lookback, channels) for p in projs], axis=0
    )
    arrived = shifted(rims, "ctx", 1)

    ft = feature_taps.astype(f32).reshape(-1, channels)
    st = jnp.repeat(short_taps.astype(f32), group_width, axis=1)
    bm = jnp.concatenate(
        [
            jnp.zeros((groups, length - reach + 1), f32),
            medium_taps.astype(f32)[:, ::-1],
            jnp.zeros((groups, length - 1), f32),
        ],
        axis=1,
    )
    rates = long_rates
    loop_length = length * blocks
    wrap_scale = -jnp.expm1(-rates * loop_length)
    gains = long_residues * jnp.sqrt(
        -jnp.expm1(-2.0 * rates) * wrap_scale / (1.0 + jnp.exp(-rates * loop_length))
    )
    offsets = jnp.arange(length, dtype=f32)
    profile = jnp.sum(gains[:, :, None] * jnp.exp(-rates[:, :, None] * offsets), axis=1)
    bl = jnp.concatenate(
        [profile[:, :1], jnp.zeros((groups, length), f32), profile[:, :0:-1]], axis=1
    )
    to_end = jnp.exp(-rates[:, :, None] * (length - 1.0 - offsets)).reshape(groups * modes, length)
    wsh, wsl = split_glue(to_end)
    starts = (gains[None] * jnp.exp(-rates[None] * (offsets + 1.0)[:, None, None])).reshape(
        length, groups * modes
    )
    ech, ecl = split_glue(starts)

    lane_block = lambda rows: pl.BlockSpec((rows, width), lambda j: (0, j))
    proj_block = pl.BlockSpec((3, length, width), lambda j: (0, 0, j))
    tail_rows = length + 16 + 2 * modes
    zs, zm, zl, tail, state = pl.pallas_call(
        functools.partial(
            features_kernel, lookback=lookback, modes=modes, group_width=group_width
        ),
        grid=(steps,),
        in_specs=[
            proj_block,
            proj_block,
            proj_block,
            lane_block(rims.shape[0]),
            lane_block(ft.shape[0]),
            pl.BlockSpec((gpb * modes, length), lambda j: (j, 0)),
            pl.BlockSpec((gpb * modes, length), lambda j: (j, 0)),
        ],
        out_specs=[
            lane_block(length),
            lane_block(length),
            lane_block(length),
            lane_block(tail_rows),
            lane_block(modes),
        ],
        out_shape=[
            jax.ShapeDtypeStruct((length, channels), bf16),
            jax.ShapeDtypeStruct((length, channels), bf16),
            jax.ShapeDtypeStruct((length, channels), bf16),
            jax.ShapeDtypeStruct((tail_rows, channels), bf16),
            jax.ShapeDtypeStruct((modes, channels), f32),
        ],
        cost_estimate=pl.CostEstimate(
            flops=length * channels * (40 + 4 * TILE),
            transcendentals=0,
            bytes_accessed=length * channels * 26,
        ),
    )(short_proj, medium_proj, long_proj, arrived, ft, wsh, wsl)

    tail_in = shifted(tail, "ctx", 1)
    tm, tlh, tll = pl.pallas_call(
        toeplitz_kernel,
        grid=(steps,),
        in_specs=[pl.BlockSpec((gpb, 2 * length), lambda j: (j, 0))] * 2
        + [pl.BlockSpec((modes, width), lambda j: (0, j))],
        out_specs=[
            pl.BlockSpec((gpb, length, 2 * length), lambda j: (j, 0, 0)),
            pl.BlockSpec((gpb, length, length), lambda j: (j, 0, 0)),
            pl.BlockSpec((gpb, length, length), lambda j: (j, 0, 0)),
        ],
        out_shape=[
            jax.ShapeDtypeStruct((groups, length, 2 * length), bf16),
            jax.ShapeDtypeStruct((groups, length, length), bf16),
            jax.ShapeDtypeStruct((groups, length, length), bf16),
        ],
        cost_estimate=pl.CostEstimate(
            flops=groups * length * length * 8,
            transcendentals=0,
            bytes_accessed=groups * length * length * 8,
        ),
    )(bm, bl, state)

    previous = tail_in[length + 16:length + 16 + modes].astype(f32) + tail_in[
        length + 16 + modes:
    ].astype(f32)
    if blocks <= 8:
        received = [previous] + [shifted(state, "ctx", k) for k in range(2, blocks)]
        stack = jnp.stack((received + [state])[:blocks])
        powers = jnp.arange(blocks, dtype=f32)
    else:
        stack = lax.all_gather(state, "ctx")
        powers = ((position - 1 - jnp.arange(blocks)) % blocks).astype(f32)
    rate_c = jnp.repeat(rates.T, group_width, axis=1)
    wrap_c = jnp.repeat(wrap_scale.T, group_width, axis=1)
    incoming = (
        jnp.sum(jnp.exp(-rate_c[None] * (length * powers)[:, None, None]) * stack, axis=0)
        / wrap_c
    )

    query_block = pl.BlockSpec((1, length, width), lambda j: (0, 0, j))
    outs = pl.pallas_call(
        functools.partial(mix_kernel, lookback=lookback, modes=modes, group_width=group_width),
        grid=(steps,),
        in_specs=[
            query_block,
            query_block,
            query_block,
            lane_block(rims.shape[0]),
            lane_block(ft.shape[0]),
            lane_block(length),
            lane_block(length),
            lane_block(length),
            lane_block(tail_rows),
            lane_block(short_count),
            pl.BlockSpec((gpb, length, 2 * length), lambda j: (j, 0, 0)),
            pl.BlockSpec((gpb, length, length), lambda j: (j, 0, 0)),
            pl.BlockSpec((gpb, length, length), lambda j: (j, 0, 0)),
            pl.BlockSpec((length, gpb * modes), lambda j: (0, j)),
            pl.BlockSpec((length, gpb * modes), lambda j: (0, j)),
            lane_block(modes),
        ],
        out_specs=[lane_block(length)] * 3,
        out_shape=[jax.ShapeDtypeStruct((length, channels), bf16)] * 3,
        scratch_shapes=[
            pltpu.VMEM((length, TILE), f32),
            pltpu.VMEM((2 * length, TILE), bf16),
        ],
        cost_estimate=pl.CostEstimate(
            flops=groups * length * TILE * length * 10,
            transcendentals=0,
            bytes_accessed=groups * length * length * 8 + length * channels * 20,
        ),
    )(short_proj, medium_proj, long_proj, arrived, ft, zs, zm, zl, tail_in, st,
      tm, tlh, tll, ech, ecl, incoming)
    return tuple(outs)


def solution(mesh):
    return jax.shard_map(
        on_device,
        mesh=mesh,
        in_specs=(
            P(None, ("group", "ctx"), "chan"),
            P(None, ("group", "ctx"), "chan"),
            P(None, ("group", "ctx"), "chan"),
            P(None, None, None, "chan"),
            P(None, "chan"),
            P("chan", None),
            P("chan", None),
            P("chan", None),
        ),
        out_specs=(
            P(("group", "ctx"), "chan"),
            P(("group", "ctx"), "chan"),
            P(("group", "ctx"), "chan"),
        ),
        check_vma=False,
    )
```

```python
import functools

import jax
import jax.numpy as jnp
from jax import lax
from jax.experimental import pallas as pl
from jax.experimental.pallas import tpu as pltpu
from jax.sharding import PartitionSpec as P

f32 = jnp.float32
bf16 = jnp.bfloat16
TILE = 128
BLOCK = 512


def shifted(block, axis, distance):
    size = lax.axis_size(axis)
    route = [((i - distance) % size, i) for i in range(size)]
    return lax.ppermute(block, axis, route)


def split_bf16(x):
    hi = x.astype(bf16)
    return hi, (x - hi.astype(f32)).astype(bf16)


def split_glue(x):
    hi = lax.reduce_precision(x, exponent_bits=8, mantissa_bits=7)
    return hi.astype(bf16), (x - hi).astype(bf16)


def feature_rows(proj_ref, rim_ref, ft_ref, lanes, operator, branch, index, lookback):
    src = proj_ref[index, :, lanes].astype(f32)
    number = operator * 3 + branch
    row = lax.broadcasted_iota(jnp.int32, src.shape, 0)
    result = ft_ref[pl.ds(number * (lookback + 1), 1), lanes] * src
    for back in range(1, lookback + 1):
        moved = pltpu.roll(src, back, 0)
        for t in range(back if rim_ref is not None else 0):
            rim_row = rim_ref[pl.ds(number * lookback + lookback + t - back, 1), lanes]
            moved = jnp.where(row == t, rim_row.astype(f32), moved)
        result = result + ft_ref[pl.ds(number * (lookback + 1) + back, 1), lanes] * moved
    return result


def toeplitz_kernel(bm_ref, bl_ref, after_ref, tm_ref, tlh_ref, tll_ref):
    per = bm_ref.shape[0]
    rows = tm_ref.shape[1]
    width = bm_ref.shape[1]
    for gl in range(per):
        base = jnp.broadcast_to(bm_ref[pl.ds(gl, 1), :], (rows, width))
        tm_ref[gl] = pltpu.roll(base, 0, 1, stride=1, stride_axis=0).astype(bf16)
        base = jnp.broadcast_to(bl_ref[pl.ds(gl, 1), :], (rows, width))
        full = pltpu.roll(base, 0, 1, stride=1, stride_axis=0)[:, :rows]
        hi, lo = split_bf16(full)
        tlh_ref[gl] = hi
        tll_ref[gl] = lo


def pre_kernel(sp_ref, mp_ref, lp_ref, ft_ref, wsh_ref, wsl_ref, full_ref, msg_ref, msg_scr,
               *, lookback, modes, group_width, msg_rows, state_row):
    length = sp_ref.shape[1]
    rows_per = TILE // group_width * modes
    head_row = 9 * lookback
    projs = (sp_ref, mp_ref, lp_ref)
    for sub in range(full_ref.shape[1] // TILE):
        lanes = pl.ds(sub * TILE, TILE)
        msg_scr[...] = jnp.zeros_like(msg_scr)
        for operator in range(3):
            for branch in range(3):
                for r in range(lookback):
                    msg_scr[pl.ds((operator * 3 + branch) * lookback + r, 1), :] = projs[operator][
                        branch, pl.ds(length - lookback + r, 1), lanes
                    ].astype(f32)
        for operator in (1, 2):
            for branch in (1, 2):
                for r in range(lookback):
                    at = head_row + ((operator - 1) * 2 + branch - 1) * lookback + r
                    msg_scr[pl.ds(at, 1), :] = projs[operator][branch, pl.ds(r, 1), lanes].astype(f32)
        products = []
        for operator, proj_ref in enumerate(projs):
            k_feat = feature_rows(proj_ref, None, ft_ref, lanes, operator, 1, 1, lookback)
            v_feat = feature_rows(proj_ref, None, ft_ref, lanes, operator, 2, 2, lookback)
            products.append((k_feat * v_feat).astype(bf16))
        zs, zm, zl = products
        full_ref[pl.ds(msg_rows, length), lanes] = zm
        full_ref[pl.ds(msg_rows + length, 16), lanes] = zs[length - 16:, :]
        weights = pl.ds(sub * rows_per, rows_per)
        full = jnp.dot(wsh_ref[weights, :], zl, preferred_element_type=f32) + jnp.dot(
            wsl_ref[weights, :], zl, preferred_element_type=f32
        )
        rows = lax.broadcasted_iota(jnp.int32, full.shape, 0) // modes
        lane_group = lax.broadcasted_iota(jnp.int32, full.shape, 1) // group_width
        full = jnp.where(rows == lane_group, full, 0.0)
        state = full[0:modes, :]
        for gl in range(1, rows_per // modes):
            state = state + full[gl * modes:(gl + 1) * modes, :]
        hi, lo = split_bf16(state)
        msg_scr[pl.ds(state_row, modes), :] = hi.astype(f32)
        msg_scr[pl.ds(state_row + modes, modes), :] = lo.astype(f32)
        packed = msg_scr[...].astype(bf16)
        msg_ref[:, lanes] = packed
        full_ref[pl.ds(0, msg_rows), lanes] = packed


def mix_kernel(sp_ref, mp_ref, lp_ref, in_ref, ft_ref, st_ref, tm_ref, tlh_ref, tll_ref,
               ech_ref, ecl_ref, inc_ref, fix_ref, so_ref, mo_ref, lo_ref, y_scr, zext_scr,
               *, lookback, modes, group_width, msg_rows):
    length = so_ref.shape[0]
    per = TILE // group_width
    row = lax.broadcasted_iota(jnp.int32, (length, TILE), 0)
    lane_group = lax.broadcasted_iota(jnp.int32, (length, TILE), 1) // group_width
    for sub in range(so_ref.shape[1] // TILE):
        lanes = pl.ds(sub * TILE, TILE)
        feats = [
            [feature_rows(ref, in_ref, ft_ref, lanes, operator, branch, branch, lookback)
             for branch in range(3)]
            for operator, ref in enumerate((sp_ref, mp_ref, lp_ref))
        ]
        zs, zm, zl = [(f[1] * f[2]).astype(bf16) for f in feats]

        zs = zs.astype(f32)
        y_scr[...] = zs
        y_scr[pl.ds(length - 16, 16), :] = in_ref[pl.ds(msg_rows + length, 16), lanes].astype(f32)
        wrapped = y_scr[...]
        conv = st_ref[pl.ds(0, 1), lanes] * zs
        for j in range(1, st_ref.shape[0]):
            back = jnp.where(row < j, pltpu.roll(wrapped, j, 0), pltpu.roll(zs, j, 0))
            conv = conv + st_ref[pl.ds(j, 1), lanes] * back
        so_ref[:, lanes] = (feats[0][0] * conv).astype(so_ref.dtype)

        zext_scr[pl.ds(0, length), :] = in_ref[pl.ds(msg_rows, length), lanes]
        first = lax.broadcasted_iota(jnp.int32, (16, TILE), 0)
        zext_scr[pl.ds(0, 16), :] = jnp.where(
            first < lookback, fix_ref[:, lanes], in_ref[pl.ds(msg_rows, 16), lanes].astype(f32)
        ).astype(bf16)
        zext_scr[pl.ds(length, length), :] = zm
        zext = zext_scr[...]
        acc = jnp.zeros((length, TILE), f32)
        for gl in range(per):
            part = jnp.dot(tm_ref[sub * per + gl], zext, preferred_element_type=f32)
            acc = jnp.where(lane_group == gl, part, acc)
        mo_ref[:, lanes] = (feats[1][0] * acc).astype(mo_ref.dtype)

        acc = jnp.zeros((length, TILE), f32)
        for gl in range(per):
            part = jnp.dot(tlh_ref[sub * per + gl], zl, preferred_element_type=f32) + jnp.dot(
                tll_ref[sub * per + gl], zl, preferred_element_type=f32
            )
            acc = jnp.where(lane_group == gl, part, acc)
        incoming = inc_ref[:, lanes]
        stacked = jnp.concatenate([incoming] * per, axis=0)
        srow = lax.broadcasted_iota(jnp.int32, stacked.shape, 0) // modes
        slane = lax.broadcasted_iota(jnp.int32, stacked.shape, 1) // group_width
        stacked = jnp.where(srow == slane, stacked, 0.0)
        ih, il = split_bf16(stacked)
        eh = ech_ref[:, lanes]
        el = ecl_ref[:, lanes]
        carried = (
            jnp.dot(eh, ih, preferred_element_type=f32)
            + jnp.dot(eh, il, preferred_element_type=f32)
            + jnp.dot(el, ih, preferred_element_type=f32)
        )
        lo_ref[:, lanes] = (feats[2][0] * (acc + carried)).astype(lo_ref.dtype)


def head_products(messages, before, ft, operator, lookback):
    head_row = 9 * lookback
    feats = []
    for branch in (1, 2):
        head = head_row + ((operator - 1) * 2 + branch - 1) * lookback
        rim = (operator * 3 + branch) * lookback
        taps = ft[(operator * 3 + branch) * (lookback + 1):(operator * 3 + branch + 1) * (lookback + 1)]
        rows = []
        for p in range(lookback):
            total = None
            for j in range(lookback + 1):
                src = messages[:, head + p - j] if p >= j else before[:, rim + lookback + p - j]
                term = taps[j] * src.astype(f32)
                total = term if total is None else total + term
            rows.append(total)
        feats.append(jnp.stack(rows, axis=1))
    return (feats[0] * feats[1]).astype(bf16)


def on_device(short_proj, medium_proj, long_proj, feature_taps, short_taps, medium_taps,
              long_rates, long_residues):
    _, length, channels = short_proj.shape
    groups, modes = long_rates.shape
    group_width = channels // groups
    lookback = feature_taps.shape[2] - 1
    reach = medium_taps.shape[1]
    short_count = short_taps.shape[0]
    assert reach <= length and short_count <= 17 and 0 < lookback <= 4 and modes % 8 == 0
    blocks = lax.axis_size("ctx")
    position = lax.axis_index("ctx")
    width = min(BLOCK, channels)
    steps = channels // width
    gpb = width // group_width
    state_row = 32
    msg_rows = state_row + 2 * modes
    full_rows = msg_rows + length + 16

    ft = feature_taps.astype(f32).reshape(-1, channels)
    st = jnp.repeat(short_taps.astype(f32), group_width, axis=1)
    rates = long_rates
    loop_length = length * blocks
    wrap_scale = -jnp.expm1(-rates * loop_length)
    gains = long_residues * jnp.sqrt(
        -jnp.expm1(-2.0 * rates) * wrap_scale / (1.0 + jnp.exp(-rates * loop_length))
    )
    offsets = jnp.arange(length, dtype=f32)
    to_end = jnp.exp(-rates[:, :, None] * (length - 1.0 - offsets))
    late = jnp.where(offsets >= lookback, to_end, 0.0).reshape(groups * modes, length)
    wsh, wsl = split_glue(late)

    lane_block = lambda rows: pl.BlockSpec((rows, width), lambda j: (0, j))
    proj_block = pl.BlockSpec((3, length, width), lambda j: (0, 0, j))
    full, msg = pl.pallas_call(
        functools.partial(
            pre_kernel, lookback=lookback, modes=modes, group_width=group_width,
            msg_rows=msg_rows, state_row=state_row,
        ),
        grid=(steps,),
        in_specs=[
            proj_block,
            proj_block,
            proj_block,
            lane_block(ft.shape[0]),
            pl.BlockSpec((gpb * modes, length), lambda j: (j, 0)),
            pl.BlockSpec((gpb * modes, length), lambda j: (j, 0)),
        ],
        out_specs=[lane_block(full_rows), lane_block(msg_rows)],
        out_shape=[
            jax.ShapeDtypeStruct((full_rows, channels), bf16),
            jax.ShapeDtypeStruct((msg_rows, channels), bf16),
        ],
        scratch_shapes=[pltpu.VMEM((msg_rows, TILE), f32)],
        cost_estimate=pl.CostEstimate(
            flops=length * channels * (30 + 4 * TILE),
            transcendentals=0,
            bytes_accessed=length * channels * 22,
        ),
    )(short_proj, medium_proj, long_proj, ft, wsh, wsl)

    arrived = shifted(full, "ctx", 1)
    if blocks <= 8:
        by_shift = [msg, arrived[:msg_rows]] + [shifted(msg, "ctx", k) for k in range(2, blocks)]
        messages = jnp.stack(by_shift[:blocks])
    else:
        messages = lax.all_gather(msg, "ctx")[(position - jnp.arange(blocks)) % blocks]
    before = jnp.roll(messages, -1, axis=0)

    head_long = head_products(messages, before, ft, 2, lookback).astype(f32)
    first_w = jnp.repeat(
        jnp.transpose(to_end[:, :, :lookback], (2, 1, 0)), group_width, axis=2
    )
    states = (
        messages[:, state_row:state_row + modes].astype(f32)
        + messages[:, state_row + modes:msg_rows].astype(f32)
        + jnp.sum(first_w[None] * head_long[:, :, None, :], axis=1)
    )
    states = jnp.roll(states, -1, axis=0)
    rate_c = jnp.repeat(rates.T, group_width, axis=1)
    wrap_c = jnp.repeat(wrap_scale.T, group_width, axis=1)
    powers = jnp.arange(blocks, dtype=f32)
    incoming = (
        jnp.sum(jnp.exp(-rate_c[None] * (length * powers)[:, None, None]) * states, axis=0)
        / wrap_c
    )
    fix = head_products(messages[1 % blocks:1 % blocks + 1], before[1 % blocks:1 % blocks + 1],
                        ft, 1, lookback)[0].astype(f32)
    fix = jnp.pad(fix, ((0, 16 - lookback), (0, 0)))

    bm = jnp.concatenate(
        [
            jnp.zeros((groups, length - reach + 1), f32),
            medium_taps.astype(f32)[:, ::-1],
            jnp.zeros((groups, length - 1), f32),
        ],
        axis=1,
    )
    profile = jnp.sum(gains[:, :, None] * jnp.exp(-rates[:, :, None] * offsets), axis=1)
    bl = jnp.concatenate(
        [profile[:, :1], jnp.zeros((groups, length), f32), profile[:, :0:-1]], axis=1
    )
    starts = (gains[None] * jnp.exp(-rates[None] * (offsets + 1.0)[:, None, None])).reshape(
        length, groups * modes
    )
    ech, ecl = split_glue(starts)
    tm, tlh, tll = pl.pallas_call(
        toeplitz_kernel,
        grid=(steps,),
        in_specs=[pl.BlockSpec((gpb, 2 * length), lambda j: (j, 0))] * 2
        + [lane_block(msg_rows)],
        out_specs=[
            pl.BlockSpec((gpb, length, 2 * length), lambda j: (j, 0, 0)),
            pl.BlockSpec((gpb, length, length), lambda j: (j, 0, 0)),
            pl.BlockSpec((gpb, length, length), lambda j: (j, 0, 0)),
        ],
        out_shape=[
            jax.ShapeDtypeStruct((groups, length, 2 * length), bf16),
            jax.ShapeDtypeStruct((groups, length, length), bf16),
            jax.ShapeDtypeStruct((groups, length, length), bf16),
        ],
        cost_estimate=pl.CostEstimate(
            flops=groups * length * length * 8,
            transcendentals=0,
            bytes_accessed=groups * length * length * 8,
        ),
    )(bm, bl, msg)

    outs = pl.pallas_call(
        functools.partial(mix_kernel, lookback=lookback, modes=modes, group_width=group_width,
                          msg_rows=msg_rows),
        grid=(steps,),
        in_specs=[
            proj_block,
            proj_block,
            proj_block,
            lane_block(full_rows),
            lane_block(ft.shape[0]),
            lane_block(short_count),
            pl.BlockSpec((gpb, length, 2 * length), lambda j: (j, 0, 0)),
            pl.BlockSpec((gpb, length, length), lambda j: (j, 0, 0)),
            pl.BlockSpec((gpb, length, length), lambda j: (j, 0, 0)),
            pl.BlockSpec((length, gpb * modes), lambda j: (0, j)),
            pl.BlockSpec((length, gpb * modes), lambda j: (0, j)),
            lane_block(modes),
            lane_block(16),
        ],
        out_specs=[lane_block(length)] * 3,
        out_shape=[jax.ShapeDtypeStruct((length, channels), bf16)] * 3,
        scratch_shapes=[
            pltpu.VMEM((length, TILE), f32),
            pltpu.VMEM((2 * length, TILE), bf16),
        ],
        cost_estimate=pl.CostEstimate(
            flops=groups * length * TILE * length * 10,
            transcendentals=0,
            bytes_accessed=groups * length * length * 8 + length * channels * 24,
        ),
    )(short_proj, medium_proj, long_proj, arrived, ft, st, tm, tlh, tll, ech, ecl, incoming, fix)
    return tuple(outs)


def solution(mesh):
    return jax.shard_map(
        on_device,
        mesh=mesh,
        in_specs=(
            P(None, ("group", "ctx"), "chan"),
            P(None, ("group", "ctx"), "chan"),
            P(None, ("group", "ctx"), "chan"),
            P(None, None, None, "chan"),
            P(None, "chan"),
            P("chan", None),
            P("chan", None),
            P("chan", None),
        ),
        out_specs=(
            P(("group", "ctx"), "chan"),
            P(("group", "ctx"), "chan"),
            P(("group", "ctx"), "chan"),
        ),
        check_vma=False,
    )
```

```python
import functools

import jax
import jax.numpy as jnp
from jax import lax
from jax.experimental import pallas as pl
from jax.experimental.pallas import tpu as pltpu
from jax.sharding import PartitionSpec as P

f32 = jnp.float32
bf16 = jnp.bfloat16
TILE = 128
BLOCK = 512


def shifted(block, axis, distance):
    size = lax.axis_size(axis)
    route = [((i - distance) % size, i) for i in range(size)]
    return lax.ppermute(block, axis, route)


def split_bf16(x):
    hi = x.astype(bf16)
    return hi, (x - hi.astype(f32)).astype(bf16)


def split_glue(x):
    hi = lax.reduce_precision(x, exponent_bits=8, mantissa_bits=7)
    return hi.astype(bf16), (x - hi).astype(bf16)


KEPT = ((1, 1), (1, 2), (2, 1), (2, 2))
OTHER = ((0, 0), (0, 1), (0, 2), (1, 0), (2, 0))


def round16(x):
    return -(-x // 16) * 16


def layout(modes, lookback):
    state_row = 0
    kept_row = 2 * modes
    head_row = kept_row + len(KEPT) * lookback
    small_rows = round16(head_row + len(KEPT) * lookback)
    msg_rows = round16(small_rows + len(OTHER) * lookback)
    return state_row, kept_row, head_row, small_rows, msg_rows


def rim_slot(operator, branch, modes, lookback):
    _, kept_row, _, small_rows, _ = layout(modes, lookback)
    if (operator, branch) in KEPT:
        return kept_row + KEPT.index((operator, branch)) * lookback
    return small_rows + OTHER.index((operator, branch)) * lookback


def head_slot(operator, branch, modes, lookback):
    return layout(modes, lookback)[2] + KEPT.index((operator, branch)) * lookback


def feature_rows(proj_ref, rim_ref, ft_ref, lanes, operator, branch, index, lookback, modes=0):
    src = proj_ref[index, :, lanes].astype(f32)
    number = operator * 3 + branch
    row = lax.broadcasted_iota(jnp.int32, src.shape, 0)
    result = ft_ref[pl.ds(number * (lookback + 1), 1), lanes] * src
    for back in range(1, lookback + 1):
        moved = pltpu.roll(src, back, 0)
        for t in range(back if rim_ref is not None else 0):
            rim_row = rim_ref[pl.ds(rim_slot(operator, branch, modes, lookback) + lookback + t - back, 1), lanes]
            moved = jnp.where(row == t, rim_row.astype(f32), moved)
        result = result + ft_ref[pl.ds(number * (lookback + 1) + back, 1), lanes] * moved
    return result


def toeplitz_kernel(bm_ref, bl_ref, after_ref, tm_ref, tlh_ref, tll_ref):
    per = bm_ref.shape[0]
    rows = tm_ref.shape[1]
    width = bm_ref.shape[1]
    for gl in range(per):
        base = jnp.broadcast_to(bm_ref[pl.ds(gl, 1), :], (rows, width))
        tm_ref[gl] = pltpu.roll(base, 0, 1, stride=1, stride_axis=0).astype(bf16)
        base = jnp.broadcast_to(bl_ref[pl.ds(gl, 1), :], (rows, width))
        full = pltpu.roll(base, 0, 1, stride=1, stride_axis=0)[:, :rows]
        hi, lo = split_bf16(full)
        tlh_ref[gl] = hi
        tll_ref[gl] = lo


def pre_kernel(sp_ref, mp_ref, lp_ref, ft_ref, wsh_ref, wsl_ref, full_ref, msg_ref, msg_scr,
               *, lookback, modes, group_width):
    length = sp_ref.shape[1]
    rows_per = TILE // group_width * modes
    state_row, _, _, small_rows, msg_rows = layout(modes, lookback)
    projs = (sp_ref, mp_ref, lp_ref)
    for sub in range(full_ref.shape[1] // TILE):
        lanes = pl.ds(sub * TILE, TILE)
        msg_scr[...] = jnp.zeros_like(msg_scr)
        for operator in range(3):
            for branch in range(3):
                for r in range(lookback):
                    msg_scr[pl.ds(rim_slot(operator, branch, modes, lookback) + r, 1), :] = projs[operator][
                        branch, pl.ds(length - lookback + r, 1), lanes
                    ].astype(f32)
        for operator in (1, 2):
            for branch in (1, 2):
                for r in range(lookback):
                    at = head_slot(operator, branch, modes, lookback) + r
                    msg_scr[pl.ds(at, 1), :] = projs[operator][branch, pl.ds(r, 1), lanes].astype(f32)
        products = []
        for operator, proj_ref in enumerate(projs):
            k_feat = feature_rows(proj_ref, None, ft_ref, lanes, operator, 1, 1, lookback)
            v_feat = feature_rows(proj_ref, None, ft_ref, lanes, operator, 2, 2, lookback)
            products.append((k_feat * v_feat).astype(bf16))
        zs, zm, zl = products
        full_ref[pl.ds(msg_rows, length), lanes] = zm
        full_ref[pl.ds(msg_rows + length, 16), lanes] = zs[length - 16:, :]
        weights = pl.ds(sub * rows_per, rows_per)
        full = jnp.dot(wsh_ref[weights, :], zl, preferred_element_type=f32) + jnp.dot(
            wsl_ref[weights, :], zl, preferred_element_type=f32
        )
        rows = lax.broadcasted_iota(jnp.int32, full.shape, 0) // modes
        lane_group = lax.broadcasted_iota(jnp.int32, full.shape, 1) // group_width
        full = jnp.where(rows == lane_group, full, 0.0)
        state = full[0:modes, :]
        for gl in range(1, rows_per // modes):
            state = state + full[gl * modes:(gl + 1) * modes, :]
        hi, lo = split_bf16(state)
        msg_scr[pl.ds(state_row, modes), :] = hi.astype(f32)
        msg_scr[pl.ds(state_row + modes, modes), :] = lo.astype(f32)
        packed = msg_scr[...].astype(bf16)
        msg_ref[:, lanes] = packed[:small_rows]
        full_ref[pl.ds(0, msg_rows), lanes] = packed


def head_rows(head_ref, before_ref, ft_ref, lanes, operator, lookback, modes):
    feats = []
    for branch in (1, 2):
        head = head_slot(operator, branch, modes, lookback)
        rim = rim_slot(operator, branch, modes, lookback)
        base = (operator * 3 + branch) * (lookback + 1)
        rows = []
        for p in range(lookback):
            total = None
            for j in range(lookback + 1):
                if p >= j:
                    src = head_ref[pl.ds(head + p - j, 1), lanes]
                else:
                    src = before_ref[pl.ds(rim + lookback + p - j, 1), lanes]
                term = ft_ref[pl.ds(base + j, 1), lanes] * src.astype(f32)
                total = term if total is None else total + term
            rows.append(total)
        feats.append(rows)
    return [(a * b).astype(bf16).astype(f32) for a, b in zip(*feats)]


def mix_kernel(*refs, lookback, modes, group_width, inline, blocks):
    (sp_ref, mp_ref, lp_ref, in_ref, ft_ref, st_ref, tm_ref, tlh_ref, tll_ref,
     ech_ref, ecl_ref) = refs[:11]
    if inline:
        coef_ref, first_ref = refs[11:13]
        by_shift = [refs[13], in_ref] + list(refs[14:12 + blocks])
        rest = refs[12 + blocks:]
    else:
        inc_ref, fix_ref = refs[11:13]
        rest = refs[13:]
    so_ref, mo_ref, lo_ref, y_scr, zext_scr = rest
    state_row, _, _, _, msg_rows = layout(modes, lookback)
    length = so_ref.shape[0]
    per = TILE // group_width
    row = lax.broadcasted_iota(jnp.int32, (length, TILE), 0)
    lane_group = lax.broadcasted_iota(jnp.int32, (length, TILE), 1) // group_width
    first = lax.broadcasted_iota(jnp.int32, (16, TILE), 0)
    for sub in range(so_ref.shape[1] // TILE):
        lanes = pl.ds(sub * TILE, TILE)
        if inline:
            incoming = None
            for k in range(blocks):
                now_ref = by_shift[k]
                head = head_rows(now_ref, by_shift[(k + 1) % blocks], ft_ref, lanes, 2, lookback, modes)
                state = now_ref[pl.ds(state_row, modes), lanes].astype(f32) + now_ref[
                    pl.ds(state_row + modes, modes), lanes
                ].astype(f32)
                for p in range(lookback):
                    state = state + first_ref[p, :, lanes] * head[p]
                term = coef_ref[(k - 1) % blocks, :, lanes] * state
                incoming = term if incoming is None else incoming + term
            fixed = head_rows(by_shift[1 % blocks], by_shift[2 % blocks], ft_ref, lanes, 1,
                              lookback, modes)
            fix = jnp.zeros((16, TILE), f32)
            for p in range(lookback):
                fix = jnp.where(first == p, fixed[p], fix)
        else:
            incoming = inc_ref[:, lanes]
            fix = fix_ref[:, lanes]
        feats = [
            [feature_rows(ref, in_ref, ft_ref, lanes, operator, branch, branch, lookback, modes)
             for branch in range(3)]
            for operator, ref in enumerate((sp_ref, mp_ref, lp_ref))
        ]
        zs, zm, zl = [(f[1] * f[2]).astype(bf16) for f in feats]

        zs = zs.astype(f32)
        y_scr[...] = zs
        y_scr[pl.ds(length - 16, 16), :] = in_ref[pl.ds(msg_rows + length, 16), lanes].astype(f32)
        wrapped = y_scr[...]
        conv = st_ref[pl.ds(0, 1), lanes] * zs
        for j in range(1, st_ref.shape[0]):
            back = jnp.where(row < j, pltpu.roll(wrapped, j, 0), pltpu.roll(zs, j, 0))
            conv = conv + st_ref[pl.ds(j, 1), lanes] * back
        so_ref[:, lanes] = (feats[0][0] * conv).astype(so_ref.dtype)

        zext_scr[pl.ds(0, length), :] = in_ref[pl.ds(msg_rows, length), lanes]
        zext_scr[pl.ds(0, 16), :] = jnp.where(
            first < lookback, fix, in_ref[pl.ds(msg_rows, 16), lanes].astype(f32)
        ).astype(bf16)
        zext_scr[pl.ds(length, length), :] = zm
        zext = zext_scr[...]
        acc = jnp.zeros((length, TILE), f32)
        for gl in range(per):
            part = jnp.dot(tm_ref[sub * per + gl], zext, preferred_element_type=f32)
            acc = jnp.where(lane_group == gl, part, acc)
        mo_ref[:, lanes] = (feats[1][0] * acc).astype(mo_ref.dtype)

        acc = jnp.zeros((length, TILE), f32)
        for gl in range(per):
            part = jnp.dot(tlh_ref[sub * per + gl], zl, preferred_element_type=f32) + jnp.dot(
                tll_ref[sub * per + gl], zl, preferred_element_type=f32
            )
            acc = jnp.where(lane_group == gl, part, acc)
        stacked = jnp.concatenate([incoming] * per, axis=0)
        srow = lax.broadcasted_iota(jnp.int32, stacked.shape, 0) // modes
        slane = lax.broadcasted_iota(jnp.int32, stacked.shape, 1) // group_width
        stacked = jnp.where(srow == slane, stacked, 0.0)
        ih, il = split_bf16(stacked)
        eh = ech_ref[:, lanes]
        el = ecl_ref[:, lanes]
        carried = (
            jnp.dot(eh, ih, preferred_element_type=f32)
            + jnp.dot(eh, il, preferred_element_type=f32)
            + jnp.dot(el, ih, preferred_element_type=f32)
        )
        lo_ref[:, lanes] = (feats[2][0] * (acc + carried)).astype(lo_ref.dtype)


def head_products(messages, before, ft, operator, lookback, modes):
    feats = []
    for branch in (1, 2):
        head = head_slot(operator, branch, modes, lookback)
        rim = rim_slot(operator, branch, modes, lookback)
        taps = ft[(operator * 3 + branch) * (lookback + 1):(operator * 3 + branch + 1) * (lookback + 1)]
        rows = []
        for p in range(lookback):
            total = None
            for j in range(lookback + 1):
                src = messages[:, head + p - j] if p >= j else before[:, rim + lookback + p - j]
                term = taps[j] * src.astype(f32)
                total = term if total is None else total + term
            rows.append(total)
        feats.append(jnp.stack(rows, axis=1))
    return lax.reduce_precision(feats[0] * feats[1], exponent_bits=8, mantissa_bits=7)


def on_device(short_proj, medium_proj, long_proj, feature_taps, short_taps, medium_taps,
              long_rates, long_residues):
    _, length, channels = short_proj.shape
    groups, modes = long_rates.shape
    group_width = channels // groups
    lookback = feature_taps.shape[2] - 1
    reach = medium_taps.shape[1]
    short_count = short_taps.shape[0]
    assert reach <= length and short_count <= 17 and 0 < lookback <= 4 and modes % 8 == 0
    blocks = lax.axis_size("ctx")
    position = lax.axis_index("ctx")
    inline = blocks <= 8
    width = min(BLOCK, channels)
    steps = channels // width
    gpb = width // group_width
    state_row, _, _, small_rows, msg_rows = layout(modes, lookback)
    full_rows = msg_rows + length + 16

    ft = feature_taps.astype(f32).reshape(-1, channels)
    st = jnp.repeat(short_taps.astype(f32), group_width, axis=1)
    rates = long_rates
    loop_length = length * blocks
    wrap_scale = -jnp.expm1(-rates * loop_length)
    gains = long_residues * jnp.sqrt(
        -jnp.expm1(-2.0 * rates) * wrap_scale / (1.0 + jnp.exp(-rates * loop_length))
    )
    offsets = jnp.arange(length, dtype=f32)
    to_end = jnp.exp(-rates[:, :, None] * (length - 1.0 - offsets))
    late = jnp.where(offsets >= lookback, to_end, 0.0).reshape(groups * modes, length)
    wsh, wsl = split_glue(late)

    lane_block = lambda rows: pl.BlockSpec((rows, width), lambda j: (0, j))
    proj_block = pl.BlockSpec((3, length, width), lambda j: (0, 0, j))
    full, msg = pl.pallas_call(
        functools.partial(pre_kernel, lookback=lookback, modes=modes, group_width=group_width),
        grid=(steps,),
        in_specs=[
            proj_block,
            proj_block,
            proj_block,
            lane_block(ft.shape[0]),
            pl.BlockSpec((gpb * modes, length), lambda j: (j, 0)),
            pl.BlockSpec((gpb * modes, length), lambda j: (j, 0)),
        ],
        out_specs=[lane_block(full_rows), lane_block(small_rows)],
        out_shape=[
            jax.ShapeDtypeStruct((full_rows, channels), bf16),
            jax.ShapeDtypeStruct((small_rows, channels), bf16),
        ],
        scratch_shapes=[pltpu.VMEM((msg_rows, TILE), f32)],
        cost_estimate=pl.CostEstimate(
            flops=length * channels * (30 + 4 * TILE),
            transcendentals=0,
            bytes_accessed=length * channels * 22,
        ),
    )(short_proj, medium_proj, long_proj, ft, wsh, wsl)

    arrived = shifted(full, "ctx", 1)
    first_w = jnp.repeat(
        jnp.transpose(to_end[:, :, :lookback], (2, 1, 0)), group_width, axis=2
    )
    rate_c = jnp.repeat(rates.T, group_width, axis=1)
    wrap_c = jnp.repeat(wrap_scale.T, group_width, axis=1)
    powers = jnp.arange(blocks, dtype=f32)
    coef = jnp.exp(-rate_c[None] * (length * powers)[:, None, None]) / wrap_c[None]
    if inline:
        others = [shifted(msg, "ctx", k) for k in range(2, blocks)]
        extra = [coef, first_w, msg] + others
        extra_specs = [
            pl.BlockSpec((blocks, modes, width), lambda j: (0, 0, j)),
            pl.BlockSpec((lookback, modes, width), lambda j: (0, 0, j)),
        ] + [lane_block(small_rows)] * (blocks - 1)
    else:
        messages = lax.all_gather(msg, "ctx")[(position - jnp.arange(blocks)) % blocks]
        before = jnp.roll(messages, -1, axis=0)
        head_long = head_products(messages, before, ft, 2, lookback, modes)
        states = (
            messages[:, state_row:state_row + modes].astype(f32)
            + messages[:, state_row + modes:state_row + 2 * modes].astype(f32)
            + jnp.sum(first_w[None] * head_long[:, :, None, :], axis=1)
        )
        incoming = jnp.sum(coef * jnp.roll(states, -1, axis=0), axis=0)
        fix = head_products(messages[1:2], before[1:2], ft, 1, lookback, modes)[0]
        fix = jnp.pad(fix, ((0, 16 - lookback), (0, 0)))
        extra = [incoming, fix]
        extra_specs = [lane_block(modes), lane_block(16)]

    bm = jnp.concatenate(
        [
            jnp.zeros((groups, length - reach + 1), f32),
            medium_taps.astype(f32)[:, ::-1],
            jnp.zeros((groups, length - 1), f32),
        ],
        axis=1,
    )
    profile = jnp.sum(gains[:, :, None] * jnp.exp(-rates[:, :, None] * offsets), axis=1)
    bl = jnp.concatenate(
        [profile[:, :1], jnp.zeros((groups, length), f32), profile[:, :0:-1]], axis=1
    )
    starts = (gains[None] * jnp.exp(-rates[None] * (offsets + 1.0)[:, None, None])).reshape(
        length, groups * modes
    )
    ech, ecl = split_glue(starts)
    tm, tlh, tll = pl.pallas_call(
        toeplitz_kernel,
        grid=(steps,),
        in_specs=[pl.BlockSpec((gpb, 2 * length), lambda j: (j, 0))] * 2
        + [lane_block(small_rows)],
        out_specs=[
            pl.BlockSpec((gpb, length, 2 * length), lambda j: (j, 0, 0)),
            pl.BlockSpec((gpb, length, length), lambda j: (j, 0, 0)),
            pl.BlockSpec((gpb, length, length), lambda j: (j, 0, 0)),
        ],
        out_shape=[
            jax.ShapeDtypeStruct((groups, length, 2 * length), bf16),
            jax.ShapeDtypeStruct((groups, length, length), bf16),
            jax.ShapeDtypeStruct((groups, length, length), bf16),
        ],
        cost_estimate=pl.CostEstimate(
            flops=groups * length * length * 8,
            transcendentals=0,
            bytes_accessed=groups * length * length * 8,
        ),
    )(bm, bl, msg)

    outs = pl.pallas_call(
        functools.partial(mix_kernel, lookback=lookback, modes=modes, group_width=group_width,
                          inline=inline, blocks=blocks),
        grid=(steps,),
        in_specs=[
            proj_block,
            proj_block,
            proj_block,
            lane_block(full_rows),
            lane_block(ft.shape[0]),
            lane_block(short_count),
            pl.BlockSpec((gpb, length, 2 * length), lambda j: (j, 0, 0)),
            pl.BlockSpec((gpb, length, length), lambda j: (j, 0, 0)),
            pl.BlockSpec((gpb, length, length), lambda j: (j, 0, 0)),
            pl.BlockSpec((length, gpb * modes), lambda j: (0, j)),
            pl.BlockSpec((length, gpb * modes), lambda j: (0, j)),
        ] + extra_specs,
        out_specs=[lane_block(length)] * 3,
        out_shape=[jax.ShapeDtypeStruct((length, channels), bf16)] * 3,
        scratch_shapes=[
            pltpu.VMEM((length, TILE), f32),
            pltpu.VMEM((2 * length, TILE), bf16),
        ],
        cost_estimate=pl.CostEstimate(
            flops=groups * length * TILE * length * 10,
            transcendentals=0,
            bytes_accessed=groups * length * length * 8 + length * channels * 24,
        ),
    )(short_proj, medium_proj, long_proj, arrived, ft, st, tm, tlh, tll, ech, ecl, *extra)
    return tuple(outs)


def solution(mesh):
    return jax.shard_map(
        on_device,
        mesh=mesh,
        in_specs=(
            P(None, ("group", "ctx"), "chan"),
            P(None, ("group", "ctx"), "chan"),
            P(None, ("group", "ctx"), "chan"),
            P(None, None, None, "chan"),
            P(None, "chan"),
            P("chan", None),
            P("chan", None),
            P("chan", None),
        ),
        out_specs=(
            P(("group", "ctx"), "chan"),
            P(("group", "ctx"), "chan"),
            P(("group", "ctx"), "chan"),
        ),
        check_vma=False,
    )
```

```python
import functools

import jax
import jax.numpy as jnp
from jax import lax
from jax.experimental import pallas as pl
from jax.experimental.pallas import tpu as pltpu
from jax.sharding import PartitionSpec as P

f32 = jnp.float32
bf16 = jnp.bfloat16
TILE = 128
BLOCK = 512
KEPT = ((1, 1), (1, 2), (2, 1), (2, 2))


def round16(x):
    return -(-x // 16) * 16


def shifted(block, axis, distance):
    size = lax.axis_size(axis)
    route = [((i - distance) % size, i) for i in range(size)]
    return lax.ppermute(block, axis, route)


def split_bf16(x):
    hi = x.astype(bf16)
    return hi, (x - hi.astype(f32)).astype(bf16)


def split_glue(x):
    hi = lax.reduce_precision(x, exponent_bits=8, mantissa_bits=7)
    return hi.astype(bf16), (x - hi).astype(bf16)


def msg_layout(modes, lookback):
    kept_row = 2 * modes
    head_row = kept_row + len(KEPT) * lookback
    return kept_row, head_row, round16(head_row + len(KEPT) * lookback)


def kept_slot(operator, branch, modes, lookback):
    return msg_layout(modes, lookback)[0] + KEPT.index((operator, branch)) * lookback


def head_slot(operator, branch, modes, lookback):
    return msg_layout(modes, lookback)[1] + KEPT.index((operator, branch)) * lookback


def early_layout(lookback):
    tail_row = round16(9 * lookback)
    return tail_row, tail_row + 16


def feature_rows(proj_ref, rim_ref, ft_ref, lanes, operator, branch, index, lookback):
    src = proj_ref[index, :, lanes].astype(f32)
    number = operator * 3 + branch
    row = lax.broadcasted_iota(jnp.int32, src.shape, 0)
    result = ft_ref[pl.ds(number * (lookback + 1), 1), lanes] * src
    for back in range(1, lookback + 1):
        moved = pltpu.roll(src, back, 0)
        for t in range(back if rim_ref is not None else 0):
            rim_row = rim_ref[pl.ds(number * lookback + lookback + t - back, 1), lanes]
            moved = jnp.where(row == t, rim_row.astype(f32), moved)
        result = result + ft_ref[pl.ds(number * (lookback + 1) + back, 1), lanes] * moved
    return result


def rim_kernel(sp_ref, mp_ref, lp_ref, ft_ref, early_ref, scr, *, lookback):
    tail_row, _ = early_layout(lookback)
    rows = sp_ref.shape[1]
    projs = (sp_ref, mp_ref, lp_ref)
    for sub in range(early_ref.shape[1] // TILE):
        lanes = pl.ds(sub * TILE, TILE)
        scr[...] = jnp.zeros_like(scr)
        for operator in range(3):
            for branch in range(3):
                for r in range(lookback):
                    scr[pl.ds((operator * 3 + branch) * lookback + r, 1), :] = projs[operator][
                        branch, pl.ds(rows - lookback + r, 1), lanes
                    ].astype(f32)
        k_feat = feature_rows(sp_ref, None, ft_ref, lanes, 0, 1, 1, lookback)
        v_feat = feature_rows(sp_ref, None, ft_ref, lanes, 0, 2, 2, lookback)
        scr[pl.ds(tail_row, 16), :] = (k_feat * v_feat).astype(bf16).astype(f32)
        early_ref[:, lanes] = scr[...].astype(bf16)


def toeplitz_kernel(bm_ref, bl_ref, after_ref, tm_ref, tlh_ref, tll_ref):
    per = bm_ref.shape[0]
    rows = tm_ref.shape[1]
    width = bm_ref.shape[1]
    for gl in range(per):
        base = jnp.broadcast_to(bm_ref[pl.ds(gl, 1), :], (rows, width))
        tm_ref[gl] = pltpu.roll(base, 0, 1, stride=1, stride_axis=0).astype(bf16)
        base = jnp.broadcast_to(bl_ref[pl.ds(gl, 1), :], (rows, width))
        full = pltpu.roll(base, 0, 1, stride=1, stride_axis=0)[:, :rows]
        hi, lo = split_bf16(full)
        tlh_ref[gl] = hi
        tll_ref[gl] = lo


def pre_kernel(sp_ref, mp_ref, lp_ref, ft_ref, wsh_ref, wsl_ref, full_ref, msg_ref, msg_scr,
               *, lookback, modes, group_width):
    length = sp_ref.shape[1]
    rows_per = TILE // group_width * modes
    small_rows = msg_layout(modes, lookback)[2]
    projs = (sp_ref, mp_ref, lp_ref)
    for sub in range(full_ref.shape[1] // TILE):
        lanes = pl.ds(sub * TILE, TILE)
        msg_scr[...] = jnp.zeros_like(msg_scr)
        for operator, branch in KEPT:
            for r in range(lookback):
                msg_scr[pl.ds(kept_slot(operator, branch, modes, lookback) + r, 1), :] = projs[
                    operator
                ][branch, pl.ds(length - lookback + r, 1), lanes].astype(f32)
                msg_scr[pl.ds(head_slot(operator, branch, modes, lookback) + r, 1), :] = projs[
                    operator
                ][branch, pl.ds(r, 1), lanes].astype(f32)
        for operator in (1, 2):
            k_feat = feature_rows(projs[operator], None, ft_ref, lanes, operator, 1, 1, lookback)
            v_feat = feature_rows(projs[operator], None, ft_ref, lanes, operator, 2, 2, lookback)
            product = (k_feat * v_feat).astype(bf16)
            if operator == 1:
                full_ref[pl.ds(small_rows, length), lanes] = product
            else:
                zl = product
        weights = pl.ds(sub * rows_per, rows_per)
        full = jnp.dot(wsh_ref[weights, :], zl, preferred_element_type=f32) + jnp.dot(
            wsl_ref[weights, :], zl, preferred_element_type=f32
        )
        rows = lax.broadcasted_iota(jnp.int32, full.shape, 0) // modes
        lane_group = lax.broadcasted_iota(jnp.int32, full.shape, 1) // group_width
        full = jnp.where(rows == lane_group, full, 0.0)
        state = full[0:modes, :]
        for gl in range(1, rows_per // modes):
            state = state + full[gl * modes:(gl + 1) * modes, :]
        hi, lo = split_bf16(state)
        msg_scr[pl.ds(0, modes), :] = hi.astype(f32)
        msg_scr[pl.ds(modes, modes), :] = lo.astype(f32)
        packed = msg_scr[...].astype(bf16)
        msg_ref[:, lanes] = packed
        full_ref[pl.ds(0, small_rows), lanes] = packed


def own_kernel(sp_ref, mp_ref, lp_ref, early_ref, ft_ref, st_ref, tm_ref, tlh_ref, tll_ref,
               so_ref, mpart_ref, lpart_ref, mq_ref, lq_ref, y_scr, *, lookback, group_width):
    tail_row, _ = early_layout(lookback)
    length = so_ref.shape[0]
    per = TILE // group_width
    row = lax.broadcasted_iota(jnp.int32, (length, TILE), 0)
    lane_group = lax.broadcasted_iota(jnp.int32, (length, TILE), 1) // group_width
    for sub in range(so_ref.shape[1] // TILE):
        lanes = pl.ds(sub * TILE, TILE)
        feats = [
            [feature_rows(ref, early_ref, ft_ref, lanes, operator, branch, branch, lookback)
             for branch in range(3)]
            for operator, ref in enumerate((sp_ref, mp_ref, lp_ref))
        ]
        zs, zm, zl = [(f[1] * f[2]).astype(bf16) for f in feats]

        zs = zs.astype(f32)
        y_scr[...] = zs
        y_scr[pl.ds(length - 16, 16), :] = early_ref[pl.ds(tail_row, 16), lanes].astype(f32)
        wrapped = y_scr[...]
        conv = st_ref[pl.ds(0, 1), lanes] * zs
        for j in range(1, st_ref.shape[0]):
            back = jnp.where(row < j, pltpu.roll(wrapped, j, 0), pltpu.roll(zs, j, 0))
            conv = conv + st_ref[pl.ds(j, 1), lanes] * back
        so_ref[:, lanes] = (feats[0][0] * conv).astype(so_ref.dtype)

        acc = jnp.zeros((length, TILE), f32)
        for gl in range(per):
            part = jnp.dot(tm_ref[sub * per + gl], zm, preferred_element_type=f32)
            acc = jnp.where(lane_group == gl, part, acc)
        mpart_ref[:, lanes] = acc
        mq_ref[:, lanes] = feats[1][0]

        acc = jnp.zeros((length, TILE), f32)
        for gl in range(per):
            part = jnp.dot(tlh_ref[sub * per + gl], zl, preferred_element_type=f32) + jnp.dot(
                tll_ref[sub * per + gl], zl, preferred_element_type=f32
            )
            acc = jnp.where(lane_group == gl, part, acc)
        lpart_ref[:, lanes] = acc
        lq_ref[:, lanes] = feats[2][0]


def head_rows(head_ref, before_ref, ft_ref, lanes, operator, lookback, modes):
    feats = []
    for branch in (1, 2):
        head = head_slot(operator, branch, modes, lookback)
        rim = kept_slot(operator, branch, modes, lookback)
        base = (operator * 3 + branch) * (lookback + 1)
        rows = []
        for p in range(lookback):
            total = None
            for j in range(lookback + 1):
                if p >= j:
                    src = head_ref[pl.ds(head + p - j, 1), lanes]
                else:
                    src = before_ref[pl.ds(rim + lookback + p - j, 1), lanes]
                term = ft_ref[pl.ds(base + j, 1), lanes] * src.astype(f32)
                total = term if total is None else total + term
            rows.append(total)
        feats.append(rows)
    return [(a * b).astype(bf16).astype(f32) for a, b in zip(*feats)]


def final_kernel(*refs, lookback, modes, group_width, inline, blocks):
    (in_ref, ft_ref, tm_ref, ech_ref, ecl_ref, mpart_ref, lpart_ref, mq_ref, lq_ref) = refs[:9]
    if inline:
        coef_ref, first_ref = refs[9:11]
        by_shift = [refs[11], in_ref] + list(refs[12:10 + blocks])
        rest = refs[10 + blocks:]
    else:
        inc_ref, fix_ref = refs[9:11]
        rest = refs[11:]
    mo_ref, lo_ref, zprev_scr = rest
    small_rows = msg_layout(modes, lookback)[2]
    length = mo_ref.shape[0]
    per = TILE // group_width
    lane_group = lax.broadcasted_iota(jnp.int32, (length, TILE), 1) // group_width
    first = lax.broadcasted_iota(jnp.int32, (16, TILE), 0)
    for sub in range(mo_ref.shape[1] // TILE):
        lanes = pl.ds(sub * TILE, TILE)
        if inline:
            incoming = None
            for k in range(blocks):
                now_ref = by_shift[k]
                head = head_rows(now_ref, by_shift[(k + 1) % blocks], ft_ref, lanes, 2, lookback,
                                 modes)
                state = now_ref[pl.ds(0, modes), lanes].astype(f32) + now_ref[
                    pl.ds(modes, modes), lanes
                ].astype(f32)
                for p in range(lookback):
                    state = state + first_ref[p, :, lanes] * head[p]
                term = coef_ref[(k - 1) % blocks, :, lanes] * state
                incoming = term if incoming is None else incoming + term
            fixed = head_rows(by_shift[1 % blocks], by_shift[2 % blocks], ft_ref, lanes, 1,
                              lookback, modes)
            fix = jnp.zeros((16, TILE), f32)
            for p in range(lookback):
                fix = jnp.where(first == p, fixed[p], fix)
        else:
            incoming = inc_ref[:, lanes]
            fix = fix_ref[:, lanes]

        zprev_scr[...] = in_ref[pl.ds(small_rows, length), lanes]
        zprev_scr[pl.ds(0, 16), :] = jnp.where(
            first < lookback, fix, in_ref[pl.ds(small_rows, 16), lanes].astype(f32)
        ).astype(bf16)
        zprev = zprev_scr[...]
        acc = mpart_ref[:, lanes]
        for gl in range(per):
            part = jnp.dot(tm_ref[sub * per + gl], zprev, preferred_element_type=f32)
            acc = jnp.where(lane_group == gl, acc + part, acc)
        mo_ref[:, lanes] = (mq_ref[:, lanes] * acc).astype(mo_ref.dtype)

        stacked = jnp.concatenate([incoming] * per, axis=0)
        srow = lax.broadcasted_iota(jnp.int32, stacked.shape, 0) // modes
        slane = lax.broadcasted_iota(jnp.int32, stacked.shape, 1) // group_width
        stacked = jnp.where(srow == slane, stacked, 0.0)
        ih, il = split_bf16(stacked)
        eh = ech_ref[:, lanes]
        el = ecl_ref[:, lanes]
        carried = (
            jnp.dot(eh, ih, preferred_element_type=f32)
            + jnp.dot(eh, il, preferred_element_type=f32)
            + jnp.dot(el, ih, preferred_element_type=f32)
        )
        lo_ref[:, lanes] = (lq_ref[:, lanes] * (lpart_ref[:, lanes] + carried)).astype(lo_ref.dtype)


def head_products(messages, before, ft, operator, lookback, modes):
    feats = []
    for branch in (1, 2):
        head = head_slot(operator, branch, modes, lookback)
        rim = kept_slot(operator, branch, modes, lookback)
        taps = ft[(operator * 3 + branch) * (lookback + 1):(operator * 3 + branch + 1) * (lookback + 1)]
        rows = []
        for p in range(lookback):
            total = None
            for j in range(lookback + 1):
                src = messages[:, head + p - j] if p >= j else before[:, rim + lookback + p - j]
                term = taps[j] * src.astype(f32)
                total = term if total is None else total + term
            rows.append(total)
        feats.append(jnp.stack(rows, axis=1))
    return lax.reduce_precision(feats[0] * feats[1], exponent_bits=8, mantissa_bits=7)


def on_device(short_proj, medium_proj, long_proj, feature_taps, short_taps, medium_taps,
              long_rates, long_residues):
    _, length, channels = short_proj.shape
    groups, modes = long_rates.shape
    group_width = channels // groups
    lookback = feature_taps.shape[2] - 1
    reach = medium_taps.shape[1]
    short_count = short_taps.shape[0]
    assert reach <= length and short_count <= 17 and 0 < lookback <= 4 and modes % 8 == 0
    assert length % 16 == 0
    blocks = lax.axis_size("ctx")
    position = lax.axis_index("ctx")
    inline = blocks <= 8
    width = min(BLOCK, channels)
    steps = channels // width
    gpb = width // group_width
    small_rows = msg_layout(modes, lookback)[2]
    full_rows = small_rows + length
    _, early_rows = early_layout(lookback)

    ft = feature_taps.astype(f32).reshape(-1, channels)
    lane_block = lambda rows: pl.BlockSpec((rows, width), lambda j: (0, j))
    proj_block = pl.BlockSpec((3, length, width), lambda j: (0, 0, j))
    last_block = pl.BlockSpec((3, 16, width), lambda j: (0, length // 16 - 1, j))

    early = pl.pallas_call(
        functools.partial(rim_kernel, lookback=lookback),
        grid=(steps,),
        in_specs=[last_block, last_block, last_block, lane_block(ft.shape[0])],
        out_specs=lane_block(early_rows),
        out_shape=jax.ShapeDtypeStruct((early_rows, channels), bf16),
        scratch_shapes=[pltpu.VMEM((early_rows, TILE), f32)],
    )(short_proj, medium_proj, long_proj, ft)
    early_in = shifted(early, "ctx", 1)

    st = jnp.repeat(short_taps.astype(f32), group_width, axis=1)
    rates = long_rates
    loop_length = length * blocks
    wrap_scale = -jnp.expm1(-rates * loop_length)
    gains = long_residues * jnp.sqrt(
        -jnp.expm1(-2.0 * rates) * wrap_scale / (1.0 + jnp.exp(-rates * loop_length))
    )
    offsets = jnp.arange(length, dtype=f32)
    to_end = jnp.exp(-rates[:, :, None] * (length - 1.0 - offsets))
    late = jnp.where(offsets >= lookback, to_end, 0.0).reshape(groups * modes, length)
    wsh, wsl = split_glue(late)

    full, msg = pl.pallas_call(
        functools.partial(pre_kernel, lookback=lookback, modes=modes, group_width=group_width),
        grid=(steps,),
        in_specs=[
            proj_block,
            proj_block,
            proj_block,
            lane_block(ft.shape[0]),
            pl.BlockSpec((gpb * modes, length), lambda j: (j, 0)),
            pl.BlockSpec((gpb * modes, length), lambda j: (j, 0)),
        ],
        out_specs=[lane_block(full_rows), lane_block(small_rows)],
        out_shape=[
            jax.ShapeDtypeStruct((full_rows, channels), bf16),
            jax.ShapeDtypeStruct((small_rows, channels), bf16),
        ],
        scratch_shapes=[pltpu.VMEM((small_rows, TILE), f32)],
        cost_estimate=pl.CostEstimate(
            flops=length * channels * (20 + 4 * TILE),
            transcendentals=0,
            bytes_accessed=length * channels * 18,
        ),
    )(short_proj, medium_proj, long_proj, ft, wsh, wsl)

    arrived = shifted(full, "ctx", 1)
    first_w = jnp.repeat(
        jnp.transpose(to_end[:, :, :lookback], (2, 1, 0)), group_width, axis=2
    )
    rate_c = jnp.repeat(rates.T, group_width, axis=1)
    wrap_c = jnp.repeat(wrap_scale.T, group_width, axis=1)
    powers = jnp.arange(blocks, dtype=f32)
    coef = jnp.exp(-rate_c[None] * (length * powers)[:, None, None]) / wrap_c[None]
    if inline:
        others = [shifted(msg, "ctx", k) for k in range(2, blocks)]
        extra = [coef, first_w, msg] + others
        extra_specs = [
            pl.BlockSpec((blocks, modes, width), lambda j: (0, 0, j)),
            pl.BlockSpec((lookback, modes, width), lambda j: (0, 0, j)),
        ] + [lane_block(small_rows)] * (blocks - 1)
    else:
        messages = lax.all_gather(msg, "ctx")[(position - jnp.arange(blocks)) % blocks]
        before = jnp.roll(messages, -1, axis=0)
        head_long = head_products(messages, before, ft, 2, lookback, modes)
        states = (
            messages[:, 0:modes].astype(f32)
            + messages[:, modes:2 * modes].astype(f32)
            + jnp.sum(first_w[None] * head_long[:, :, None, :], axis=1)
        )
        incoming = jnp.sum(coef * jnp.roll(states, -1, axis=0), axis=0)
        fix = head_products(messages[1:2], before[1:2], ft, 1, lookback, modes)[0]
        fix = jnp.pad(fix, ((0, 16 - lookback), (0, 0)))
        extra = [incoming, fix]
        extra_specs = [lane_block(modes), lane_block(16)]

    bm = jnp.concatenate(
        [
            jnp.zeros((groups, length - reach + 1), f32),
            medium_taps.astype(f32)[:, ::-1],
            jnp.zeros((groups, length - 1), f32),
        ],
        axis=1,
    )
    profile = jnp.sum(gains[:, :, None] * jnp.exp(-rates[:, :, None] * offsets), axis=1)
    bl = jnp.concatenate(
        [profile[:, :1], jnp.zeros((groups, length), f32), profile[:, :0:-1]], axis=1
    )
    starts = (gains[None] * jnp.exp(-rates[None] * (offsets + 1.0)[:, None, None])).reshape(
        length, groups * modes
    )
    ech, ecl = split_glue(starts)
    tm, tlh, tll = pl.pallas_call(
        toeplitz_kernel,
        grid=(steps,),
        in_specs=[pl.BlockSpec((gpb, 2 * length), lambda j: (j, 0))] * 2
        + [lane_block(small_rows)],
        out_specs=[
            pl.BlockSpec((gpb, length, 2 * length), lambda j: (j, 0, 0)),
            pl.BlockSpec((gpb, length, length), lambda j: (j, 0, 0)),
            pl.BlockSpec((gpb, length, length), lambda j: (j, 0, 0)),
        ],
        out_shape=[
            jax.ShapeDtypeStruct((groups, length, 2 * length), bf16),
            jax.ShapeDtypeStruct((groups, length, length), bf16),
            jax.ShapeDtypeStruct((groups, length, length), bf16),
        ],
        cost_estimate=pl.CostEstimate(
            flops=groups * length * length * 8,
            transcendentals=0,
            bytes_accessed=groups * length * length * 8,
        ),
    )(bm, bl, msg)

    half = lambda part: pl.BlockSpec((gpb, length, length), lambda j: (j, 0, part))
    plain = lambda: pl.BlockSpec((gpb, length, length), lambda j: (j, 0, 0))
    short_mixed, mpart, lpart, mq, lq = pl.pallas_call(
        functools.partial(own_kernel, lookback=lookback, group_width=group_width),
        grid=(steps,),
        in_specs=[
            proj_block,
            proj_block,
            proj_block,
            lane_block(early_rows),
            lane_block(ft.shape[0]),
            lane_block(short_count),
            half(1),
            plain(),
            plain(),
        ],
        out_specs=[lane_block(length)] * 5,
        out_shape=[jax.ShapeDtypeStruct((length, channels), bf16)]
        + [jax.ShapeDtypeStruct((length, channels), f32)] * 4,
        scratch_shapes=[pltpu.VMEM((length, TILE), f32)],
        cost_estimate=pl.CostEstimate(
            flops=groups * length * TILE * length * 6,
            transcendentals=0,
            bytes_accessed=groups * length * length * 6 + length * channels * 36,
        ),
    )(short_proj, medium_proj, long_proj, early_in, ft, st, tm, tlh, tll)

    medium_mixed, long_mixed = pl.pallas_call(
        functools.partial(final_kernel, lookback=lookback, modes=modes, group_width=group_width,
                          inline=inline, blocks=blocks),
        grid=(steps,),
        in_specs=[
            lane_block(full_rows),
            lane_block(ft.shape[0]),
            half(0),
            pl.BlockSpec((length, gpb * modes), lambda j: (0, j)),
            pl.BlockSpec((length, gpb * modes), lambda j: (0, j)),
            lane_block(length),
            lane_block(length),
            lane_block(length),
            lane_block(length),
        ] + extra_specs,
        out_specs=[lane_block(length)] * 2,
        out_shape=[jax.ShapeDtypeStruct((length, channels), bf16)] * 2,
        scratch_shapes=[pltpu.VMEM((length, TILE), bf16)],
        cost_estimate=pl.CostEstimate(
            flops=groups * length * TILE * length * 4,
            transcendentals=0,
            bytes_accessed=groups * length * length * 2 + length * channels * 24,
        ),
    )(arrived, ft, tm, ech, ecl, mpart, lpart, mq, lq, *extra)
    return short_mixed, medium_mixed, long_mixed


def solution(mesh):
    return jax.shard_map(
        on_device,
        mesh=mesh,
        in_specs=(
            P(None, ("group", "ctx"), "chan"),
            P(None, ("group", "ctx"), "chan"),
            P(None, ("group", "ctx"), "chan"),
            P(None, None, None, "chan"),
            P(None, "chan"),
            P("chan", None),
            P("chan", None),
            P("chan", None),
        ),
        out_specs=(
            P(("group", "ctx"), "chan"),
            P(("group", "ctx"), "chan"),
            P(("group", "ctx"), "chan"),
        ),
        check_vma=False,
    )
```

```python
import functools

import jax
import jax.numpy as jnp
from jax import lax
from jax.experimental import pallas as pl
from jax.experimental.pallas import tpu as pltpu
from jax.sharding import PartitionSpec as P

f32 = jnp.float32
bf16 = jnp.bfloat16
TILE = 128
BLOCK = 512


def shifted(block, axis, distance):
    size = lax.axis_size(axis)
    route = [((i - distance) % size, i) for i in range(size)]
    return lax.ppermute(block, axis, route)


def split_bf16(x):
    hi = x.astype(bf16)
    return hi, (x - hi.astype(f32)).astype(bf16)


def split_glue(x):
    hi = lax.reduce_precision(x, exponent_bits=8, mantissa_bits=7)
    return hi.astype(bf16), (x - hi).astype(bf16)


KEPT = ((1, 1), (1, 2), (2, 1), (2, 2))
OTHER = ((0, 0), (0, 1), (0, 2), (1, 0), (2, 0))


def round16(x):
    return -(-x // 16) * 16


def layout(modes, lookback):
    state_row = 0
    kept_row = 2 * modes
    head_row = kept_row + len(KEPT) * lookback
    small_rows = round16(head_row + len(KEPT) * lookback)
    msg_rows = round16(small_rows + len(OTHER) * lookback)
    return state_row, kept_row, head_row, small_rows, msg_rows


def rim_slot(operator, branch, modes, lookback):
    _, kept_row, _, small_rows, _ = layout(modes, lookback)
    if (operator, branch) in KEPT:
        return kept_row + KEPT.index((operator, branch)) * lookback
    return small_rows + OTHER.index((operator, branch)) * lookback


def head_slot(operator, branch, modes, lookback):
    return layout(modes, lookback)[2] + KEPT.index((operator, branch)) * lookback


def feature_rows(proj_ref, rim_ref, ft_ref, lanes, operator, branch, index, lookback, modes=0):
    src = proj_ref[index, :, lanes].astype(f32)
    number = operator * 3 + branch
    row = lax.broadcasted_iota(jnp.int32, src.shape, 0)
    result = ft_ref[operator, branch, pl.ds(0, 1), lanes].astype(f32) * src
    for back in range(1, lookback + 1):
        moved = pltpu.roll(src, back, 0)
        for t in range(back if rim_ref is not None else 0):
            rim_row = rim_ref[pl.ds(rim_slot(operator, branch, modes, lookback) + lookback + t - back, 1), lanes]
            moved = jnp.where(row == t, rim_row.astype(f32), moved)
        result = result + ft_ref[operator, branch, pl.ds(back, 1), lanes].astype(f32) * moved
    return result


def toeplitz_kernel(bm_ref, bl_ref, after_ref, tm_ref, tlh_ref, tll_ref):
    per = bm_ref.shape[0]
    rows = tm_ref.shape[1]
    width = bm_ref.shape[1]
    for gl in range(per):
        base = jnp.broadcast_to(bm_ref[pl.ds(gl, 1), :], (rows, width))
        tm_ref[gl] = pltpu.roll(base, 0, 1, stride=1, stride_axis=0).astype(bf16)
        base = jnp.broadcast_to(bl_ref[pl.ds(gl, 1), :], (rows, width))
        full = pltpu.roll(base, 0, 1, stride=1, stride_axis=0)[:, :rows]
        hi, lo = split_bf16(full)
        tlh_ref[gl] = hi
        tll_ref[gl] = lo


def pre_kernel(sp_ref, mp_ref, lp_ref, ft_ref, wsh_ref, wsl_ref, full_ref, msg_ref, msg_scr,
               *, lookback, modes, group_width):
    length = sp_ref.shape[1]
    rows_per = TILE // group_width * modes
    state_row, _, _, small_rows, msg_rows = layout(modes, lookback)
    projs = (sp_ref, mp_ref, lp_ref)
    for sub in range(full_ref.shape[1] // TILE):
        lanes = pl.ds(sub * TILE, TILE)
        msg_scr[...] = jnp.zeros_like(msg_scr)
        for operator in range(3):
            for branch in range(3):
                for r in range(lookback):
                    msg_scr[pl.ds(rim_slot(operator, branch, modes, lookback) + r, 1), :] = projs[operator][
                        branch, pl.ds(length - lookback + r, 1), lanes
                    ].astype(f32)
        for operator in (1, 2):
            for branch in (1, 2):
                for r in range(lookback):
                    at = head_slot(operator, branch, modes, lookback) + r
                    msg_scr[pl.ds(at, 1), :] = projs[operator][branch, pl.ds(r, 1), lanes].astype(f32)
        products = []
        for operator, proj_ref in enumerate(projs):
            k_feat = feature_rows(proj_ref, None, ft_ref, lanes, operator, 1, 1, lookback)
            v_feat = feature_rows(proj_ref, None, ft_ref, lanes, operator, 2, 2, lookback)
            products.append((k_feat * v_feat).astype(bf16))
        zs, zm, zl = products
        full_ref[pl.ds(msg_rows, length), lanes] = zm
        full_ref[pl.ds(msg_rows + length, 16), lanes] = zs[length - 16:, :]
        weights = pl.ds(sub * rows_per, rows_per)
        full = jnp.dot(wsh_ref[weights, :], zl, preferred_element_type=f32) + jnp.dot(
            wsl_ref[weights, :], zl, preferred_element_type=f32
        )
        rows = lax.broadcasted_iota(jnp.int32, full.shape, 0) // modes
        lane_group = lax.broadcasted_iota(jnp.int32, full.shape, 1) // group_width
        full = jnp.where(rows == lane_group, full, 0.0)
        state = full[0:modes, :]
        for gl in range(1, rows_per // modes):
            state = state + full[gl * modes:(gl + 1) * modes, :]
        hi, lo = split_bf16(state)
        msg_scr[pl.ds(state_row, modes), :] = hi.astype(f32)
        msg_scr[pl.ds(state_row + modes, modes), :] = lo.astype(f32)
        packed = msg_scr[...].astype(bf16)
        msg_ref[:, lanes] = packed[:small_rows]
        full_ref[pl.ds(0, msg_rows), lanes] = packed


def head_rows(head_ref, before_ref, ft_ref, lanes, operator, lookback, modes):
    feats = []
    for branch in (1, 2):
        head = head_slot(operator, branch, modes, lookback)
        rim = rim_slot(operator, branch, modes, lookback)
        base = (operator * 3 + branch) * (lookback + 1)
        rows = []
        for p in range(lookback):
            total = None
            for j in range(lookback + 1):
                if p >= j:
                    src = head_ref[pl.ds(head + p - j, 1), lanes]
                else:
                    src = before_ref[pl.ds(rim + lookback + p - j, 1), lanes]
                term = ft_ref[operator, branch, pl.ds(j, 1), lanes].astype(f32) * src.astype(f32)
                total = term if total is None else total + term
            rows.append(total)
        feats.append(rows)
    return [(a * b).astype(bf16).astype(f32) for a, b in zip(*feats)]


def mix_kernel(*refs, lookback, modes, group_width, inline, blocks):
    (sp_ref, mp_ref, lp_ref, in_ref, ft_ref, st_ref, tm_ref, tlh_ref, tll_ref,
     ech_ref, ecl_ref) = refs[:11]
    if inline:
        coef_ref, first_ref = refs[11:13]
        by_shift = [refs[13], in_ref] + list(refs[14:12 + blocks])
        rest = refs[12 + blocks:]
    else:
        inc_ref, fix_ref = refs[11:13]
        rest = refs[13:]
    so_ref, mo_ref, lo_ref, y_scr, zext_scr = rest
    state_row, _, _, _, msg_rows = layout(modes, lookback)
    length = so_ref.shape[0]
    per = TILE // group_width
    row = lax.broadcasted_iota(jnp.int32, (length, TILE), 0)
    lane_group = lax.broadcasted_iota(jnp.int32, (length, TILE), 1) // group_width
    first = lax.broadcasted_iota(jnp.int32, (16, TILE), 0)
    for sub in range(so_ref.shape[1] // TILE):
        lanes = pl.ds(sub * TILE, TILE)
        if inline:
            incoming = None
            for k in range(blocks):
                now_ref = by_shift[k]
                head = head_rows(now_ref, by_shift[(k + 1) % blocks], ft_ref, lanes, 2, lookback, modes)
                state = now_ref[pl.ds(state_row, modes), lanes].astype(f32) + now_ref[
                    pl.ds(state_row + modes, modes), lanes
                ].astype(f32)
                for p in range(lookback):
                    state = state + first_ref[p, :, lanes] * head[p]
                term = coef_ref[(k - 1) % blocks, :, lanes] * state
                incoming = term if incoming is None else incoming + term
            fixed = head_rows(by_shift[1 % blocks], by_shift[2 % blocks], ft_ref, lanes, 1,
                              lookback, modes)
            fix = jnp.zeros((16, TILE), f32)
            for p in range(lookback):
                fix = jnp.where(first == p, fixed[p], fix)
        else:
            incoming = inc_ref[:, lanes]
            fix = fix_ref[:, lanes]
        feats = [
            [feature_rows(ref, in_ref, ft_ref, lanes, operator, branch, branch, lookback, modes)
             for branch in range(3)]
            for operator, ref in enumerate((sp_ref, mp_ref, lp_ref))
        ]
        zs, zm, zl = [(f[1] * f[2]).astype(bf16) for f in feats]

        zs = zs.astype(f32)
        y_scr[...] = zs
        y_scr[pl.ds(length - 16, 16), :] = in_ref[pl.ds(msg_rows + length, 16), lanes].astype(f32)
        wrapped = y_scr[...]
        conv = st_ref[pl.ds(0, 1), lanes] * zs
        for j in range(1, st_ref.shape[0]):
            back = jnp.where(row < j, pltpu.roll(wrapped, j, 0), pltpu.roll(zs, j, 0))
            conv = conv + st_ref[pl.ds(j, 1), lanes] * back
        so_ref[:, lanes] = (feats[0][0] * conv).astype(so_ref.dtype)

        zext_scr[pl.ds(0, length), :] = in_ref[pl.ds(msg_rows, length), lanes]
        zext_scr[pl.ds(0, 16), :] = jnp.where(
            first < lookback, fix, in_ref[pl.ds(msg_rows, 16), lanes].astype(f32)
        ).astype(bf16)
        zext_scr[pl.ds(length, length), :] = zm
        zext = zext_scr[...]
        acc = jnp.zeros((length, TILE), f32)
        for gl in range(per):
            part = jnp.dot(tm_ref[sub * per + gl], zext, preferred_element_type=f32)
            acc = jnp.where(lane_group == gl, part, acc)
        mo_ref[:, lanes] = (feats[1][0] * acc).astype(mo_ref.dtype)

        acc = jnp.zeros((length, TILE), f32)
        for gl in range(per):
            part = jnp.dot(tlh_ref[sub * per + gl], zl, preferred_element_type=f32) + jnp.dot(
                tll_ref[sub * per + gl], zl, preferred_element_type=f32
            )
            acc = jnp.where(lane_group == gl, part, acc)
        stacked = jnp.concatenate([incoming] * per, axis=0)
        srow = lax.broadcasted_iota(jnp.int32, stacked.shape, 0) // modes
        slane = lax.broadcasted_iota(jnp.int32, stacked.shape, 1) // group_width
        stacked = jnp.where(srow == slane, stacked, 0.0)
        ih, il = split_bf16(stacked)
        eh = ech_ref[:, lanes]
        el = ecl_ref[:, lanes]
        carried = (
            jnp.dot(eh, ih, preferred_element_type=f32)
            + jnp.dot(eh, il, preferred_element_type=f32)
            + jnp.dot(el, ih, preferred_element_type=f32)
        )
        lo_ref[:, lanes] = (feats[2][0] * (acc + carried)).astype(lo_ref.dtype)


def head_products(messages, before, ft, operator, lookback, modes):
    feats = []
    for branch in (1, 2):
        head = head_slot(operator, branch, modes, lookback)
        rim = rim_slot(operator, branch, modes, lookback)
        taps = ft[(operator * 3 + branch) * (lookback + 1):(operator * 3 + branch + 1) * (lookback + 1)]
        rows = []
        for p in range(lookback):
            total = None
            for j in range(lookback + 1):
                src = messages[:, head + p - j] if p >= j else before[:, rim + lookback + p - j]
                term = taps[j] * src.astype(f32)
                total = term if total is None else total + term
            rows.append(total)
        feats.append(jnp.stack(rows, axis=1))
    return lax.reduce_precision(feats[0] * feats[1], exponent_bits=8, mantissa_bits=7)


def on_device(short_proj, medium_proj, long_proj, feature_taps, short_taps, medium_taps,
              long_rates, long_residues):
    _, length, channels = short_proj.shape
    groups, modes = long_rates.shape
    group_width = channels // groups
    lookback = feature_taps.shape[2] - 1
    reach = medium_taps.shape[1]
    short_count = short_taps.shape[0]
    assert reach <= length and short_count <= 17 and 0 < lookback <= 4 and modes % 8 == 0
    blocks = lax.axis_size("ctx")
    position = lax.axis_index("ctx")
    inline = blocks <= 8
    width = min(BLOCK, channels)
    steps = channels // width
    gpb = width // group_width
    state_row, _, _, small_rows, msg_rows = layout(modes, lookback)
    full_rows = msg_rows + length + 16

    ft = feature_taps.astype(f32).reshape(-1, channels)
    st = jnp.repeat(short_taps.astype(f32), group_width, axis=1)
    rates = long_rates
    loop_length = length * blocks
    wrap_scale = -jnp.expm1(-rates * loop_length)
    gains = long_residues * jnp.sqrt(
        -jnp.expm1(-2.0 * rates) * wrap_scale / (1.0 + jnp.exp(-rates * loop_length))
    )
    offsets = jnp.arange(length, dtype=f32)
    to_end = jnp.exp(-rates[:, :, None] * (length - 1.0 - offsets))
    late = jnp.where(offsets >= lookback, to_end, 0.0).reshape(groups * modes, length)
    wsh, wsl = split_glue(late)

    lane_block = lambda rows: pl.BlockSpec((rows, width), lambda j: (0, j))
    taps_block = pl.BlockSpec((3, 3, lookback + 1, width), lambda j: (0, 0, 0, j))
    proj_block = pl.BlockSpec((3, length, width), lambda j: (0, 0, j))
    full, msg = pl.pallas_call(
        functools.partial(pre_kernel, lookback=lookback, modes=modes, group_width=group_width),
        grid=(steps,),
        in_specs=[
            proj_block,
            proj_block,
            proj_block,
            taps_block,
            pl.BlockSpec((gpb * modes, length), lambda j: (j, 0)),
            pl.BlockSpec((gpb * modes, length), lambda j: (j, 0)),
        ],
        out_specs=[lane_block(full_rows), lane_block(small_rows)],
        out_shape=[
            jax.ShapeDtypeStruct((full_rows, channels), bf16),
            jax.ShapeDtypeStruct((small_rows, channels), bf16),
        ],
        scratch_shapes=[pltpu.VMEM((msg_rows, TILE), f32)],
        cost_estimate=pl.CostEstimate(
            flops=length * channels * (30 + 4 * TILE),
            transcendentals=0,
            bytes_accessed=length * channels * 22,
        ),
    )(short_proj, medium_proj, long_proj, feature_taps, wsh, wsl)

    arrived = shifted(full, "ctx", 1)
    first_w = jnp.repeat(
        jnp.transpose(to_end[:, :, :lookback], (2, 1, 0)), group_width, axis=2
    )
    rate_c = jnp.repeat(rates.T, group_width, axis=1)
    wrap_c = jnp.repeat(wrap_scale.T, group_width, axis=1)
    powers = jnp.arange(blocks, dtype=f32)
    coef = jnp.exp(-rate_c[None] * (length * powers)[:, None, None]) / wrap_c[None]
    if inline:
        others = [shifted(msg, "ctx", k) for k in range(2, blocks)]
        extra = [coef, first_w, msg] + others
        extra_specs = [
            pl.BlockSpec((blocks, modes, width), lambda j: (0, 0, j)),
            pl.BlockSpec((lookback, modes, width), lambda j: (0, 0, j)),
        ] + [lane_block(small_rows)] * (blocks - 1)
    else:
        messages = lax.all_gather(msg, "ctx")[(position - jnp.arange(blocks)) % blocks]
        before = jnp.roll(messages, -1, axis=0)
        head_long = head_products(messages, before, ft, 2, lookback, modes)
        states = (
            messages[:, state_row:state_row + modes].astype(f32)
            + messages[:, state_row + modes:state_row + 2 * modes].astype(f32)
            + jnp.sum(first_w[None] * head_long[:, :, None, :], axis=1)
        )
        incoming = jnp.sum(coef * jnp.roll(states, -1, axis=0), axis=0)
        fix = head_products(messages[1:2], before[1:2], ft, 1, lookback, modes)[0]
        fix = jnp.pad(fix, ((0, 16 - lookback), (0, 0)))
        extra = [incoming, fix]
        extra_specs = [lane_block(modes), lane_block(16)]

    bm = jnp.concatenate(
        [
            jnp.zeros((groups, length - reach + 1), f32),
            medium_taps.astype(f32)[:, ::-1],
            jnp.zeros((groups, length - 1), f32),
        ],
        axis=1,
    )
    profile = jnp.sum(gains[:, :, None] * jnp.exp(-rates[:, :, None] * offsets), axis=1)
    bl = jnp.concatenate(
        [profile[:, :1], jnp.zeros((groups, length), f32), profile[:, :0:-1]], axis=1
    )
    starts = (gains[None] * jnp.exp(-rates[None] * (offsets + 1.0)[:, None, None])).reshape(
        length, groups * modes
    )
    ech, ecl = split_glue(starts)
    tm, tlh, tll = pl.pallas_call(
        toeplitz_kernel,
        grid=(steps,),
        in_specs=[pl.BlockSpec((gpb, 2 * length), lambda j: (j, 0))] * 2
        + [lane_block(small_rows)],
        out_specs=[
            pl.BlockSpec((gpb, length, 2 * length), lambda j: (j, 0, 0)),
            pl.BlockSpec((gpb, length, length), lambda j: (j, 0, 0)),
            pl.BlockSpec((gpb, length, length), lambda j: (j, 0, 0)),
        ],
        out_shape=[
            jax.ShapeDtypeStruct((groups, length, 2 * length), bf16),
            jax.ShapeDtypeStruct((groups, length, length), bf16),
            jax.ShapeDtypeStruct((groups, length, length), bf16),
        ],
        cost_estimate=pl.CostEstimate(
            flops=groups * length * length * 8,
            transcendentals=0,
            bytes_accessed=groups * length * length * 8,
        ),
    )(bm, bl, msg)

    outs = pl.pallas_call(
        functools.partial(mix_kernel, lookback=lookback, modes=modes, group_width=group_width,
                          inline=inline, blocks=blocks),
        grid=(steps,),
        in_specs=[
            proj_block,
            proj_block,
            proj_block,
            lane_block(full_rows),
            taps_block,
            lane_block(short_count),
            pl.BlockSpec((gpb, length, 2 * length), lambda j: (j, 0, 0)),
            pl.BlockSpec((gpb, length, length), lambda j: (j, 0, 0)),
            pl.BlockSpec((gpb, length, length), lambda j: (j, 0, 0)),
            pl.BlockSpec((length, gpb * modes), lambda j: (0, j)),
            pl.BlockSpec((length, gpb * modes), lambda j: (0, j)),
        ] + extra_specs,
        out_specs=[lane_block(length)] * 3,
        out_shape=[jax.ShapeDtypeStruct((length, channels), bf16)] * 3,
        scratch_shapes=[
            pltpu.VMEM((length, TILE), f32),
            pltpu.VMEM((2 * length, TILE), bf16),
        ],
        cost_estimate=pl.CostEstimate(
            flops=groups * length * TILE * length * 10,
            transcendentals=0,
            bytes_accessed=groups * length * length * 8 + length * channels * 24,
        ),
    )(short_proj, medium_proj, long_proj, arrived, feature_taps, st, tm, tlh, tll, ech, ecl, *extra)
    return tuple(outs)


def solution(mesh):
    return jax.shard_map(
        on_device,
        mesh=mesh,
        in_specs=(
            P(None, ("group", "ctx"), "chan"),
            P(None, ("group", "ctx"), "chan"),
            P(None, ("group", "ctx"), "chan"),
            P(None, None, None, "chan"),
            P(None, "chan"),
            P("chan", None),
            P("chan", None),
            P("chan", None),
        ),
        out_specs=(
            P(("group", "ctx"), "chan"),
            P(("group", "ctx"), "chan"),
            P(("group", "ctx"), "chan"),
        ),
        check_vma=False,
    )
```

```python
import functools

import jax
import jax.numpy as jnp
from jax import lax
from jax.experimental import pallas as pl
from jax.experimental.pallas import tpu as pltpu
from jax.sharding import PartitionSpec as P

f32 = jnp.float32
bf16 = jnp.bfloat16
TILE = 128
BLOCK = 512


def shifted(block, axis, distance):
    size = lax.axis_size(axis)
    route = [((i - distance) % size, i) for i in range(size)]
    return lax.ppermute(block, axis, route)


def split_bf16(x):
    hi = x.astype(bf16)
    return hi, (x - hi.astype(f32)).astype(bf16)


def split_glue(x):
    hi = lax.reduce_precision(x, exponent_bits=8, mantissa_bits=7)
    return hi.astype(bf16), (x - hi).astype(bf16)


KEPT = ((1, 1), (1, 2), (2, 1), (2, 2))
OTHER = ((0, 0), (0, 1), (0, 2), (1, 0), (2, 0))


def round16(x):
    return -(-x // 16) * 16


def layout(modes, lookback):
    state_row = 0
    kept_row = 2 * modes
    head_row = kept_row + len(KEPT) * lookback
    small_rows = round16(head_row + len(KEPT) * lookback)
    msg_rows = round16(small_rows + len(OTHER) * lookback)
    return state_row, kept_row, head_row, small_rows, msg_rows


def rim_slot(operator, branch, modes, lookback):
    _, kept_row, _, small_rows, _ = layout(modes, lookback)
    if (operator, branch) in KEPT:
        return kept_row + KEPT.index((operator, branch)) * lookback
    return small_rows + OTHER.index((operator, branch)) * lookback


def head_slot(operator, branch, modes, lookback):
    return layout(modes, lookback)[2] + KEPT.index((operator, branch)) * lookback


def feature_rows(proj_ref, rim_ref, ft_ref, lanes, operator, branch, index, lookback, modes=0,
                 rows=None):
    if rows is None:
        src = proj_ref[index, :, lanes].astype(f32)
    else:
        src = proj_ref[index, pl.ds(proj_ref.shape[1] - rows, rows), lanes].astype(f32)
    number = operator * 3 + branch
    row = lax.broadcasted_iota(jnp.int32, src.shape, 0)
    result = ft_ref[operator, branch, pl.ds(0, 1), lanes].astype(f32) * src
    for back in range(1, lookback + 1):
        moved = pltpu.roll(src, back, 0)
        for t in range(back if rim_ref is not None else 0):
            rim_row = rim_ref[pl.ds(rim_slot(operator, branch, modes, lookback) + lookback + t - back, 1), lanes]
            moved = jnp.where(row == t, rim_row.astype(f32), moved)
        result = result + ft_ref[operator, branch, pl.ds(back, 1), lanes].astype(f32) * moved
    return result


def toeplitz_kernel(bm_ref, bl_ref, after_ref, tm_ref, tlh_ref, tll_ref):
    per = bm_ref.shape[0]
    rows = tm_ref.shape[1]
    width = bm_ref.shape[1]
    for gl in range(per):
        base = jnp.broadcast_to(bm_ref[pl.ds(gl, 1), :], (rows, width))
        tm_ref[gl] = pltpu.roll(base, 0, 1, stride=1, stride_axis=0).astype(bf16)
        base = jnp.broadcast_to(bl_ref[pl.ds(gl, 1), :], (rows, width))
        full = pltpu.roll(base, 0, 1, stride=1, stride_axis=0)[:, :rows]
        hi, lo = split_bf16(full)
        tlh_ref[gl] = hi
        tll_ref[gl] = lo


def pre_kernel(sp_ref, mp_ref, lp_ref, ft_ref, rate_ref, full_ref, msg_ref, msg_scr,
               *, lookback, modes, group_width):
    length = sp_ref.shape[1]
    rows_per = TILE // group_width * modes
    state_row, _, _, small_rows, msg_rows = layout(modes, lookback)
    projs = (sp_ref, mp_ref, lp_ref)
    for sub in range(full_ref.shape[1] // TILE):
        lanes = pl.ds(sub * TILE, TILE)
        msg_scr[...] = jnp.zeros_like(msg_scr)
        for operator in range(3):
            for branch in range(3):
                for r in range(lookback):
                    msg_scr[pl.ds(rim_slot(operator, branch, modes, lookback) + r, 1), :] = projs[operator][
                        branch, pl.ds(length - lookback + r, 1), lanes
                    ].astype(f32)
        for operator in (1, 2):
            for branch in (1, 2):
                for r in range(lookback):
                    at = head_slot(operator, branch, modes, lookback) + r
                    msg_scr[pl.ds(at, 1), :] = projs[operator][branch, pl.ds(r, 1), lanes].astype(f32)
        products = []
        for operator, proj_ref in enumerate(projs):
            k_feat = feature_rows(proj_ref, None, ft_ref, lanes, operator, 1, 1, lookback,
                                  rows=16 if operator == 0 else None)
            v_feat = feature_rows(proj_ref, None, ft_ref, lanes, operator, 2, 2, lookback,
                                  rows=16 if operator == 0 else None)
            products.append((k_feat * v_feat).astype(bf16))
        zs, zm, zl = products
        full_ref[pl.ds(msg_rows, length), lanes] = zm
        full_ref[pl.ds(msg_rows + length, 16), lanes] = zs
        rate = rate_ref[pl.ds(sub * rows_per, rows_per), :]
        place = lax.broadcasted_iota(jnp.int32, (rows_per, length), 1)
        weights = jnp.where(
            place >= lookback, jnp.exp(-rate * (length - 1 - place).astype(f32)), 0.0
        )
        wh, wl = split_bf16(weights)
        full = jnp.dot(wh, zl, preferred_element_type=f32) + jnp.dot(
            wl, zl, preferred_element_type=f32
        )
        rows = lax.broadcasted_iota(jnp.int32, full.shape, 0) // modes
        lane_group = lax.broadcasted_iota(jnp.int32, full.shape, 1) // group_width
        full = jnp.where(rows == lane_group, full, 0.0)
        state = full[0:modes, :]
        for gl in range(1, rows_per // modes):
            state = state + full[gl * modes:(gl + 1) * modes, :]
        hi, lo = split_bf16(state)
        msg_scr[pl.ds(state_row, modes), :] = hi.astype(f32)
        msg_scr[pl.ds(state_row + modes, modes), :] = lo.astype(f32)
        packed = msg_scr[...].astype(bf16)
        msg_ref[:, lanes] = packed[:small_rows]
        full_ref[pl.ds(0, msg_rows), lanes] = packed


def head_rows(head_ref, before_ref, ft_ref, lanes, operator, lookback, modes):
    feats = []
    for branch in (1, 2):
        head = head_slot(operator, branch, modes, lookback)
        rim = rim_slot(operator, branch, modes, lookback)
        base = (operator * 3 + branch) * (lookback + 1)
        rows = []
        for p in range(lookback):
            total = None
            for j in range(lookback + 1):
                if p >= j:
                    src = head_ref[pl.ds(head + p - j, 1), lanes]
                else:
                    src = before_ref[pl.ds(rim + lookback + p - j, 1), lanes]
                term = ft_ref[operator, branch, pl.ds(j, 1), lanes].astype(f32) * src.astype(f32)
                total = term if total is None else total + term
            rows.append(total)
        feats.append(rows)
    return [(a * b).astype(bf16).astype(f32) for a, b in zip(*feats)]


def mix_kernel(*refs, lookback, modes, group_width, inline, blocks):
    (sp_ref, mp_ref, lp_ref, in_ref, ft_ref, st_ref, tm_ref, tlh_ref, tll_ref,
     ech_ref, ecl_ref) = refs[:11]
    if inline:
        coef_ref, first_ref = refs[11:13]
        by_shift = [refs[13], in_ref] + list(refs[14:12 + blocks])
        rest = refs[12 + blocks:]
    else:
        inc_ref, fix_ref = refs[11:13]
        rest = refs[13:]
    so_ref, mo_ref, lo_ref, y_scr, zext_scr = rest
    state_row, _, _, _, msg_rows = layout(modes, lookback)
    length = so_ref.shape[0]
    per = TILE // group_width
    row = lax.broadcasted_iota(jnp.int32, (length, TILE), 0)
    lane_group = lax.broadcasted_iota(jnp.int32, (length, TILE), 1) // group_width
    first = lax.broadcasted_iota(jnp.int32, (16, TILE), 0)
    for sub in range(so_ref.shape[1] // TILE):
        lanes = pl.ds(sub * TILE, TILE)
        if inline:
            incoming = None
            for k in range(blocks):
                now_ref = by_shift[k]
                head = head_rows(now_ref, by_shift[(k + 1) % blocks], ft_ref, lanes, 2, lookback, modes)
                state = now_ref[pl.ds(state_row, modes), lanes].astype(f32) + now_ref[
                    pl.ds(state_row + modes, modes), lanes
                ].astype(f32)
                for p in range(lookback):
                    state = state + first_ref[p, :, lanes] * head[p]
                term = coef_ref[(k - 1) % blocks, :, lanes] * state
                incoming = term if incoming is None else incoming + term
            fixed = head_rows(by_shift[1 % blocks], by_shift[2 % blocks], ft_ref, lanes, 1,
                              lookback, modes)
            fix = jnp.zeros((16, TILE), f32)
            for p in range(lookback):
                fix = jnp.where(first == p, fixed[p], fix)
        else:
            incoming = inc_ref[:, lanes]
            fix = fix_ref[:, lanes]
        feats = [
            [feature_rows(ref, in_ref, ft_ref, lanes, operator, branch, branch, lookback, modes)
             for branch in range(3)]
            for operator, ref in enumerate((sp_ref, mp_ref, lp_ref))
        ]
        zs, zm, zl = [(f[1] * f[2]).astype(bf16) for f in feats]

        zs = zs.astype(f32)
        y_scr[...] = zs
        y_scr[pl.ds(length - 16, 16), :] = in_ref[pl.ds(msg_rows + length, 16), lanes].astype(f32)
        wrapped = y_scr[...]
        conv = st_ref[pl.ds(0, 1), lanes] * zs
        for j in range(1, st_ref.shape[0]):
            back = jnp.where(row < j, pltpu.roll(wrapped, j, 0), pltpu.roll(zs, j, 0))
            conv = conv + st_ref[pl.ds(j, 1), lanes] * back
        so_ref[:, lanes] = (feats[0][0] * conv).astype(so_ref.dtype)

        zext_scr[pl.ds(0, length), :] = in_ref[pl.ds(msg_rows, length), lanes]
        zext_scr[pl.ds(0, 16), :] = jnp.where(
            first < lookback, fix, in_ref[pl.ds(msg_rows, 16), lanes].astype(f32)
        ).astype(bf16)
        zext_scr[pl.ds(length, length), :] = zm
        zext = zext_scr[...]
        acc = jnp.zeros((length, TILE), f32)
        for gl in range(per):
            part = jnp.dot(tm_ref[sub * per + gl], zext, preferred_element_type=f32)
            acc = jnp.where(lane_group == gl, part, acc)
        mo_ref[:, lanes] = (feats[1][0] * acc).astype(mo_ref.dtype)

        acc = jnp.zeros((length, TILE), f32)
        for gl in range(per):
            part = jnp.dot(tlh_ref[sub * per + gl], zl, preferred_element_type=f32) + jnp.dot(
                tll_ref[sub * per + gl], zl, preferred_element_type=f32
            )
            acc = jnp.where(lane_group == gl, part, acc)
        stacked = jnp.concatenate([incoming] * per, axis=0)
        srow = lax.broadcasted_iota(jnp.int32, stacked.shape, 0) // modes
        slane = lax.broadcasted_iota(jnp.int32, stacked.shape, 1) // group_width
        stacked = jnp.where(srow == slane, stacked, 0.0)
        ih, il = split_bf16(stacked)
        eh = ech_ref[:, lanes]
        el = ecl_ref[:, lanes]
        carried = (
            jnp.dot(eh, ih, preferred_element_type=f32)
            + jnp.dot(eh, il, preferred_element_type=f32)
            + jnp.dot(el, ih, preferred_element_type=f32)
        )
        lo_ref[:, lanes] = (feats[2][0] * (acc + carried)).astype(lo_ref.dtype)


def head_products(messages, before, ft, operator, lookback, modes):
    feats = []
    for branch in (1, 2):
        head = head_slot(operator, branch, modes, lookback)
        rim = rim_slot(operator, branch, modes, lookback)
        taps = ft[(operator * 3 + branch) * (lookback + 1):(operator * 3 + branch + 1) * (lookback + 1)]
        rows = []
        for p in range(lookback):
            total = None
            for j in range(lookback + 1):
                src = messages[:, head + p - j] if p >= j else before[:, rim + lookback + p - j]
                term = taps[j] * src.astype(f32)
                total = term if total is None else total + term
            rows.append(total)
        feats.append(jnp.stack(rows, axis=1))
    return lax.reduce_precision(feats[0] * feats[1], exponent_bits=8, mantissa_bits=7)


def on_device(short_proj, medium_proj, long_proj, feature_taps, short_taps, medium_taps,
              long_rates, long_residues):
    _, length, channels = short_proj.shape
    groups, modes = long_rates.shape
    group_width = channels // groups
    lookback = feature_taps.shape[2] - 1
    reach = medium_taps.shape[1]
    short_count = short_taps.shape[0]
    assert reach <= length and short_count <= 17 and 0 < lookback <= 4 and modes % 8 == 0
    blocks = lax.axis_size("ctx")
    position = lax.axis_index("ctx")
    inline = blocks <= 8
    width = min(BLOCK, channels)
    steps = channels // width
    gpb = width // group_width
    state_row, _, _, small_rows, msg_rows = layout(modes, lookback)
    full_rows = msg_rows + length + 16

    ft = feature_taps.astype(f32).reshape(-1, channels)
    st = jnp.repeat(short_taps.astype(f32), group_width, axis=1)
    rates = long_rates
    loop_length = length * blocks
    wrap_scale = -jnp.expm1(-rates * loop_length)
    gains = long_residues * jnp.sqrt(
        -jnp.expm1(-2.0 * rates) * wrap_scale / (1.0 + jnp.exp(-rates * loop_length))
    )
    offsets = jnp.arange(length, dtype=f32)
    to_end = jnp.exp(-rates[:, :, None] * (length - 1.0 - offsets))
    rate_col = rates.reshape(groups * modes, 1)

    lane_block = lambda rows: pl.BlockSpec((rows, width), lambda j: (0, j))
    taps_block = pl.BlockSpec((3, 3, lookback + 1, width), lambda j: (0, 0, 0, j))
    proj_block = pl.BlockSpec((3, length, width), lambda j: (0, 0, j))
    full, msg = pl.pallas_call(
        functools.partial(pre_kernel, lookback=lookback, modes=modes, group_width=group_width),
        grid=(steps,),
        in_specs=[
            proj_block,
            proj_block,
            proj_block,
            taps_block,
            pl.BlockSpec((gpb * modes, 1), lambda j: (j, 0)),
        ],
        out_specs=[lane_block(full_rows), lane_block(small_rows)],
        out_shape=[
            jax.ShapeDtypeStruct((full_rows, channels), bf16),
            jax.ShapeDtypeStruct((small_rows, channels), bf16),
        ],
        scratch_shapes=[pltpu.VMEM((msg_rows, TILE), f32)],
        cost_estimate=pl.CostEstimate(
            flops=length * channels * (30 + 4 * TILE),
            transcendentals=0,
            bytes_accessed=length * channels * 22,
        ),
    )(short_proj, medium_proj, long_proj, feature_taps, rate_col)

    arrived = shifted(full, "ctx", 1)
    first_w = jnp.repeat(
        jnp.transpose(to_end[:, :, :lookback], (2, 1, 0)), group_width, axis=2
    )
    rate_c = jnp.repeat(rates.T, group_width, axis=1)
    wrap_c = jnp.repeat(wrap_scale.T, group_width, axis=1)
    powers = jnp.arange(blocks, dtype=f32)
    coef = jnp.exp(-rate_c[None] * (length * powers)[:, None, None]) / wrap_c[None]
    if inline:
        others = [shifted(msg, "ctx", k) for k in range(2, blocks)]
        extra = [coef, first_w, msg] + others
        extra_specs = [
            pl.BlockSpec((blocks, modes, width), lambda j: (0, 0, j)),
            pl.BlockSpec((lookback, modes, width), lambda j: (0, 0, j)),
        ] + [lane_block(small_rows)] * (blocks - 1)
    else:
        messages = lax.all_gather(msg, "ctx")[(position - jnp.arange(blocks)) % blocks]
        before = jnp.roll(messages, -1, axis=0)
        head_long = head_products(messages, before, ft, 2, lookback, modes)
        states = (
            messages[:, state_row:state_row + modes].astype(f32)
            + messages[:, state_row + modes:state_row + 2 * modes].astype(f32)
            + jnp.sum(first_w[None] * head_long[:, :, None, :], axis=1)
        )
        incoming = jnp.sum(coef * jnp.roll(states, -1, axis=0), axis=0)
        fix = head_products(messages[1:2], before[1:2], ft, 1, lookback, modes)[0]
        fix = jnp.pad(fix, ((0, 16 - lookback), (0, 0)))
        extra = [incoming, fix]
        extra_specs = [lane_block(modes), lane_block(16)]

    bm = jnp.concatenate(
        [
            jnp.zeros((groups, length - reach + 1), f32),
            medium_taps.astype(f32)[:, ::-1],
            jnp.zeros((groups, length - 1), f32),
        ],
        axis=1,
    )
    profile = jnp.sum(gains[:, :, None] * jnp.exp(-rates[:, :, None] * offsets), axis=1)
    bl = jnp.concatenate(
        [profile[:, :1], jnp.zeros((groups, length), f32), profile[:, :0:-1]], axis=1
    )
    starts = (gains[None] * jnp.exp(-rates[None] * (offsets + 1.0)[:, None, None])).reshape(
        length, groups * modes
    )
    ech, ecl = split_glue(starts)
    tm, tlh, tll = pl.pallas_call(
        toeplitz_kernel,
        grid=(steps,),
        in_specs=[pl.BlockSpec((gpb, 2 * length), lambda j: (j, 0))] * 2
        + [lane_block(small_rows)],
        out_specs=[
            pl.BlockSpec((gpb, length, 2 * length), lambda j: (j, 0, 0)),
            pl.BlockSpec((gpb, length, length), lambda j: (j, 0, 0)),
            pl.BlockSpec((gpb, length, length), lambda j: (j, 0, 0)),
        ],
        out_shape=[
            jax.ShapeDtypeStruct((groups, length, 2 * length), bf16),
            jax.ShapeDtypeStruct((groups, length, length), bf16),
            jax.ShapeDtypeStruct((groups, length, length), bf16),
        ],
        cost_estimate=pl.CostEstimate(
            flops=groups * length * length * 8,
            transcendentals=0,
            bytes_accessed=groups * length * length * 8,
        ),
    )(bm, bl, msg)

    outs = pl.pallas_call(
        functools.partial(mix_kernel, lookback=lookback, modes=modes, group_width=group_width,
                          inline=inline, blocks=blocks),
        grid=(steps,),
        in_specs=[
            proj_block,
            proj_block,
            proj_block,
            lane_block(full_rows),
            taps_block,
            lane_block(short_count),
            pl.BlockSpec((gpb, length, 2 * length), lambda j: (j, 0, 0)),
            pl.BlockSpec((gpb, length, length), lambda j: (j, 0, 0)),
            pl.BlockSpec((gpb, length, length), lambda j: (j, 0, 0)),
            pl.BlockSpec((length, gpb * modes), lambda j: (0, j)),
            pl.BlockSpec((length, gpb * modes), lambda j: (0, j)),
        ] + extra_specs,
        out_specs=[lane_block(length)] * 3,
        out_shape=[jax.ShapeDtypeStruct((length, channels), bf16)] * 3,
        scratch_shapes=[
            pltpu.VMEM((length, TILE), f32),
            pltpu.VMEM((2 * length, TILE), bf16),
        ],
        cost_estimate=pl.CostEstimate(
            flops=groups * length * TILE * length * 10,
            transcendentals=0,
            bytes_accessed=groups * length * length * 8 + length * channels * 24,
        ),
    )(short_proj, medium_proj, long_proj, arrived, feature_taps, st, tm, tlh, tll, ech, ecl, *extra)
    return tuple(outs)


def solution(mesh):
    return jax.shard_map(
        on_device,
        mesh=mesh,
        in_specs=(
            P(None, ("group", "ctx"), "chan"),
            P(None, ("group", "ctx"), "chan"),
            P(None, ("group", "ctx"), "chan"),
            P(None, None, None, "chan"),
            P(None, "chan"),
            P("chan", None),
            P("chan", None),
            P("chan", None),
        ),
        out_specs=(
            P(("group", "ctx"), "chan"),
            P(("group", "ctx"), "chan"),
            P(("group", "ctx"), "chan"),
        ),
        check_vma=False,
    )
```

```python
import functools

import jax
import jax.numpy as jnp
from jax import lax
from jax.experimental import pallas as pl
from jax.experimental.pallas import tpu as pltpu
from jax.sharding import PartitionSpec as P

f32 = jnp.float32
bf16 = jnp.bfloat16
TILE = 128
BLOCK = 512


def shifted(block, axis, distance):
    size = lax.axis_size(axis)
    route = [((i - distance) % size, i) for i in range(size)]
    return lax.ppermute(block, axis, route)


def split_bf16(x):
    hi = x.astype(bf16)
    return hi, (x - hi.astype(f32)).astype(bf16)


def split_glue(x):
    hi = lax.reduce_precision(x, exponent_bits=8, mantissa_bits=7)
    return hi.astype(bf16), (x - hi).astype(bf16)


KEPT = ((1, 1), (1, 2), (2, 1), (2, 2))
OTHER = ((0, 0), (0, 1), (0, 2), (1, 0), (2, 0))


def round16(x):
    return -(-x // 16) * 16


def layout(modes, lookback):
    state_row = 0
    kept_row = 2 * modes
    head_row = kept_row + len(KEPT) * lookback
    small_rows = round16(head_row + len(KEPT) * lookback)
    msg_rows = round16(small_rows + len(OTHER) * lookback)
    return state_row, kept_row, head_row, small_rows, msg_rows


def rim_slot(operator, branch, modes, lookback):
    _, kept_row, _, small_rows, _ = layout(modes, lookback)
    if (operator, branch) in KEPT:
        return kept_row + KEPT.index((operator, branch)) * lookback
    return small_rows + OTHER.index((operator, branch)) * lookback


def head_slot(operator, branch, modes, lookback):
    return layout(modes, lookback)[2] + KEPT.index((operator, branch)) * lookback


def feature_rows(proj_ref, rim_ref, ft_ref, lanes, operator, branch, index, lookback, modes=0,
                 rows=None):
    if rows is None:
        src = proj_ref[index, :, lanes].astype(f32)
    else:
        src = proj_ref[index, pl.ds(0, rows), lanes].astype(f32)
    number = operator * 3 + branch
    row = lax.broadcasted_iota(jnp.int32, src.shape, 0)
    result = ft_ref[operator, branch, pl.ds(0, 1), lanes].astype(f32) * src
    for back in range(1, lookback + 1):
        moved = pltpu.roll(src, back, 0)
        for t in range(back if rim_ref is not None else 0):
            rim_row = rim_ref[pl.ds(rim_slot(operator, branch, modes, lookback) + lookback + t - back, 1), lanes]
            moved = jnp.where(row == t, rim_row.astype(f32), moved)
        result = result + ft_ref[operator, branch, pl.ds(back, 1), lanes].astype(f32) * moved
    return result


def toeplitz_kernel(bm_ref, bl_ref, after_ref, tm_ref, tlh_ref, tll_ref):
    per = bm_ref.shape[0]
    rows = tm_ref.shape[1]
    width = bm_ref.shape[1]
    for gl in range(per):
        base = jnp.broadcast_to(bm_ref[pl.ds(gl, 1), :], (rows, width))
        tm_ref[gl] = pltpu.roll(base, 0, 1, stride=1, stride_axis=0).astype(bf16)
        base = jnp.broadcast_to(bl_ref[pl.ds(gl, 1), :], (rows, width))
        full = pltpu.roll(base, 0, 1, stride=1, stride_axis=0)[:, :rows]
        hi, lo = split_bf16(full)
        tlh_ref[gl] = hi
        tll_ref[gl] = lo


def pre_kernel(sp_ref, mp_ref, lp_ref, ft_ref, wsh_ref, wsl_ref, full_ref, msg_ref,
               zs_ref, zm_ref, zl_ref, msg_scr,
               *, lookback, modes, group_width):
    length = sp_ref.shape[1]
    rows_per = TILE // group_width * modes
    state_row, _, _, small_rows, msg_rows = layout(modes, lookback)
    projs = (sp_ref, mp_ref, lp_ref)
    for sub in range(full_ref.shape[1] // TILE):
        lanes = pl.ds(sub * TILE, TILE)
        msg_scr[...] = jnp.zeros_like(msg_scr)
        for operator in range(3):
            for branch in range(3):
                for r in range(lookback):
                    msg_scr[pl.ds(rim_slot(operator, branch, modes, lookback) + r, 1), :] = projs[operator][
                        branch, pl.ds(length - lookback + r, 1), lanes
                    ].astype(f32)
        for operator in (1, 2):
            for branch in (1, 2):
                for r in range(lookback):
                    at = head_slot(operator, branch, modes, lookback) + r
                    msg_scr[pl.ds(at, 1), :] = projs[operator][branch, pl.ds(r, 1), lanes].astype(f32)
        products = []
        for operator, proj_ref in enumerate(projs):
            k_feat = feature_rows(proj_ref, None, ft_ref, lanes, operator, 1, 1, lookback)
            v_feat = feature_rows(proj_ref, None, ft_ref, lanes, operator, 2, 2, lookback)
            products.append((k_feat * v_feat).astype(bf16))
        zs, zm, zl = products
        zs_ref[:, lanes] = zs
        zm_ref[:, lanes] = zm
        zl_ref[:, lanes] = zl
        full_ref[pl.ds(msg_rows, length), lanes] = zm
        full_ref[pl.ds(msg_rows + length, 16), lanes] = zs[length - 16:, :]
        weights = pl.ds(sub * rows_per, rows_per)
        full = jnp.dot(wsh_ref[weights, :], zl, preferred_element_type=f32) + jnp.dot(
            wsl_ref[weights, :], zl, preferred_element_type=f32
        )
        rows = lax.broadcasted_iota(jnp.int32, full.shape, 0) // modes
        lane_group = lax.broadcasted_iota(jnp.int32, full.shape, 1) // group_width
        full = jnp.where(rows == lane_group, full, 0.0)
        state = full[0:modes, :]
        for gl in range(1, rows_per // modes):
            state = state + full[gl * modes:(gl + 1) * modes, :]
        hi, lo = split_bf16(state)
        msg_scr[pl.ds(state_row, modes), :] = hi.astype(f32)
        msg_scr[pl.ds(state_row + modes, modes), :] = lo.astype(f32)
        packed = msg_scr[...].astype(bf16)
        msg_ref[:, lanes] = packed[:small_rows]
        full_ref[pl.ds(0, msg_rows), lanes] = packed


def head_rows(head_ref, before_ref, ft_ref, lanes, operator, lookback, modes):
    feats = []
    for branch in (1, 2):
        head = head_slot(operator, branch, modes, lookback)
        rim = rim_slot(operator, branch, modes, lookback)
        base = (operator * 3 + branch) * (lookback + 1)
        rows = []
        for p in range(lookback):
            total = None
            for j in range(lookback + 1):
                if p >= j:
                    src = head_ref[pl.ds(head + p - j, 1), lanes]
                else:
                    src = before_ref[pl.ds(rim + lookback + p - j, 1), lanes]
                term = ft_ref[operator, branch, pl.ds(j, 1), lanes].astype(f32) * src.astype(f32)
                total = term if total is None else total + term
            rows.append(total)
        feats.append(rows)
    return [(a * b).astype(bf16).astype(f32) for a, b in zip(*feats)]


def mix_kernel(*refs, lookback, modes, group_width, inline, blocks):
    (sp_ref, mp_ref, lp_ref, in_ref, ft_ref, st_ref, tm_ref, tlh_ref, tll_ref,
     ech_ref, ecl_ref, zs_ref, zm_ref, zl_ref) = refs[:14]
    own_refs = (zs_ref, zm_ref, zl_ref)
    if inline:
        coef_ref, first_ref = refs[14:16]
        by_shift = [refs[16], in_ref] + list(refs[17:15 + blocks])
        rest = refs[15 + blocks:]
    else:
        inc_ref, fix_ref = refs[14:16]
        rest = refs[16:]
    so_ref, mo_ref, lo_ref, y_scr, zext_scr, z_scr = rest
    state_row, _, _, _, msg_rows = layout(modes, lookback)
    length = so_ref.shape[0]
    per = TILE // group_width
    row = lax.broadcasted_iota(jnp.int32, (length, TILE), 0)
    lane_group = lax.broadcasted_iota(jnp.int32, (length, TILE), 1) // group_width
    first = lax.broadcasted_iota(jnp.int32, (16, TILE), 0)
    for sub in range(so_ref.shape[1] // TILE):
        lanes = pl.ds(sub * TILE, TILE)
        if inline:
            incoming = None
            for k in range(blocks):
                now_ref = by_shift[k]
                head = head_rows(now_ref, by_shift[(k + 1) % blocks], ft_ref, lanes, 2, lookback, modes)
                state = now_ref[pl.ds(state_row, modes), lanes].astype(f32) + now_ref[
                    pl.ds(state_row + modes, modes), lanes
                ].astype(f32)
                for p in range(lookback):
                    state = state + first_ref[p, :, lanes] * head[p]
                term = coef_ref[(k - 1) % blocks, :, lanes] * state
                incoming = term if incoming is None else incoming + term
            fixed = head_rows(by_shift[1 % blocks], by_shift[2 % blocks], ft_ref, lanes, 1,
                              lookback, modes)
            fix = jnp.zeros((16, TILE), f32)
            for p in range(lookback):
                fix = jnp.where(first == p, fixed[p], fix)
        else:
            incoming = inc_ref[:, lanes]
            fix = fix_ref[:, lanes]
        queries = []
        products = []
        for operator, ref in enumerate((sp_ref, mp_ref, lp_ref)):
            queries.append(feature_rows(ref, in_ref, ft_ref, lanes, operator, 0, 0, lookback, modes))
            k_feat = feature_rows(ref, in_ref, ft_ref, lanes, operator, 1, 1, lookback, modes, rows=16)
            v_feat = feature_rows(ref, in_ref, ft_ref, lanes, operator, 2, 2, lookback, modes, rows=16)
            z_scr[operator] = own_refs[operator][:, lanes]
            z_scr[operator, pl.ds(0, 16), :] = (k_feat * v_feat).astype(bf16)
            products.append(z_scr[operator])
        zs, zm, zl = products
        feats = [[q] for q in queries]

        zs = zs.astype(f32)
        y_scr[...] = zs
        y_scr[pl.ds(length - 16, 16), :] = in_ref[pl.ds(msg_rows + length, 16), lanes].astype(f32)
        wrapped = y_scr[...]
        conv = st_ref[pl.ds(0, 1), lanes] * zs
        for j in range(1, st_ref.shape[0]):
            back = jnp.where(row < j, pltpu.roll(wrapped, j, 0), pltpu.roll(zs, j, 0))
            conv = conv + st_ref[pl.ds(j, 1), lanes] * back
        so_ref[:, lanes] = (feats[0][0] * conv).astype(so_ref.dtype)

        zext_scr[pl.ds(0, length), :] = in_ref[pl.ds(msg_rows, length), lanes]
        zext_scr[pl.ds(0, 16), :] = jnp.where(
            first < lookback, fix, in_ref[pl.ds(msg_rows, 16), lanes].astype(f32)
        ).astype(bf16)
        zext_scr[pl.ds(length, length), :] = zm
        zext = zext_scr[...]
        acc = jnp.zeros((length, TILE), f32)
        for gl in range(per):
            part = jnp.dot(tm_ref[sub * per + gl], zext, preferred_element_type=f32)
            acc = jnp.where(lane_group == gl, part, acc)
        mo_ref[:, lanes] = (feats[1][0] * acc).astype(mo_ref.dtype)

        acc = jnp.zeros((length, TILE), f32)
        for gl in range(per):
            part = jnp.dot(tlh_ref[sub * per + gl], zl, preferred_element_type=f32) + jnp.dot(
                tll_ref[sub * per + gl], zl, preferred_element_type=f32
            )
            acc = jnp.where(lane_group == gl, part, acc)
        stacked = jnp.concatenate([incoming] * per, axis=0)
        srow = lax.broadcasted_iota(jnp.int32, stacked.shape, 0) // modes
        slane = lax.broadcasted_iota(jnp.int32, stacked.shape, 1) // group_width
        stacked = jnp.where(srow == slane, stacked, 0.0)
        ih, il = split_bf16(stacked)
        eh = ech_ref[:, lanes]
        el = ecl_ref[:, lanes]
        carried = (
            jnp.dot(eh, ih, preferred_element_type=f32)
            + jnp.dot(eh, il, preferred_element_type=f32)
            + jnp.dot(el, ih, preferred_element_type=f32)
        )
        lo_ref[:, lanes] = (feats[2][0] * (acc + carried)).astype(lo_ref.dtype)


def head_products(messages, before, ft, operator, lookback, modes):
    feats = []
    for branch in (1, 2):
        head = head_slot(operator, branch, modes, lookback)
        rim = rim_slot(operator, branch, modes, lookback)
        taps = ft[(operator * 3 + branch) * (lookback + 1):(operator * 3 + branch + 1) * (lookback + 1)]
        rows = []
        for p in range(lookback):
            total = None
            for j in range(lookback + 1):
                src = messages[:, head + p - j] if p >= j else before[:, rim + lookback + p - j]
                term = taps[j] * src.astype(f32)
                total = term if total is None else total + term
            rows.append(total)
        feats.append(jnp.stack(rows, axis=1))
    return lax.reduce_precision(feats[0] * feats[1], exponent_bits=8, mantissa_bits=7)


def on_device(short_proj, medium_proj, long_proj, feature_taps, short_taps, medium_taps,
              long_rates, long_residues):
    _, length, channels = short_proj.shape
    groups, modes = long_rates.shape
    group_width = channels // groups
    lookback = feature_taps.shape[2] - 1
    reach = medium_taps.shape[1]
    short_count = short_taps.shape[0]
    assert reach <= length and short_count <= 17 and 0 < lookback <= 4 and modes % 8 == 0
    blocks = lax.axis_size("ctx")
    position = lax.axis_index("ctx")
    inline = blocks <= 8
    width = min(BLOCK, channels)
    steps = channels // width
    gpb = width // group_width
    state_row, _, _, small_rows, msg_rows = layout(modes, lookback)
    full_rows = msg_rows + length + 16

    ft = feature_taps.astype(f32).reshape(-1, channels)
    st = jnp.repeat(short_taps.astype(f32), group_width, axis=1)
    rates = long_rates
    loop_length = length * blocks
    wrap_scale = -jnp.expm1(-rates * loop_length)
    gains = long_residues * jnp.sqrt(
        -jnp.expm1(-2.0 * rates) * wrap_scale / (1.0 + jnp.exp(-rates * loop_length))
    )
    offsets = jnp.arange(length, dtype=f32)
    to_end = jnp.exp(-rates[:, :, None] * (length - 1.0 - offsets))
    late = jnp.where(offsets >= lookback, to_end, 0.0).reshape(groups * modes, length)
    wsh, wsl = split_glue(late)

    lane_block = lambda rows: pl.BlockSpec((rows, width), lambda j: (0, j))
    taps_block = pl.BlockSpec((3, 3, lookback + 1, width), lambda j: (0, 0, 0, j))
    proj_block = pl.BlockSpec((3, length, width), lambda j: (0, 0, j))
    full, msg, zs_own, zm_own, zl_own = pl.pallas_call(
        functools.partial(pre_kernel, lookback=lookback, modes=modes, group_width=group_width),
        grid=(steps,),
        in_specs=[
            proj_block,
            proj_block,
            proj_block,
            taps_block,
            pl.BlockSpec((gpb * modes, length), lambda j: (j, 0)),
            pl.BlockSpec((gpb * modes, length), lambda j: (j, 0)),
        ],
        out_specs=[lane_block(full_rows), lane_block(small_rows)] + [lane_block(length)] * 3,
        out_shape=[
            jax.ShapeDtypeStruct((full_rows, channels), bf16),
            jax.ShapeDtypeStruct((small_rows, channels), bf16),
        ] + [jax.ShapeDtypeStruct((length, channels), bf16)] * 3,
        scratch_shapes=[pltpu.VMEM((msg_rows, TILE), f32)],
        cost_estimate=pl.CostEstimate(
            flops=length * channels * (30 + 4 * TILE),
            transcendentals=0,
            bytes_accessed=length * channels * 22,
        ),
    )(short_proj, medium_proj, long_proj, feature_taps, wsh, wsl)

    arrived = shifted(full, "ctx", 1)
    first_w = jnp.repeat(
        jnp.transpose(to_end[:, :, :lookback], (2, 1, 0)), group_width, axis=2
    )
    rate_c = jnp.repeat(rates.T, group_width, axis=1)
    wrap_c = jnp.repeat(wrap_scale.T, group_width, axis=1)
    powers = jnp.arange(blocks, dtype=f32)
    coef = jnp.exp(-rate_c[None] * (length * powers)[:, None, None]) / wrap_c[None]
    if inline:
        others = [shifted(msg, "ctx", k) for k in range(2, blocks)]
        extra = [coef, first_w, msg] + others
        extra_specs = [
            pl.BlockSpec((blocks, modes, width), lambda j: (0, 0, j)),
            pl.BlockSpec((lookback, modes, width), lambda j: (0, 0, j)),
        ] + [lane_block(small_rows)] * (blocks - 1)
    else:
        messages = lax.all_gather(msg, "ctx")[(position - jnp.arange(blocks)) % blocks]
        before = jnp.roll(messages, -1, axis=0)
        head_long = head_products(messages, before, ft, 2, lookback, modes)
        states = (
            messages[:, state_row:state_row + modes].astype(f32)
            + messages[:, state_row + modes:state_row + 2 * modes].astype(f32)
            + jnp.sum(first_w[None] * head_long[:, :, None, :], axis=1)
        )
        incoming = jnp.sum(coef * jnp.roll(states, -1, axis=0), axis=0)
        fix = head_products(messages[1:2], before[1:2], ft, 1, lookback, modes)[0]
        fix = jnp.pad(fix, ((0, 16 - lookback), (0, 0)))
        extra = [incoming, fix]
        extra_specs = [lane_block(modes), lane_block(16)]

    bm = jnp.concatenate(
        [
            jnp.zeros((groups, length - reach + 1), f32),
            medium_taps.astype(f32)[:, ::-1],
            jnp.zeros((groups, length - 1), f32),
        ],
        axis=1,
    )
    profile = jnp.sum(gains[:, :, None] * jnp.exp(-rates[:, :, None] * offsets), axis=1)
    bl = jnp.concatenate(
        [profile[:, :1], jnp.zeros((groups, length), f32), profile[:, :0:-1]], axis=1
    )
    starts = (gains[None] * jnp.exp(-rates[None] * (offsets + 1.0)[:, None, None])).reshape(
        length, groups * modes
    )
    ech, ecl = split_glue(starts)
    tm, tlh, tll = pl.pallas_call(
        toeplitz_kernel,
        grid=(steps,),
        in_specs=[pl.BlockSpec((gpb, 2 * length), lambda j: (j, 0))] * 2
        + [lane_block(small_rows)],
        out_specs=[
            pl.BlockSpec((gpb, length, 2 * length), lambda j: (j, 0, 0)),
            pl.BlockSpec((gpb, length, length), lambda j: (j, 0, 0)),
            pl.BlockSpec((gpb, length, length), lambda j: (j, 0, 0)),
        ],
        out_shape=[
            jax.ShapeDtypeStruct((groups, length, 2 * length), bf16),
            jax.ShapeDtypeStruct((groups, length, length), bf16),
            jax.ShapeDtypeStruct((groups, length, length), bf16),
        ],
        cost_estimate=pl.CostEstimate(
            flops=groups * length * length * 8,
            transcendentals=0,
            bytes_accessed=groups * length * length * 8,
        ),
    )(bm, bl, msg)

    outs = pl.pallas_call(
        functools.partial(mix_kernel, lookback=lookback, modes=modes, group_width=group_width,
                          inline=inline, blocks=blocks),
        grid=(steps,),
        in_specs=[
            proj_block,
            proj_block,
            proj_block,
            lane_block(full_rows),
            taps_block,
            lane_block(short_count),
            pl.BlockSpec((gpb, length, 2 * length), lambda j: (j, 0, 0)),
            pl.BlockSpec((gpb, length, length), lambda j: (j, 0, 0)),
            pl.BlockSpec((gpb, length, length), lambda j: (j, 0, 0)),
            pl.BlockSpec((length, gpb * modes), lambda j: (0, j)),
            pl.BlockSpec((length, gpb * modes), lambda j: (0, j)),
            lane_block(length),
            lane_block(length),
            lane_block(length),
        ] + extra_specs,
        out_specs=[lane_block(length)] * 3,
        out_shape=[jax.ShapeDtypeStruct((length, channels), bf16)] * 3,
        scratch_shapes=[
            pltpu.VMEM((length, TILE), f32),
            pltpu.VMEM((2 * length, TILE), bf16),
            pltpu.VMEM((3, length, TILE), bf16),
        ],
        cost_estimate=pl.CostEstimate(
            flops=groups * length * TILE * length * 10,
            transcendentals=0,
            bytes_accessed=groups * length * length * 8 + length * channels * 24,
        ),
    )(short_proj, medium_proj, long_proj, arrived, feature_taps, st, tm, tlh, tll, ech, ecl,
      zs_own, zm_own, zl_own, *extra)
    return tuple(outs)


def solution(mesh):
    return jax.shard_map(
        on_device,
        mesh=mesh,
        in_specs=(
            P(None, ("group", "ctx"), "chan"),
            P(None, ("group", "ctx"), "chan"),
            P(None, ("group", "ctx"), "chan"),
            P(None, None, None, "chan"),
            P(None, "chan"),
            P("chan", None),
            P("chan", None),
            P("chan", None),
        ),
        out_specs=(
            P(("group", "ctx"), "chan"),
            P(("group", "ctx"), "chan"),
            P(("group", "ctx"), "chan"),
        ),
        check_vma=False,
    )
```

```python
import functools

import jax
import jax.numpy as jnp
from jax import lax
from jax.experimental import pallas as pl
from jax.experimental.pallas import tpu as pltpu
from jax.sharding import PartitionSpec as P

f32 = jnp.float32
bf16 = jnp.bfloat16
TILE = 128
BLOCK = 512


def shifted(block, axis, distance):
    size = lax.axis_size(axis)
    route = [((i - distance) % size, i) for i in range(size)]
    return lax.ppermute(block, axis, route)


def split_bf16(x):
    hi = x.astype(bf16)
    return hi, (x - hi.astype(f32)).astype(bf16)


def split_glue(x):
    hi = lax.reduce_precision(x, exponent_bits=8, mantissa_bits=7)
    return hi.astype(bf16), (x - hi).astype(bf16)


KEPT = ((1, 1), (1, 2), (2, 1), (2, 2))
OTHER = ((0, 0), (0, 1), (0, 2), (1, 0), (2, 0))


def round16(x):
    return -(-x // 16) * 16


def layout(modes, lookback):
    state_row = 0
    kept_row = modes
    head_row = kept_row + len(KEPT) * lookback
    small_rows = round16(head_row + len(KEPT) * lookback)
    msg_rows = round16(small_rows + len(OTHER) * lookback)
    return state_row, kept_row, head_row, small_rows, msg_rows


def rim_slot(operator, branch, modes, lookback):
    _, kept_row, _, small_rows, _ = layout(modes, lookback)
    if (operator, branch) in KEPT:
        return kept_row + KEPT.index((operator, branch)) * lookback
    return small_rows + OTHER.index((operator, branch)) * lookback


def head_slot(operator, branch, modes, lookback):
    return layout(modes, lookback)[2] + KEPT.index((operator, branch)) * lookback


def feature_rows(proj_ref, rim_ref, ft_ref, lanes, operator, branch, index, lookback, modes=0,
                 rows=None):
    if rows is None:
        src = proj_ref[index, :, lanes].astype(f32)
    else:
        src = proj_ref[index, pl.ds(0, rows), lanes].astype(f32)
    number = operator * 3 + branch
    row = lax.broadcasted_iota(jnp.int32, src.shape, 0)
    result = ft_ref[operator, branch, pl.ds(0, 1), lanes].astype(f32) * src
    for back in range(1, lookback + 1):
        moved = pltpu.roll(src, back, 0)
        for t in range(back if rim_ref is not None else 0):
            rim_row = rim_ref[pl.ds(rim_slot(operator, branch, modes, lookback) + lookback + t - back, 1), lanes]
            moved = jnp.where(row == t, rim_row.astype(f32), moved)
        result = result + ft_ref[operator, branch, pl.ds(back, 1), lanes].astype(f32) * moved
    return result


def toeplitz_kernel(bm_ref, bl_ref, after_ref, tm_ref, tlh_ref, tll_ref):
    per = bm_ref.shape[0]
    rows = tm_ref.shape[1]
    width = bm_ref.shape[1]
    for gl in range(per):
        base = jnp.broadcast_to(bm_ref[pl.ds(gl, 1), :], (rows, width))
        tm_ref[gl] = pltpu.roll(base, 0, 1, stride=1, stride_axis=0).astype(bf16)
        base = jnp.broadcast_to(bl_ref[pl.ds(gl, 1), :], (rows, width))
        full = pltpu.roll(base, 0, 1, stride=1, stride_axis=0)[:, :rows]
        hi, lo = split_bf16(full)
        tlh_ref[gl] = hi
        tll_ref[gl] = lo


def pre_kernel(sp_ref, mp_ref, lp_ref, ft_ref, wsh_ref, wsl_ref, full_ref, msg_ref,
               zs_ref, zm_ref, zl_ref, msg_scr,
               *, lookback, modes, group_width):
    length = sp_ref.shape[1]
    rows_per = TILE // group_width * modes
    state_row, _, _, small_rows, msg_rows = layout(modes, lookback)
    projs = (sp_ref, mp_ref, lp_ref)
    for sub in range(full_ref.shape[1] // TILE):
        lanes = pl.ds(sub * TILE, TILE)
        msg_scr[...] = jnp.zeros_like(msg_scr)
        for operator in range(3):
            for branch in range(3):
                for r in range(lookback):
                    msg_scr[pl.ds(rim_slot(operator, branch, modes, lookback) + r, 1), :] = projs[operator][
                        branch, pl.ds(length - lookback + r, 1), lanes
                    ].astype(f32)
        for operator in (1, 2):
            for branch in (1, 2):
                for r in range(lookback):
                    at = head_slot(operator, branch, modes, lookback) + r
                    msg_scr[pl.ds(at, 1), :] = projs[operator][branch, pl.ds(r, 1), lanes].astype(f32)
        products = []
        for operator, proj_ref in enumerate(projs):
            k_feat = feature_rows(proj_ref, None, ft_ref, lanes, operator, 1, 1, lookback)
            v_feat = feature_rows(proj_ref, None, ft_ref, lanes, operator, 2, 2, lookback)
            products.append((k_feat * v_feat).astype(bf16))
        zs, zm, zl = products
        zs_ref[:, lanes] = zs
        zm_ref[:, lanes] = zm
        zl_ref[:, lanes] = zl
        full_ref[pl.ds(msg_rows, length), lanes] = zm
        full_ref[pl.ds(msg_rows + length, 16), lanes] = zs[length - 16:, :]
        weights = pl.ds(sub * rows_per, rows_per)
        full = jnp.dot(wsh_ref[weights, :], zl, preferred_element_type=f32) + jnp.dot(
            wsl_ref[weights, :], zl, preferred_element_type=f32
        )
        rows = lax.broadcasted_iota(jnp.int32, full.shape, 0) // modes
        lane_group = lax.broadcasted_iota(jnp.int32, full.shape, 1) // group_width
        full = jnp.where(rows == lane_group, full, 0.0)
        state = full[0:modes, :]
        for gl in range(1, rows_per // modes):
            state = state + full[gl * modes:(gl + 1) * modes, :]
        msg_scr[pl.ds(state_row, modes), :] = state
        packed = msg_scr[...].astype(bf16)
        msg_ref[:, lanes] = packed[:small_rows]
        full_ref[pl.ds(0, msg_rows), lanes] = packed


def head_rows(head_ref, before_ref, ft_ref, lanes, operator, lookback, modes):
    feats = []
    for branch in (1, 2):
        head = head_slot(operator, branch, modes, lookback)
        rim = rim_slot(operator, branch, modes, lookback)
        base = (operator * 3 + branch) * (lookback + 1)
        rows = []
        for p in range(lookback):
            total = None
            for j in range(lookback + 1):
                if p >= j:
                    src = head_ref[pl.ds(head + p - j, 1), lanes]
                else:
                    src = before_ref[pl.ds(rim + lookback + p - j, 1), lanes]
                term = ft_ref[operator, branch, pl.ds(j, 1), lanes].astype(f32) * src.astype(f32)
                total = term if total is None else total + term
            rows.append(total)
        feats.append(rows)
    return [(a * b).astype(bf16).astype(f32) for a, b in zip(*feats)]


def mix_kernel(*refs, lookback, modes, group_width, inline, blocks):
    (sp_ref, mp_ref, lp_ref, in_ref, ft_ref, st_ref, tm_ref, tlh_ref, tll_ref,
     ech_ref, ecl_ref, zs_ref, zm_ref, zl_ref) = refs[:14]
    own_refs = (zs_ref, zm_ref, zl_ref)
    if inline:
        coef_ref, first_ref = refs[14:16]
        by_shift = [refs[16], in_ref] + list(refs[17:15 + blocks])
        rest = refs[15 + blocks:]
    else:
        inc_ref, fix_ref = refs[14:16]
        rest = refs[16:]
    so_ref, mo_ref, lo_ref, y_scr, zext_scr, z_scr = rest
    state_row, _, _, _, msg_rows = layout(modes, lookback)
    length = so_ref.shape[0]
    per = TILE // group_width
    row = lax.broadcasted_iota(jnp.int32, (length, TILE), 0)
    lane_group = lax.broadcasted_iota(jnp.int32, (length, TILE), 1) // group_width
    first = lax.broadcasted_iota(jnp.int32, (16, TILE), 0)
    for sub in range(so_ref.shape[1] // TILE):
        lanes = pl.ds(sub * TILE, TILE)
        if inline:
            incoming = None
            for k in range(blocks):
                now_ref = by_shift[k]
                head = head_rows(now_ref, by_shift[(k + 1) % blocks], ft_ref, lanes, 2, lookback, modes)
                state = now_ref[pl.ds(state_row, modes), lanes].astype(f32)
                for p in range(lookback):
                    state = state + first_ref[p, :, lanes] * head[p]
                term = coef_ref[(k - 1) % blocks, :, lanes] * state
                incoming = term if incoming is None else incoming + term
            fixed = head_rows(by_shift[1 % blocks], by_shift[2 % blocks], ft_ref, lanes, 1,
                              lookback, modes)
            fix = jnp.zeros((16, TILE), f32)
            for p in range(lookback):
                fix = jnp.where(first == p, fixed[p], fix)
        else:
            incoming = inc_ref[:, lanes]
            fix = fix_ref[:, lanes]
        queries = []
        products = []
        for operator, ref in enumerate((sp_ref, mp_ref, lp_ref)):
            queries.append(feature_rows(ref, in_ref, ft_ref, lanes, operator, 0, 0, lookback, modes))
            k_feat = feature_rows(ref, in_ref, ft_ref, lanes, operator, 1, 1, lookback, modes, rows=16)
            v_feat = feature_rows(ref, in_ref, ft_ref, lanes, operator, 2, 2, lookback, modes, rows=16)
            z_scr[operator] = own_refs[operator][:, lanes]
            z_scr[operator, pl.ds(0, 16), :] = (k_feat * v_feat).astype(bf16)
            products.append(z_scr[operator])
        zs, zm, zl = products
        feats = [[q] for q in queries]

        zs = zs.astype(f32)
        y_scr[...] = zs
        y_scr[pl.ds(length - 16, 16), :] = in_ref[pl.ds(msg_rows + length, 16), lanes].astype(f32)
        wrapped = y_scr[...]
        conv = st_ref[pl.ds(0, 1), lanes] * zs
        for j in range(1, st_ref.shape[0]):
            back = jnp.where(row < j, pltpu.roll(wrapped, j, 0), pltpu.roll(zs, j, 0))
            conv = conv + st_ref[pl.ds(j, 1), lanes] * back
        so_ref[:, lanes] = (feats[0][0] * conv).astype(so_ref.dtype)

        zext_scr[pl.ds(0, length), :] = in_ref[pl.ds(msg_rows, length), lanes]
        zext_scr[pl.ds(0, 16), :] = jnp.where(
            first < lookback, fix, in_ref[pl.ds(msg_rows, 16), lanes].astype(f32)
        ).astype(bf16)
        zext_scr[pl.ds(length, length), :] = zm
        zext = zext_scr[...]
        acc = jnp.zeros((length, TILE), f32)
        for gl in range(per):
            part = jnp.dot(tm_ref[sub * per + gl], zext, preferred_element_type=f32)
            acc = jnp.where(lane_group == gl, part, acc)
        mo_ref[:, lanes] = (feats[1][0] * acc).astype(mo_ref.dtype)

        acc = jnp.zeros((length, TILE), f32)
        for gl in range(per):
            part = jnp.dot(tlh_ref[sub * per + gl], zl, preferred_element_type=f32) + jnp.dot(
                tll_ref[sub * per + gl], zl, preferred_element_type=f32
            )
            acc = jnp.where(lane_group == gl, part, acc)
        stacked = jnp.concatenate([incoming] * per, axis=0)
        srow = lax.broadcasted_iota(jnp.int32, stacked.shape, 0) // modes
        slane = lax.broadcasted_iota(jnp.int32, stacked.shape, 1) // group_width
        stacked = jnp.where(srow == slane, stacked, 0.0)
        ih, il = split_bf16(stacked)
        eh = ech_ref[:, lanes]
        el = ecl_ref[:, lanes]
        carried = (
            jnp.dot(eh, ih, preferred_element_type=f32)
            + jnp.dot(eh, il, preferred_element_type=f32)
            + jnp.dot(el, ih, preferred_element_type=f32)
        )
        lo_ref[:, lanes] = (feats[2][0] * (acc + carried)).astype(lo_ref.dtype)


def head_products(messages, before, ft, operator, lookback, modes):
    feats = []
    for branch in (1, 2):
        head = head_slot(operator, branch, modes, lookback)
        rim = rim_slot(operator, branch, modes, lookback)
        taps = ft[(operator * 3 + branch) * (lookback + 1):(operator * 3 + branch + 1) * (lookback + 1)]
        rows = []
        for p in range(lookback):
            total = None
            for j in range(lookback + 1):
                src = messages[:, head + p - j] if p >= j else before[:, rim + lookback + p - j]
                term = taps[j] * src.astype(f32)
                total = term if total is None else total + term
            rows.append(total)
        feats.append(jnp.stack(rows, axis=1))
    return lax.reduce_precision(feats[0] * feats[1], exponent_bits=8, mantissa_bits=7)


def on_device(short_proj, medium_proj, long_proj, feature_taps, short_taps, medium_taps,
              long_rates, long_residues):
    _, length, channels = short_proj.shape
    groups, modes = long_rates.shape
    group_width = channels // groups
    lookback = feature_taps.shape[2] - 1
    reach = medium_taps.shape[1]
    short_count = short_taps.shape[0]
    assert reach <= length and short_count <= 17 and 0 < lookback <= 4 and modes % 8 == 0
    blocks = lax.axis_size("ctx")
    position = lax.axis_index("ctx")
    inline = blocks <= 8
    width = min(BLOCK, channels)
    steps = channels // width
    gpb = width // group_width
    state_row, _, _, small_rows, msg_rows = layout(modes, lookback)
    full_rows = msg_rows + length + 16

    ft = feature_taps.astype(f32).reshape(-1, channels)
    st = jnp.repeat(short_taps.astype(f32), group_width, axis=1)
    rates = long_rates
    loop_length = length * blocks
    wrap_scale = -jnp.expm1(-rates * loop_length)
    gains = long_residues * jnp.sqrt(
        -jnp.expm1(-2.0 * rates) * wrap_scale / (1.0 + jnp.exp(-rates * loop_length))
    )
    offsets = jnp.arange(length, dtype=f32)
    to_end = jnp.exp(-rates[:, :, None] * (length - 1.0 - offsets))
    late = jnp.where(offsets >= lookback, to_end, 0.0).reshape(groups * modes, length)
    wsh, wsl = split_glue(late)

    lane_block = lambda rows: pl.BlockSpec((rows, width), lambda j: (0, j))
    taps_block = pl.BlockSpec((3, 3, lookback + 1, width), lambda j: (0, 0, 0, j))
    proj_block = pl.BlockSpec((3, length, width), lambda j: (0, 0, j))
    full, msg, zs_own, zm_own, zl_own = pl.pallas_call(
        functools.partial(pre_kernel, lookback=lookback, modes=modes, group_width=group_width),
        grid=(steps,),
        in_specs=[
            proj_block,
            proj_block,
            proj_block,
            taps_block,
            pl.BlockSpec((gpb * modes, length), lambda j: (j, 0)),
            pl.BlockSpec((gpb * modes, length), lambda j: (j, 0)),
        ],
        out_specs=[lane_block(full_rows), lane_block(small_rows)] + [lane_block(length)] * 3,
        out_shape=[
            jax.ShapeDtypeStruct((full_rows, channels), bf16),
            jax.ShapeDtypeStruct((small_rows, channels), bf16),
        ] + [jax.ShapeDtypeStruct((length, channels), bf16)] * 3,
        scratch_shapes=[pltpu.VMEM((msg_rows, TILE), f32)],
        cost_estimate=pl.CostEstimate(
            flops=length * channels * (30 + 4 * TILE),
            transcendentals=0,
            bytes_accessed=length * channels * 22,
        ),
    )(short_proj, medium_proj, long_proj, feature_taps, wsh, wsl)

    arrived = shifted(full, "ctx", 1)
    first_w = jnp.repeat(
        jnp.transpose(to_end[:, :, :lookback], (2, 1, 0)), group_width, axis=2
    )
    rate_c = jnp.repeat(rates.T, group_width, axis=1)
    wrap_c = jnp.repeat(wrap_scale.T, group_width, axis=1)
    powers = jnp.arange(blocks, dtype=f32)
    coef = jnp.exp(-rate_c[None] * (length * powers)[:, None, None]) / wrap_c[None]
    if inline:
        others = [shifted(msg, "ctx", k) for k in range(2, blocks)]
        extra = [coef, first_w, msg] + others
        extra_specs = [
            pl.BlockSpec((blocks, modes, width), lambda j: (0, 0, j)),
            pl.BlockSpec((lookback, modes, width), lambda j: (0, 0, j)),
        ] + [lane_block(small_rows)] * (blocks - 1)
    else:
        messages = lax.all_gather(msg, "ctx")[(position - jnp.arange(blocks)) % blocks]
        before = jnp.roll(messages, -1, axis=0)
        head_long = head_products(messages, before, ft, 2, lookback, modes)
        states = (
            messages[:, state_row:state_row + modes].astype(f32)
            + jnp.sum(first_w[None] * head_long[:, :, None, :], axis=1)
        )
        incoming = jnp.sum(coef * jnp.roll(states, -1, axis=0), axis=0)
        fix = head_products(messages[1:2], before[1:2], ft, 1, lookback, modes)[0]
        fix = jnp.pad(fix, ((0, 16 - lookback), (0, 0)))
        extra = [incoming, fix]
        extra_specs = [lane_block(modes), lane_block(16)]

    bm = jnp.concatenate(
        [
            jnp.zeros((groups, length - reach + 1), f32),
            medium_taps.astype(f32)[:, ::-1],
            jnp.zeros((groups, length - 1), f32),
        ],
        axis=1,
    )
    profile = jnp.sum(gains[:, :, None] * jnp.exp(-rates[:, :, None] * offsets), axis=1)
    bl = jnp.concatenate(
        [profile[:, :1], jnp.zeros((groups, length), f32), profile[:, :0:-1]], axis=1
    )
    starts = (gains[None] * jnp.exp(-rates[None] * (offsets + 1.0)[:, None, None])).reshape(
        length, groups * modes
    )
    ech, ecl = split_glue(starts)
    tm, tlh, tll = pl.pallas_call(
        toeplitz_kernel,
        grid=(steps,),
        in_specs=[pl.BlockSpec((gpb, 2 * length), lambda j: (j, 0))] * 2
        + [lane_block(small_rows)],
        out_specs=[
            pl.BlockSpec((gpb, length, 2 * length), lambda j: (j, 0, 0)),
            pl.BlockSpec((gpb, length, length), lambda j: (j, 0, 0)),
            pl.BlockSpec((gpb, length, length), lambda j: (j, 0, 0)),
        ],
        out_shape=[
            jax.ShapeDtypeStruct((groups, length, 2 * length), bf16),
            jax.ShapeDtypeStruct((groups, length, length), bf16),
            jax.ShapeDtypeStruct((groups, length, length), bf16),
        ],
        cost_estimate=pl.CostEstimate(
            flops=groups * length * length * 8,
            transcendentals=0,
            bytes_accessed=groups * length * length * 8,
        ),
    )(bm, bl, msg)

    outs = pl.pallas_call(
        functools.partial(mix_kernel, lookback=lookback, modes=modes, group_width=group_width,
                          inline=inline, blocks=blocks),
        grid=(steps,),
        in_specs=[
            proj_block,
            proj_block,
            proj_block,
            lane_block(full_rows),
            taps_block,
            lane_block(short_count),
            pl.BlockSpec((gpb, length, 2 * length), lambda j: (j, 0, 0)),
            pl.BlockSpec((gpb, length, length), lambda j: (j, 0, 0)),
            pl.BlockSpec((gpb, length, length), lambda j: (j, 0, 0)),
            pl.BlockSpec((length, gpb * modes), lambda j: (0, j)),
            pl.BlockSpec((length, gpb * modes), lambda j: (0, j)),
            lane_block(length),
            lane_block(length),
            lane_block(length),
        ] + extra_specs,
        out_specs=[lane_block(length)] * 3,
        out_shape=[jax.ShapeDtypeStruct((length, channels), bf16)] * 3,
        scratch_shapes=[
            pltpu.VMEM((length, TILE), f32),
            pltpu.VMEM((2 * length, TILE), bf16),
            pltpu.VMEM((3, length, TILE), bf16),
        ],
        cost_estimate=pl.CostEstimate(
            flops=groups * length * TILE * length * 10,
            transcendentals=0,
            bytes_accessed=groups * length * length * 8 + length * channels * 24,
        ),
    )(short_proj, medium_proj, long_proj, arrived, feature_taps, st, tm, tlh, tll, ech, ecl,
      zs_own, zm_own, zl_own, *extra)
    return tuple(outs)


def solution(mesh):
    return jax.shard_map(
        on_device,
        mesh=mesh,
        in_specs=(
            P(None, ("group", "ctx"), "chan"),
            P(None, ("group", "ctx"), "chan"),
            P(None, ("group", "ctx"), "chan"),
            P(None, None, None, "chan"),
            P(None, "chan"),
            P("chan", None),
            P("chan", None),
            P("chan", None),
        ),
        out_specs=(
            P(("group", "ctx"), "chan"),
            P(("group", "ctx"), "chan"),
            P(("group", "ctx"), "chan"),
        ),
        check_vma=False,
    )
```

```python
import functools

import jax
import jax.numpy as jnp
from jax import lax
from jax.experimental import pallas as pl
from jax.experimental.pallas import tpu as pltpu
from jax.sharding import PartitionSpec as P

f32 = jnp.float32
bf16 = jnp.bfloat16
TILE = 128
BLOCK = 512


def shifted(block, axis, distance):
    size = lax.axis_size(axis)
    route = [((i - distance) % size, i) for i in range(size)]
    return lax.ppermute(block, axis, route)


def split_bf16(x):
    hi = x.astype(bf16)
    return hi, (x - hi.astype(f32)).astype(bf16)


def split_glue(x):
    hi = lax.reduce_precision(x, exponent_bits=8, mantissa_bits=7)
    return hi.astype(bf16), (x - hi).astype(bf16)


KEPT = ((1, 1), (1, 2), (2, 1), (2, 2))
OTHER = ((0, 0), (0, 1), (0, 2), (1, 0), (2, 0))


def round16(x):
    return -(-x // 16) * 16


def layout(modes, lookback, tail=0):
    state_row = 0
    kept_row = 2 * modes
    head_row = kept_row + len(KEPT) * lookback
    small_rows = round16(head_row + len(KEPT) * lookback)
    msg_rows = round16(small_rows + len(OTHER) * lookback + tail)
    return state_row, kept_row, head_row, small_rows, msg_rows


def tail_slot(modes, lookback):
    return layout(modes, lookback)[3] + len(OTHER) * lookback


def rim_slot(operator, branch, modes, lookback):
    _, kept_row, _, small_rows, _ = layout(modes, lookback)
    if (operator, branch) in KEPT:
        return kept_row + KEPT.index((operator, branch)) * lookback
    return small_rows + OTHER.index((operator, branch)) * lookback


def head_slot(operator, branch, modes, lookback):
    return layout(modes, lookback)[2] + KEPT.index((operator, branch)) * lookback


def feature_rows(proj_ref, rim_ref, ft_ref, lanes, operator, branch, index, lookback, modes=0):
    src = proj_ref[index, :, lanes].astype(f32)
    number = operator * 3 + branch
    row = lax.broadcasted_iota(jnp.int32, src.shape, 0)
    result = ft_ref[operator, branch, pl.ds(0, 1), lanes].astype(f32) * src
    for back in range(1, lookback + 1):
        moved = pltpu.roll(src, back, 0)
        for t in range(back if rim_ref is not None else 0):
            rim_row = rim_ref[pl.ds(rim_slot(operator, branch, modes, lookback) + lookback + t - back, 1), lanes]
            moved = jnp.where(row == t, rim_row.astype(f32), moved)
        result = result + ft_ref[operator, branch, pl.ds(back, 1), lanes].astype(f32) * moved
    return result


def toeplitz_kernel(bm_ref, bl_ref, after_ref, tm_ref, tlh_ref, tll_ref):
    per = bm_ref.shape[0]
    rows = tm_ref.shape[1]
    width = bm_ref.shape[1]
    for gl in range(per):
        base = jnp.broadcast_to(bm_ref[pl.ds(gl, 1), :], (rows, width))
        tm_ref[gl] = pltpu.roll(base, 0, 1, stride=1, stride_axis=0).astype(bf16)
        base = jnp.broadcast_to(bl_ref[pl.ds(gl, 1), :], (rows, width))
        full = pltpu.roll(base, 0, 1, stride=1, stride_axis=0)[:, :rows]
        hi, lo = split_bf16(full)
        tlh_ref[gl] = hi
        tll_ref[gl] = lo


def pre_kernel(sp_ref, mp_ref, lp_ref, ft_ref, wsh_ref, wsl_ref, full_ref, msg_ref, msg_scr,
               *, lookback, modes, group_width, tail):
    length = sp_ref.shape[1]
    rows_per = TILE // group_width * modes
    state_row, _, _, small_rows, msg_rows = layout(modes, lookback, tail)
    projs = (sp_ref, mp_ref, lp_ref)
    for sub in range(full_ref.shape[1] // TILE):
        lanes = pl.ds(sub * TILE, TILE)
        msg_scr[...] = jnp.zeros_like(msg_scr)
        for operator in range(3):
            for branch in range(3):
                for r in range(lookback):
                    msg_scr[pl.ds(rim_slot(operator, branch, modes, lookback) + r, 1), :] = projs[operator][
                        branch, pl.ds(length - lookback + r, 1), lanes
                    ].astype(f32)
        for operator in (1, 2):
            for branch in (1, 2):
                for r in range(lookback):
                    at = head_slot(operator, branch, modes, lookback) + r
                    msg_scr[pl.ds(at, 1), :] = projs[operator][branch, pl.ds(r, 1), lanes].astype(f32)
        products = []
        for operator, proj_ref in enumerate(projs):
            k_feat = feature_rows(proj_ref, None, ft_ref, lanes, operator, 1, 1, lookback)
            v_feat = feature_rows(proj_ref, None, ft_ref, lanes, operator, 2, 2, lookback)
            products.append((k_feat * v_feat).astype(bf16))
        zs, zm, zl = products
        full_ref[pl.ds(msg_rows, length), lanes] = zm
        msg_scr[pl.ds(tail_slot(modes, lookback), tail), :] = zs.astype(f32)[length - tail:, :]
        weights = pl.ds(sub * rows_per, rows_per)
        full = jnp.dot(wsh_ref[weights, :], zl, preferred_element_type=f32) + jnp.dot(
            wsl_ref[weights, :], zl, preferred_element_type=f32
        )
        rows = lax.broadcasted_iota(jnp.int32, full.shape, 0) // modes
        lane_group = lax.broadcasted_iota(jnp.int32, full.shape, 1) // group_width
        full = jnp.where(rows == lane_group, full, 0.0)
        state = full[0:modes, :]
        for gl in range(1, rows_per // modes):
            state = state + full[gl * modes:(gl + 1) * modes, :]
        hi, lo = split_bf16(state)
        msg_scr[pl.ds(state_row, modes), :] = hi.astype(f32)
        msg_scr[pl.ds(state_row + modes, modes), :] = lo.astype(f32)
        packed = msg_scr[...].astype(bf16)
        msg_ref[:, lanes] = packed[:small_rows]
        full_ref[pl.ds(0, msg_rows), lanes] = packed


def head_rows(head_ref, before_ref, ft_ref, lanes, operator, lookback, modes):
    feats = []
    for branch in (1, 2):
        head = head_slot(operator, branch, modes, lookback)
        rim = rim_slot(operator, branch, modes, lookback)
        base = (operator * 3 + branch) * (lookback + 1)
        rows = []
        for p in range(lookback):
            total = None
            for j in range(lookback + 1):
                if p >= j:
                    src = head_ref[pl.ds(head + p - j, 1), lanes]
                else:
                    src = before_ref[pl.ds(rim + lookback + p - j, 1), lanes]
                term = ft_ref[operator, branch, pl.ds(j, 1), lanes].astype(f32) * src.astype(f32)
                total = term if total is None else total + term
            rows.append(total)
        feats.append(rows)
    return [(a * b).astype(bf16).astype(f32) for a, b in zip(*feats)]


def mix_kernel(*refs, lookback, modes, group_width, inline, blocks, tail):
    (sp_ref, mp_ref, lp_ref, in_ref, ft_ref, st_ref, tm_ref, tlh_ref, tll_ref,
     ech_ref, ecl_ref) = refs[:11]
    if inline:
        coef_ref, first_ref = refs[11:13]
        by_shift = [refs[13], in_ref] + list(refs[14:12 + blocks])
        rest = refs[12 + blocks:]
    else:
        inc_ref, fix_ref = refs[11:13]
        rest = refs[13:]
    so_ref, mo_ref, lo_ref, y_scr, zext_scr = rest
    state_row, _, _, _, msg_rows = layout(modes, lookback, tail)
    length = so_ref.shape[0]
    per = TILE // group_width
    row = lax.broadcasted_iota(jnp.int32, (length, TILE), 0)
    lane_group = lax.broadcasted_iota(jnp.int32, (length, TILE), 1) // group_width
    first = lax.broadcasted_iota(jnp.int32, (16, TILE), 0)
    for sub in range(so_ref.shape[1] // TILE):
        lanes = pl.ds(sub * TILE, TILE)
        if inline:
            incoming = None
            for k in range(blocks):
                now_ref = by_shift[k]
                head = head_rows(now_ref, by_shift[(k + 1) % blocks], ft_ref, lanes, 2, lookback, modes)
                state = now_ref[pl.ds(state_row, modes), lanes].astype(f32) + now_ref[
                    pl.ds(state_row + modes, modes), lanes
                ].astype(f32)
                for p in range(lookback):
                    state = state + first_ref[p, :, lanes] * head[p]
                term = coef_ref[(k - 1) % blocks, :, lanes] * state
                incoming = term if incoming is None else incoming + term
            fixed = head_rows(by_shift[1 % blocks], by_shift[2 % blocks], ft_ref, lanes, 1,
                              lookback, modes)
            fix = jnp.zeros((16, TILE), f32)
            for p in range(lookback):
                fix = jnp.where(first == p, fixed[p], fix)
        else:
            incoming = inc_ref[:, lanes]
            fix = fix_ref[:, lanes]
        feats = [
            [feature_rows(ref, in_ref, ft_ref, lanes, operator, branch, branch, lookback, modes)
             for branch in range(3)]
            for operator, ref in enumerate((sp_ref, mp_ref, lp_ref))
        ]
        zs, zm, zl = [(f[1] * f[2]).astype(bf16) for f in feats]

        zs = zs.astype(f32)
        y_scr[...] = zs
        y_scr[pl.ds(length - tail, tail), :] = in_ref[
            pl.ds(tail_slot(modes, lookback), tail), lanes
        ].astype(f32)
        wrapped = y_scr[...]
        conv = st_ref[pl.ds(0, 1), lanes] * zs
        for j in range(1, st_ref.shape[0]):
            back = jnp.where(row < j, pltpu.roll(wrapped, j, 0), pltpu.roll(zs, j, 0))
            conv = conv + st_ref[pl.ds(j, 1), lanes] * back
        so_ref[:, lanes] = (feats[0][0] * conv).astype(so_ref.dtype)

        zext_scr[pl.ds(0, length), :] = in_ref[pl.ds(msg_rows, length), lanes]
        zext_scr[pl.ds(0, 16), :] = jnp.where(
            first < lookback, fix, in_ref[pl.ds(msg_rows, 16), lanes].astype(f32)
        ).astype(bf16)
        zext_scr[pl.ds(length, length), :] = zm
        zext = zext_scr[...]
        acc = jnp.zeros((length, TILE), f32)
        for gl in range(per):
            part = jnp.dot(tm_ref[sub * per + gl], zext, preferred_element_type=f32)
            acc = jnp.where(lane_group == gl, part, acc)
        mo_ref[:, lanes] = (feats[1][0] * acc).astype(mo_ref.dtype)

        acc = jnp.zeros((length, TILE), f32)
        for gl in range(per):
            part = jnp.dot(tlh_ref[sub * per + gl], zl, preferred_element_type=f32) + jnp.dot(
                tll_ref[sub * per + gl], zl, preferred_element_type=f32
            )
            acc = jnp.where(lane_group == gl, part, acc)
        stacked = jnp.concatenate([incoming] * per, axis=0)
        srow = lax.broadcasted_iota(jnp.int32, stacked.shape, 0) // modes
        slane = lax.broadcasted_iota(jnp.int32, stacked.shape, 1) // group_width
        stacked = jnp.where(srow == slane, stacked, 0.0)
        ih, il = split_bf16(stacked)
        eh = ech_ref[:, lanes]
        el = ecl_ref[:, lanes]
        carried = (
            jnp.dot(eh, ih, preferred_element_type=f32)
            + jnp.dot(eh, il, preferred_element_type=f32)
            + jnp.dot(el, ih, preferred_element_type=f32)
        )
        lo_ref[:, lanes] = (feats[2][0] * (acc + carried)).astype(lo_ref.dtype)


def head_products(messages, before, ft, operator, lookback, modes):
    feats = []
    for branch in (1, 2):
        head = head_slot(operator, branch, modes, lookback)
        rim = rim_slot(operator, branch, modes, lookback)
        taps = ft[(operator * 3 + branch) * (lookback + 1):(operator * 3 + branch + 1) * (lookback + 1)]
        rows = []
        for p in range(lookback):
            total = None
            for j in range(lookback + 1):
                src = messages[:, head + p - j] if p >= j else before[:, rim + lookback + p - j]
                term = taps[j] * src.astype(f32)
                total = term if total is None else total + term
            rows.append(total)
        feats.append(jnp.stack(rows, axis=1))
    return lax.reduce_precision(feats[0] * feats[1], exponent_bits=8, mantissa_bits=7)


def on_device(short_proj, medium_proj, long_proj, feature_taps, short_taps, medium_taps,
              long_rates, long_residues):
    _, length, channels = short_proj.shape
    groups, modes = long_rates.shape
    group_width = channels // groups
    lookback = feature_taps.shape[2] - 1
    reach = medium_taps.shape[1]
    short_count = short_taps.shape[0]
    assert reach <= length and short_count <= 17 and 0 < lookback <= 4 and modes % 8 == 0
    blocks = lax.axis_size("ctx")
    position = lax.axis_index("ctx")
    inline = blocks <= 8
    width = min(BLOCK, channels)
    steps = channels // width
    gpb = width // group_width
    tail = short_count - 1
    state_row, _, _, small_rows, msg_rows = layout(modes, lookback, tail)
    full_rows = msg_rows + length

    ft = feature_taps.astype(f32).reshape(-1, channels)
    st = jnp.repeat(short_taps.astype(f32), group_width, axis=1)
    rates = long_rates
    loop_length = length * blocks
    wrap_scale = -jnp.expm1(-rates * loop_length)
    gains = long_residues * jnp.sqrt(
        -jnp.expm1(-2.0 * rates) * wrap_scale / (1.0 + jnp.exp(-rates * loop_length))
    )
    offsets = jnp.arange(length, dtype=f32)
    to_end = jnp.exp(-rates[:, :, None] * (length - 1.0 - offsets))
    late = jnp.where(offsets >= lookback, to_end, 0.0).reshape(groups * modes, length)
    wsh, wsl = split_glue(late)

    lane_block = lambda rows: pl.BlockSpec((rows, width), lambda j: (0, j))
    taps_block = pl.BlockSpec((3, 3, lookback + 1, width), lambda j: (0, 0, 0, j))
    proj_block = pl.BlockSpec((3, length, width), lambda j: (0, 0, j))
    full, msg = pl.pallas_call(
        functools.partial(pre_kernel, lookback=lookback, modes=modes, group_width=group_width,
                          tail=tail),
        grid=(steps,),
        in_specs=[
            proj_block,
            proj_block,
            proj_block,
            taps_block,
            pl.BlockSpec((gpb * modes, length), lambda j: (j, 0)),
            pl.BlockSpec((gpb * modes, length), lambda j: (j, 0)),
        ],
        out_specs=[lane_block(full_rows), lane_block(small_rows)],
        out_shape=[
            jax.ShapeDtypeStruct((full_rows, channels), bf16),
            jax.ShapeDtypeStruct((small_rows, channels), bf16),
        ],
        scratch_shapes=[pltpu.VMEM((msg_rows, TILE), f32)],
        cost_estimate=pl.CostEstimate(
            flops=length * channels * (30 + 4 * TILE),
            transcendentals=0,
            bytes_accessed=length * channels * 22,
        ),
    )(short_proj, medium_proj, long_proj, feature_taps, wsh, wsl)

    arrived = shifted(full, "ctx", 1)
    first_w = jnp.repeat(
        jnp.transpose(to_end[:, :, :lookback], (2, 1, 0)), group_width, axis=2
    )
    rate_c = jnp.repeat(rates.T, group_width, axis=1)
    wrap_c = jnp.repeat(wrap_scale.T, group_width, axis=1)
    powers = jnp.arange(blocks, dtype=f32)
    coef = jnp.exp(-rate_c[None] * (length * powers)[:, None, None]) / wrap_c[None]
    if inline:
        others = [shifted(msg, "ctx", k) for k in range(2, blocks)]
        extra = [coef, first_w, msg] + others
        extra_specs = [
            pl.BlockSpec((blocks, modes, width), lambda j: (0, 0, j)),
            pl.BlockSpec((lookback, modes, width), lambda j: (0, 0, j)),
        ] + [lane_block(small_rows)] * (blocks - 1)
    else:
        messages = lax.all_gather(msg, "ctx")[(position - jnp.arange(blocks)) % blocks]
        before = jnp.roll(messages, -1, axis=0)
        head_long = head_products(messages, before, ft, 2, lookback, modes)
        states = (
            messages[:, state_row:state_row + modes].astype(f32)
            + messages[:, state_row + modes:state_row + 2 * modes].astype(f32)
            + jnp.sum(first_w[None] * head_long[:, :, None, :], axis=1)
        )
        incoming = jnp.sum(coef * jnp.roll(states, -1, axis=0), axis=0)
        fix = head_products(messages[1:2], before[1:2], ft, 1, lookback, modes)[0]
        fix = jnp.pad(fix, ((0, 16 - lookback), (0, 0)))
        extra = [incoming, fix]
        extra_specs = [lane_block(modes), lane_block(16)]

    bm = jnp.concatenate(
        [
            jnp.zeros((groups, length - reach + 1), f32),
            medium_taps.astype(f32)[:, ::-1],
            jnp.zeros((groups, length - 1), f32),
        ],
        axis=1,
    )
    profile = jnp.sum(gains[:, :, None] * jnp.exp(-rates[:, :, None] * offsets), axis=1)
    bl = jnp.concatenate(
        [profile[:, :1], jnp.zeros((groups, length), f32), profile[:, :0:-1]], axis=1
    )
    starts = (gains[None] * jnp.exp(-rates[None] * (offsets + 1.0)[:, None, None])).reshape(
        length, groups * modes
    )
    ech, ecl = split_glue(starts)
    tm, tlh, tll = pl.pallas_call(
        toeplitz_kernel,
        grid=(steps,),
        in_specs=[pl.BlockSpec((gpb, 2 * length), lambda j: (j, 0))] * 2
        + [lane_block(small_rows)],
        out_specs=[
            pl.BlockSpec((gpb, length, 2 * length), lambda j: (j, 0, 0)),
            pl.BlockSpec((gpb, length, length), lambda j: (j, 0, 0)),
            pl.BlockSpec((gpb, length, length), lambda j: (j, 0, 0)),
        ],
        out_shape=[
            jax.ShapeDtypeStruct((groups, length, 2 * length), bf16),
            jax.ShapeDtypeStruct((groups, length, length), bf16),
            jax.ShapeDtypeStruct((groups, length, length), bf16),
        ],
        cost_estimate=pl.CostEstimate(
            flops=groups * length * length * 8,
            transcendentals=0,
            bytes_accessed=groups * length * length * 8,
        ),
    )(bm, bl, msg)

    outs = pl.pallas_call(
        functools.partial(mix_kernel, lookback=lookback, modes=modes, group_width=group_width,
                          inline=inline, blocks=blocks, tail=tail),
        grid=(steps,),
        in_specs=[
            proj_block,
            proj_block,
            proj_block,
            lane_block(full_rows),
            taps_block,
            lane_block(short_count),
            pl.BlockSpec((gpb, length, 2 * length), lambda j: (j, 0, 0)),
            pl.BlockSpec((gpb, length, length), lambda j: (j, 0, 0)),
            pl.BlockSpec((gpb, length, length), lambda j: (j, 0, 0)),
            pl.BlockSpec((length, gpb * modes), lambda j: (0, j)),
            pl.BlockSpec((length, gpb * modes), lambda j: (0, j)),
        ] + extra_specs,
        out_specs=[lane_block(length)] * 3,
        out_shape=[jax.ShapeDtypeStruct((length, channels), bf16)] * 3,
        scratch_shapes=[
            pltpu.VMEM((length, TILE), f32),
            pltpu.VMEM((2 * length, TILE), bf16),
        ],
        cost_estimate=pl.CostEstimate(
            flops=groups * length * TILE * length * 10,
            transcendentals=0,
            bytes_accessed=groups * length * length * 8 + length * channels * 24,
        ),
    )(short_proj, medium_proj, long_proj, arrived, feature_taps, st, tm, tlh, tll, ech, ecl, *extra)
    return tuple(outs)


def solution(mesh):
    return jax.shard_map(
        on_device,
        mesh=mesh,
        in_specs=(
            P(None, ("group", "ctx"), "chan"),
            P(None, ("group", "ctx"), "chan"),
            P(None, ("group", "ctx"), "chan"),
            P(None, None, None, "chan"),
            P(None, "chan"),
            P("chan", None),
            P("chan", None),
            P("chan", None),
        ),
        out_specs=(
            P(("group", "ctx"), "chan"),
            P(("group", "ctx"), "chan"),
            P(("group", "ctx"), "chan"),
        ),
        check_vma=False,
    )
```

```python
import functools

import jax
import jax.numpy as jnp
from jax import lax
from jax.experimental import pallas as pl
from jax.experimental.pallas import tpu as pltpu
from jax.sharding import PartitionSpec as P

f32 = jnp.float32
bf16 = jnp.bfloat16
TILE = 128
BLOCK = 512


def shifted(block, axis, distance):
    size = lax.axis_size(axis)
    route = [((i - distance) % size, i) for i in range(size)]
    return lax.ppermute(block, axis, route)


def split_bf16(x):
    hi = x.astype(bf16)
    return hi, (x - hi.astype(f32)).astype(bf16)


def split_glue(x):
    hi = lax.reduce_precision(x, exponent_bits=8, mantissa_bits=7)
    return hi.astype(bf16), (x - hi).astype(bf16)


KEPT = ((1, 1), (1, 2), (2, 1), (2, 2))
OTHER = ((0, 0), (0, 1), (0, 2), (1, 0), (2, 0))


def round16(x):
    return -(-x // 16) * 16


def layout(modes, lookback, tail=0):
    state_row = 0
    kept_row = 2 * modes
    head_row = kept_row + len(KEPT) * lookback
    small_rows = round16(head_row + len(KEPT) * lookback)
    msg_rows = round16(small_rows + len(OTHER) * lookback + tail)
    return state_row, kept_row, head_row, small_rows, msg_rows


def tail_slot(modes, lookback):
    return layout(modes, lookback)[3] + len(OTHER) * lookback


def rim_slot(operator, branch, modes, lookback):
    _, kept_row, _, small_rows, _ = layout(modes, lookback)
    if (operator, branch) in KEPT:
        return kept_row + KEPT.index((operator, branch)) * lookback
    return small_rows + OTHER.index((operator, branch)) * lookback


def head_slot(operator, branch, modes, lookback):
    return layout(modes, lookback)[2] + KEPT.index((operator, branch)) * lookback


def feature_rows(proj_ref, rim_ref, ft_ref, lanes, operator, branch, index, lookback, modes=0):
    src = proj_ref[index, :, lanes].astype(f32)
    number = operator * 3 + branch
    row = lax.broadcasted_iota(jnp.int32, src.shape, 0)
    result = ft_ref[operator, branch, pl.ds(0, 1), lanes].astype(f32) * src
    for back in range(1, lookback + 1):
        moved = pltpu.roll(src, back, 0)
        for t in range(back if rim_ref is not None else 0):
            rim_row = rim_ref[pl.ds(rim_slot(operator, branch, modes, lookback) + lookback + t - back, 1), lanes]
            moved = jnp.where(row == t, rim_row.astype(f32), moved)
        result = result + ft_ref[operator, branch, pl.ds(back, 1), lanes].astype(f32) * moved
    return result


def toeplitz_kernel(bm_ref, bl_ref, after_ref, tm_ref, tlh_ref, tll_ref):
    per = bm_ref.shape[0]
    rows = tm_ref.shape[1]
    width = bm_ref.shape[1]
    for gl in range(per):
        base = jnp.broadcast_to(bm_ref[pl.ds(gl, 1), :], (rows, width))
        tm_ref[gl] = pltpu.roll(base, 0, 1, stride=1, stride_axis=0).astype(bf16)
        base = jnp.broadcast_to(bl_ref[pl.ds(gl, 1), :], (rows, width))
        full = pltpu.roll(base, 0, 1, stride=1, stride_axis=0)[:, :rows]
        hi, lo = split_bf16(full)
        tlh_ref[gl] = hi
        tll_ref[gl] = lo


def pre_kernel(sp_ref, mp_ref, lp_ref, ft_ref, wsh_ref, wsl_ref, full_ref, msg_ref, msg_scr,
               *, lookback, modes, group_width, tail):
    length = sp_ref.shape[1]
    rows_per = TILE // group_width * modes
    state_row, _, _, small_rows, msg_rows = layout(modes, lookback, tail)
    projs = (sp_ref, mp_ref, lp_ref)
    for sub in range(full_ref.shape[1] // TILE):
        lanes = pl.ds(sub * TILE, TILE)
        msg_scr[...] = jnp.zeros_like(msg_scr)
        for operator in range(3):
            for branch in range(3):
                for r in range(lookback):
                    msg_scr[pl.ds(rim_slot(operator, branch, modes, lookback) + r, 1), :] = projs[operator][
                        branch, pl.ds(length - lookback + r, 1), lanes
                    ].astype(f32)
        for operator in (1, 2):
            for branch in (1, 2):
                for r in range(lookback):
                    at = head_slot(operator, branch, modes, lookback) + r
                    msg_scr[pl.ds(at, 1), :] = projs[operator][branch, pl.ds(r, 1), lanes].astype(f32)
        products = []
        for operator, proj_ref in enumerate(projs):
            k_feat = feature_rows(proj_ref, None, ft_ref, lanes, operator, 1, 1, lookback)
            v_feat = feature_rows(proj_ref, None, ft_ref, lanes, operator, 2, 2, lookback)
            products.append((k_feat * v_feat).astype(bf16))
        zs, zm, zl = products
        full_ref[pl.ds(msg_rows, length), lanes] = zm
        msg_scr[pl.ds(tail_slot(modes, lookback), tail), :] = zs.astype(f32)[length - tail:, :]
        weights = pl.ds(sub * rows_per, rows_per)
        full = jnp.dot(wsh_ref[weights, :], zl, preferred_element_type=f32) + jnp.dot(
            wsl_ref[weights, :], zl, preferred_element_type=f32
        )
        rows = lax.broadcasted_iota(jnp.int32, full.shape, 0) // modes
        lane_group = lax.broadcasted_iota(jnp.int32, full.shape, 1) // group_width
        full = jnp.where(rows == lane_group, full, 0.0)
        state = full[0:modes, :]
        for gl in range(1, rows_per // modes):
            state = state + full[gl * modes:(gl + 1) * modes, :]
        hi, lo = split_bf16(state)
        msg_scr[pl.ds(state_row, modes), :] = hi.astype(f32)
        msg_scr[pl.ds(state_row + modes, modes), :] = lo.astype(f32)
        packed = msg_scr[...].astype(bf16)
        msg_ref[:, lanes] = packed[:small_rows]
        full_ref[pl.ds(0, msg_rows), lanes] = packed


def head_rows(head_ref, before_ref, ft_ref, lanes, operator, lookback, modes):
    feats = []
    for branch in (1, 2):
        head = head_slot(operator, branch, modes, lookback)
        rim = rim_slot(operator, branch, modes, lookback)
        base = (operator * 3 + branch) * (lookback + 1)
        rows = []
        for p in range(lookback):
            total = None
            for j in range(lookback + 1):
                if p >= j:
                    src = head_ref[pl.ds(head + p - j, 1), lanes]
                else:
                    src = before_ref[pl.ds(rim + lookback + p - j, 1), lanes]
                term = ft_ref[operator, branch, pl.ds(j, 1), lanes].astype(f32) * src.astype(f32)
                total = term if total is None else total + term
            rows.append(total)
        feats.append(rows)
    return [(a * b).astype(bf16).astype(f32) for a, b in zip(*feats)]


def mix_kernel(*refs, lookback, modes, group_width, inline, blocks, tail):
    (sp_ref, mp_ref, lp_ref, in_ref, ft_ref, st_ref, tm_ref, tlh_ref, tll_ref,
     ech_ref, ecl_ref) = refs[:11]
    if inline:
        coef_ref, first_ref = refs[11:13]
        by_shift = [refs[13], in_ref] + list(refs[14:12 + blocks])
        rest = refs[12 + blocks:]
    else:
        inc_ref, fix_ref = refs[11:13]
        rest = refs[13:]
    so_ref, mo_ref, lo_ref, y_scr, zext_scr = rest
    state_row, _, _, _, msg_rows = layout(modes, lookback, tail)
    length = so_ref.shape[0]
    per = TILE // group_width
    row = lax.broadcasted_iota(jnp.int32, (length, TILE), 0)
    lane_group = lax.broadcasted_iota(jnp.int32, (length, TILE), 1) // group_width
    first = lax.broadcasted_iota(jnp.int32, (16, TILE), 0)
    for sub in range(so_ref.shape[1] // TILE):
        lanes = pl.ds(sub * TILE, TILE)
        if inline:
            incoming = None
            for k in range(blocks):
                now_ref = by_shift[k]
                head = head_rows(now_ref, by_shift[(k + 1) % blocks], ft_ref, lanes, 2, lookback, modes)
                state = now_ref[pl.ds(state_row, modes), lanes].astype(f32) + now_ref[
                    pl.ds(state_row + modes, modes), lanes
                ].astype(f32)
                for p in range(lookback):
                    state = state + first_ref[p, :, lanes] * head[p]
                term = coef_ref[(k - 1) % blocks, :, lanes] * state
                incoming = term if incoming is None else incoming + term
            fixed = head_rows(by_shift[1 % blocks], by_shift[2 % blocks], ft_ref, lanes, 1,
                              lookback, modes)
            fix = jnp.zeros((16, TILE), f32)
            for p in range(lookback):
                fix = jnp.where(first == p, fixed[p], fix)
        else:
            incoming = inc_ref[:, lanes]
            fix = fix_ref[:, lanes]
        feats = [
            [feature_rows(ref, in_ref, ft_ref, lanes, operator, branch, branch, lookback, modes)
             for branch in range(3)]
            for operator, ref in enumerate((sp_ref, mp_ref, lp_ref))
        ]
        zs, zm, zl = [(f[1] * f[2]).astype(bf16) for f in feats]

        zs = zs.astype(f32)
        y_scr[...] = zs
        y_scr[pl.ds(length - tail, tail), :] = in_ref[
            pl.ds(tail_slot(modes, lookback), tail), lanes
        ].astype(f32)
        wrapped = y_scr[...]
        conv = st_ref[pl.ds(0, 1), lanes] * zs
        for j in range(1, st_ref.shape[0]):
            back = jnp.where(row < j, pltpu.roll(wrapped, j, 0), pltpu.roll(zs, j, 0))
            conv = conv + st_ref[pl.ds(j, 1), lanes] * back
        so_ref[:, lanes] = (feats[0][0] * conv).astype(so_ref.dtype)

        zext_scr[pl.ds(0, length), :] = in_ref[pl.ds(msg_rows, length), lanes]
        zext_scr[pl.ds(0, 16), :] = jnp.where(
            first < lookback, fix, in_ref[pl.ds(msg_rows, 16), lanes].astype(f32)
        ).astype(bf16)
        zext_scr[pl.ds(length, length), :] = zm
        zext = zext_scr[...]
        acc = jnp.zeros((length, TILE), f32)
        for gl in range(per):
            part = jnp.dot(tm_ref[sub * per + gl], zext, preferred_element_type=f32)
            acc = jnp.where(lane_group == gl, part, acc)
        mo_ref[:, lanes] = (feats[1][0] * acc).astype(mo_ref.dtype)

        acc = jnp.zeros((length, TILE), f32)
        for gl in range(per):
            part = jnp.dot(tlh_ref[sub * per + gl], zl, preferred_element_type=f32) + jnp.dot(
                tll_ref[sub * per + gl], zl, preferred_element_type=f32
            )
            acc = jnp.where(lane_group == gl, part, acc)
        stacked = jnp.concatenate([incoming] * per, axis=0)
        srow = lax.broadcasted_iota(jnp.int32, stacked.shape, 0) // modes
        slane = lax.broadcasted_iota(jnp.int32, stacked.shape, 1) // group_width
        stacked = jnp.where(srow == slane, stacked, 0.0)
        ih, il = split_bf16(stacked)
        eh = ech_ref[:, lanes]
        el = ecl_ref[:, lanes]
        carried = (
            jnp.dot(eh, ih, preferred_element_type=f32)
            + jnp.dot(eh, il, preferred_element_type=f32)
            + jnp.dot(el, ih, preferred_element_type=f32)
        )
        lo_ref[:, lanes] = (feats[2][0] * (acc + carried)).astype(lo_ref.dtype)


def head_products(messages, before, ft, operator, lookback, modes):
    feats = []
    for branch in (1, 2):
        head = head_slot(operator, branch, modes, lookback)
        rim = rim_slot(operator, branch, modes, lookback)
        taps = ft[(operator * 3 + branch) * (lookback + 1):(operator * 3 + branch + 1) * (lookback + 1)]
        rows = []
        for p in range(lookback):
            total = None
            for j in range(lookback + 1):
                src = messages[:, head + p - j] if p >= j else before[:, rim + lookback + p - j]
                term = taps[j] * src.astype(f32)
                total = term if total is None else total + term
            rows.append(total)
        feats.append(jnp.stack(rows, axis=1))
    return lax.reduce_precision(feats[0] * feats[1], exponent_bits=8, mantissa_bits=7)


def on_device(short_proj, medium_proj, long_proj, feature_taps, short_taps, medium_taps,
              long_rates, long_residues):
    _, length, channels = short_proj.shape
    groups, modes = long_rates.shape
    group_width = channels // groups
    lookback = feature_taps.shape[2] - 1
    reach = medium_taps.shape[1]
    short_count = short_taps.shape[0]
    assert reach <= length and short_count <= 17 and 0 < lookback <= 4 and modes % 8 == 0
    blocks = lax.axis_size("ctx")
    position = lax.axis_index("ctx")
    inline = blocks <= 8
    width = min(BLOCK, channels)
    steps = channels // width
    gpb = width // group_width
    tail = short_count - 1
    state_row, _, _, small_rows, msg_rows = layout(modes, lookback, tail)
    full_rows = msg_rows + length

    ft = feature_taps.astype(f32).reshape(-1, channels)
    st = jnp.repeat(short_taps.astype(f32), group_width, axis=1)
    rates = long_rates
    loop_length = length * blocks
    wrap_scale = -jnp.expm1(-rates * loop_length)
    gains = long_residues * jnp.sqrt(
        -jnp.expm1(-2.0 * rates) * wrap_scale / (1.0 + jnp.exp(-rates * loop_length))
    )
    offsets = jnp.arange(length, dtype=f32)
    to_end = jnp.exp(-rates[:, :, None] * (length - 1.0 - offsets))
    late = jnp.where(offsets >= lookback, to_end, 0.0).reshape(groups * modes, length)
    wsh, wsl = split_glue(late)

    lane_block = lambda rows: pl.BlockSpec((rows, width), lambda j: (0, j))
    taps_block = pl.BlockSpec((3, 3, lookback + 1, width), lambda j: (0, 0, 0, j))
    proj_block = pl.BlockSpec((3, length, width), lambda j: (0, 0, j))
    full, msg = pl.pallas_call(
        functools.partial(pre_kernel, lookback=lookback, modes=modes, group_width=group_width,
                          tail=tail),
        grid=(steps,),
        in_specs=[
            proj_block,
            proj_block,
            proj_block,
            taps_block,
            pl.BlockSpec((gpb * modes, length), lambda j: (j, 0)),
            pl.BlockSpec((gpb * modes, length), lambda j: (j, 0)),
        ],
        out_specs=[lane_block(full_rows), lane_block(small_rows)],
        out_shape=[
            jax.ShapeDtypeStruct((full_rows, channels), bf16),
            jax.ShapeDtypeStruct((small_rows, channels), bf16),
        ],
        scratch_shapes=[pltpu.VMEM((msg_rows, TILE), f32)],
        cost_estimate=pl.CostEstimate(
            flops=length * channels * (30 + 4 * TILE),
            transcendentals=0,
            bytes_accessed=length * channels * 22,
        ),
    )(short_proj, medium_proj, long_proj, feature_taps, wsh, wsl)

    arrived = shifted(full, "ctx", 1)
    first_w = jnp.repeat(
        jnp.transpose(to_end[:, :, :lookback], (2, 1, 0)), group_width, axis=2
    )
    rate_c = jnp.repeat(rates.T, group_width, axis=1)
    wrap_c = jnp.repeat(wrap_scale.T, group_width, axis=1)
    powers = jnp.arange(blocks, dtype=f32)
    coef = jnp.exp(-rate_c[None] * (length * powers)[:, None, None]) / wrap_c[None]
    if inline:
        others = [shifted(msg, "ctx", k) for k in range(2, blocks)]
        extra = [coef, first_w, msg] + others
        extra_specs = [
            pl.BlockSpec((blocks, modes, width), lambda j: (0, 0, j)),
            pl.BlockSpec((lookback, modes, width), lambda j: (0, 0, j)),
        ] + [lane_block(small_rows)] * (blocks - 1)
    else:
        messages = lax.all_gather(msg, "ctx")[(position - jnp.arange(blocks)) % blocks]
        before = jnp.roll(messages, -1, axis=0)
        head_long = head_products(messages, before, ft, 2, lookback, modes)
        states = (
            messages[:, state_row:state_row + modes].astype(f32)
            + messages[:, state_row + modes:state_row + 2 * modes].astype(f32)
            + jnp.sum(first_w[None] * head_long[:, :, None, :], axis=1)
        )
        incoming = jnp.sum(coef * jnp.roll(states, -1, axis=0), axis=0)
        fix = head_products(messages[1:2], before[1:2], ft, 1, lookback, modes)[0]
        fix = jnp.pad(fix, ((0, 16 - lookback), (0, 0)))
        extra = [incoming, fix]
        extra_specs = [lane_block(modes), lane_block(16)]

    bm = jnp.concatenate(
        [
            jnp.zeros((groups, length - reach + 1), f32),
            medium_taps.astype(f32)[:, ::-1],
            jnp.zeros((groups, length - 1), f32),
        ],
        axis=1,
    )
    profile = jnp.sum(gains[:, :, None] * jnp.exp(-rates[:, :, None] * offsets), axis=1)
    bl = jnp.concatenate(
        [profile[:, :1], jnp.zeros((groups, length), f32), profile[:, :0:-1]], axis=1
    )
    starts = (gains[None] * jnp.exp(-rates[None] * (offsets + 1.0)[:, None, None])).reshape(
        length, groups * modes
    )
    ech, ecl = split_glue(starts)
    tm, tlh, tll = pl.pallas_call(
        toeplitz_kernel,
        grid=(steps,),
        in_specs=[pl.BlockSpec((gpb, 2 * length), lambda j: (j, 0))] * 2
        + [lane_block(small_rows)],
        out_specs=[
            pl.BlockSpec((gpb, length, 2 * length), lambda j: (j, 0, 0)),
            pl.BlockSpec((gpb, length, length), lambda j: (j, 0, 0)),
            pl.BlockSpec((gpb, length, length), lambda j: (j, 0, 0)),
        ],
        out_shape=[
            jax.ShapeDtypeStruct((groups, length, 2 * length), bf16),
            jax.ShapeDtypeStruct((groups, length, length), bf16),
            jax.ShapeDtypeStruct((groups, length, length), bf16),
        ],
        cost_estimate=pl.CostEstimate(
            flops=groups * length * length * 8,
            transcendentals=0,
            bytes_accessed=groups * length * length * 8,
        ),
    )(bm, bl, msg)

    mwidth = min(BLOCK // 2, channels)
    mgpb = mwidth // group_width
    m_lane = lambda rows: pl.BlockSpec((rows, mwidth), lambda j: (0, j))
    m_proj = pl.BlockSpec((3, length, mwidth), lambda j: (0, 0, j))
    m_taps = pl.BlockSpec((3, 3, lookback + 1, mwidth), lambda j: (0, 0, 0, j))
    if inline:
        m_extra = [
            pl.BlockSpec((blocks, modes, mwidth), lambda j: (0, 0, j)),
            pl.BlockSpec((lookback, modes, mwidth), lambda j: (0, 0, j)),
        ] + [m_lane(small_rows)] * (blocks - 1)
    else:
        m_extra = [m_lane(modes), m_lane(16)]
    outs = pl.pallas_call(
        functools.partial(mix_kernel, lookback=lookback, modes=modes, group_width=group_width,
                          inline=inline, blocks=blocks, tail=tail),
        grid=(channels // mwidth,),
        in_specs=[
            m_proj,
            m_proj,
            m_proj,
            m_lane(full_rows),
            m_taps,
            m_lane(short_count),
            pl.BlockSpec((mgpb, length, 2 * length), lambda j: (j, 0, 0)),
            pl.BlockSpec((mgpb, length, length), lambda j: (j, 0, 0)),
            pl.BlockSpec((mgpb, length, length), lambda j: (j, 0, 0)),
            pl.BlockSpec((length, mgpb * modes), lambda j: (0, j)),
            pl.BlockSpec((length, mgpb * modes), lambda j: (0, j)),
        ] + m_extra,
        out_specs=[m_lane(length)] * 3,
        out_shape=[jax.ShapeDtypeStruct((length, channels), bf16)] * 3,
        scratch_shapes=[
            pltpu.VMEM((length, TILE), f32),
            pltpu.VMEM((2 * length, TILE), bf16),
        ],
        cost_estimate=pl.CostEstimate(
            flops=groups * length * TILE * length * 10,
            transcendentals=0,
            bytes_accessed=groups * length * length * 8 + length * channels * 24,
        ),
    )(short_proj, medium_proj, long_proj, arrived, feature_taps, st, tm, tlh, tll, ech, ecl, *extra)
    return tuple(outs)


def solution(mesh):
    return jax.shard_map(
        on_device,
        mesh=mesh,
        in_specs=(
            P(None, ("group", "ctx"), "chan"),
            P(None, ("group", "ctx"), "chan"),
            P(None, ("group", "ctx"), "chan"),
            P(None, None, None, "chan"),
            P(None, "chan"),
            P("chan", None),
            P("chan", None),
            P("chan", None),
        ),
        out_specs=(
            P(("group", "ctx"), "chan"),
            P(("group", "ctx"), "chan"),
            P(("group", "ctx"), "chan"),
        ),
        check_vma=False,
    )
```

```python
import functools

import jax
import jax.numpy as jnp
from jax import lax
from jax.experimental import pallas as pl
from jax.experimental.pallas import tpu as pltpu
from jax.sharding import PartitionSpec as P

f32 = jnp.float32
bf16 = jnp.bfloat16
TILE = 128
BLOCK = 512


def shifted(block, axis, distance):
    size = lax.axis_size(axis)
    route = [((i - distance) % size, i) for i in range(size)]
    return lax.ppermute(block, axis, route)


def split_bf16(x):
    hi = x.astype(bf16)
    return hi, (x - hi.astype(f32)).astype(bf16)


def split_glue(x):
    hi = lax.reduce_precision(x, exponent_bits=8, mantissa_bits=7)
    return hi.astype(bf16), (x - hi).astype(bf16)


KEPT = ((1, 1), (1, 2), (2, 1), (2, 2))
HEADS = ((2, 1), (2, 2), (1, 1), (1, 2))
OTHER = ((0, 0), (0, 1), (0, 2), (1, 0), (2, 0))


def round16(x):
    return -(-x // 16) * 16


def layout(modes, lookback, tail=0):
    state_row = 0
    kept_row = 2 * modes
    head_row = kept_row + len(KEPT) * lookback
    small_rows = head_row + 2 * lookback
    msg_rows = round16(other_row(modes, lookback) + len(OTHER) * lookback + tail)
    return state_row, kept_row, head_row, small_rows, msg_rows


def other_row(modes, lookback):
    return 2 * modes + len(KEPT) * lookback + len(HEADS) * lookback


def tail_slot(modes, lookback):
    return other_row(modes, lookback) + len(OTHER) * lookback


def rim_slot(operator, branch, modes, lookback):
    kept_row = layout(modes, lookback)[1]
    if (operator, branch) in KEPT:
        return kept_row + KEPT.index((operator, branch)) * lookback
    return other_row(modes, lookback) + OTHER.index((operator, branch)) * lookback


def head_slot(operator, branch, modes, lookback):
    return layout(modes, lookback)[2] + HEADS.index((operator, branch)) * lookback


def feature_rows(proj_ref, rim_ref, ft_ref, lanes, operator, branch, index, lookback, modes=0):
    src = proj_ref[index, :, lanes].astype(f32)
    number = operator * 3 + branch
    row = lax.broadcasted_iota(jnp.int32, src.shape, 0)
    result = ft_ref[operator, branch, pl.ds(0, 1), lanes].astype(f32) * src
    for back in range(1, lookback + 1):
        moved = pltpu.roll(src, back, 0)
        for t in range(back if rim_ref is not None else 0):
            rim_row = rim_ref[pl.ds(rim_slot(operator, branch, modes, lookback) + lookback + t - back, 1), lanes]
            moved = jnp.where(row == t, rim_row.astype(f32), moved)
        result = result + ft_ref[operator, branch, pl.ds(back, 1), lanes].astype(f32) * moved
    return result


def toeplitz_kernel(bm_ref, bl_ref, after_ref, tm_ref, tlh_ref, tll_ref):
    per = bm_ref.shape[0]
    rows = tm_ref.shape[1]
    width = bm_ref.shape[1]
    for gl in range(per):
        base = jnp.broadcast_to(bm_ref[pl.ds(gl, 1), :], (rows, width))
        tm_ref[gl] = pltpu.roll(base, 0, 1, stride=1, stride_axis=0).astype(bf16)
        base = jnp.broadcast_to(bl_ref[pl.ds(gl, 1), :], (rows, width))
        full = pltpu.roll(base, 0, 1, stride=1, stride_axis=0)[:, :rows]
        hi, lo = split_bf16(full)
        tlh_ref[gl] = hi
        tll_ref[gl] = lo


def pre_kernel(sp_ref, mp_ref, lp_ref, ft_ref, wsh_ref, wsl_ref, full_ref, msg_ref, msg_scr,
               *, lookback, modes, group_width, tail):
    length = sp_ref.shape[1]
    rows_per = TILE // group_width * modes
    state_row, _, _, small_rows, msg_rows = layout(modes, lookback, tail)
    projs = (sp_ref, mp_ref, lp_ref)
    for sub in range(full_ref.shape[1] // TILE):
        lanes = pl.ds(sub * TILE, TILE)
        msg_scr[...] = jnp.zeros_like(msg_scr)
        for operator in range(3):
            for branch in range(3):
                for r in range(lookback):
                    msg_scr[pl.ds(rim_slot(operator, branch, modes, lookback) + r, 1), :] = projs[operator][
                        branch, pl.ds(length - lookback + r, 1), lanes
                    ].astype(f32)
        for operator in (1, 2):
            for branch in (1, 2):
                for r in range(lookback):
                    at = head_slot(operator, branch, modes, lookback) + r
                    msg_scr[pl.ds(at, 1), :] = projs[operator][branch, pl.ds(r, 1), lanes].astype(f32)
        products = []
        for operator, proj_ref in enumerate(projs):
            k_feat = feature_rows(proj_ref, None, ft_ref, lanes, operator, 1, 1, lookback)
            v_feat = feature_rows(proj_ref, None, ft_ref, lanes, operator, 2, 2, lookback)
            products.append((k_feat * v_feat).astype(bf16))
        zs, zm, zl = products
        full_ref[pl.ds(msg_rows, length), lanes] = zm
        msg_scr[pl.ds(tail_slot(modes, lookback), tail), :] = zs.astype(f32)[length - tail:, :]
        weights = pl.ds(sub * rows_per, rows_per)
        full = jnp.dot(wsh_ref[weights, :], zl, preferred_element_type=f32) + jnp.dot(
            wsl_ref[weights, :], zl, preferred_element_type=f32
        )
        rows = lax.broadcasted_iota(jnp.int32, full.shape, 0) // modes
        lane_group = lax.broadcasted_iota(jnp.int32, full.shape, 1) // group_width
        full = jnp.where(rows == lane_group, full, 0.0)
        state = full[0:modes, :]
        for gl in range(1, rows_per // modes):
            state = state + full[gl * modes:(gl + 1) * modes, :]
        hi, lo = split_bf16(state)
        msg_scr[pl.ds(state_row, modes), :] = hi.astype(f32)
        msg_scr[pl.ds(state_row + modes, modes), :] = lo.astype(f32)
        packed = msg_scr[...].astype(bf16)
        msg_ref[:, lanes] = msg_scr[pl.ds(0, small_rows), :].astype(bf16)
        full_ref[pl.ds(0, msg_rows), lanes] = packed


def head_rows(head_ref, before_ref, ft_ref, lanes, operator, lookback, modes):
    feats = []
    for branch in (1, 2):
        head = head_slot(operator, branch, modes, lookback)
        rim = rim_slot(operator, branch, modes, lookback)
        base = (operator * 3 + branch) * (lookback + 1)
        rows = []
        for p in range(lookback):
            total = None
            for j in range(lookback + 1):
                if p >= j:
                    src = head_ref[pl.ds(head + p - j, 1), lanes]
                else:
                    src = before_ref[pl.ds(rim + lookback + p - j, 1), lanes]
                term = ft_ref[operator, branch, pl.ds(j, 1), lanes].astype(f32) * src.astype(f32)
                total = term if total is None else total + term
            rows.append(total)
        feats.append(rows)
    return [(a * b).astype(bf16).astype(f32) for a, b in zip(*feats)]


def mix_kernel(*refs, lookback, modes, group_width, inline, blocks, tail):
    (sp_ref, mp_ref, lp_ref, in_ref, ft_ref, st_ref, tm_ref, tlh_ref, tll_ref,
     ech_ref, ecl_ref) = refs[:11]
    if inline:
        coef_ref, first_ref = refs[11:13]
        by_shift = [refs[13], in_ref] + list(refs[14:12 + blocks])
        rest = refs[12 + blocks:]
    else:
        inc_ref, fix_ref = refs[11:13]
        rest = refs[13:]
    so_ref, mo_ref, lo_ref, y_scr, zext_scr = rest
    state_row, _, _, _, msg_rows = layout(modes, lookback, tail)
    length = so_ref.shape[0]
    per = TILE // group_width
    row = lax.broadcasted_iota(jnp.int32, (length, TILE), 0)
    lane_group = lax.broadcasted_iota(jnp.int32, (length, TILE), 1) // group_width
    first = lax.broadcasted_iota(jnp.int32, (16, TILE), 0)
    for sub in range(so_ref.shape[1] // TILE):
        lanes = pl.ds(sub * TILE, TILE)
        if inline:
            incoming = None
            for k in range(blocks):
                now_ref = by_shift[k]
                head = head_rows(now_ref, by_shift[(k + 1) % blocks], ft_ref, lanes, 2, lookback, modes)
                state = now_ref[pl.ds(state_row, modes), lanes].astype(f32) + now_ref[
                    pl.ds(state_row + modes, modes), lanes
                ].astype(f32)
                for p in range(lookback):
                    state = state + first_ref[p, :, lanes] * head[p]
                term = coef_ref[(k - 1) % blocks, :, lanes] * state
                incoming = term if incoming is None else incoming + term
            fixed = head_rows(by_shift[1 % blocks], by_shift[2 % blocks], ft_ref, lanes, 1,
                              lookback, modes)
            fix = jnp.zeros((16, TILE), f32)
            for p in range(lookback):
                fix = jnp.where(first == p, fixed[p], fix)
        else:
            incoming = inc_ref[:, lanes]
            fix = fix_ref[:, lanes]
        feats = [
            [feature_rows(ref, in_ref, ft_ref, lanes, operator, branch, branch, lookback, modes)
             for branch in range(3)]
            for operator, ref in enumerate((sp_ref, mp_ref, lp_ref))
        ]
        zs, zm, zl = [(f[1] * f[2]).astype(bf16) for f in feats]

        zs = zs.astype(f32)
        y_scr[...] = zs
        y_scr[pl.ds(length - tail, tail), :] = in_ref[
            pl.ds(tail_slot(modes, lookback), tail), lanes
        ].astype(f32)
        wrapped = y_scr[...]
        conv = st_ref[pl.ds(0, 1), lanes] * zs
        for j in range(1, st_ref.shape[0]):
            back = jnp.where(row < j, pltpu.roll(wrapped, j, 0), pltpu.roll(zs, j, 0))
            conv = conv + st_ref[pl.ds(j, 1), lanes] * back
        so_ref[:, lanes] = (feats[0][0] * conv).astype(so_ref.dtype)

        zext_scr[pl.ds(0, length), :] = in_ref[pl.ds(msg_rows, length), lanes]
        zext_scr[pl.ds(0, 16), :] = jnp.where(
            first < lookback, fix, in_ref[pl.ds(msg_rows, 16), lanes].astype(f32)
        ).astype(bf16)
        zext_scr[pl.ds(length, length), :] = zm
        zext = zext_scr[...]
        acc = jnp.zeros((length, TILE), f32)
        for gl in range(per):
            part = jnp.dot(tm_ref[sub * per + gl], zext, preferred_element_type=f32)
            acc = jnp.where(lane_group == gl, part, acc)
        mo_ref[:, lanes] = (feats[1][0] * acc).astype(mo_ref.dtype)

        acc = jnp.zeros((length, TILE), f32)
        for gl in range(per):
            part = jnp.dot(tlh_ref[sub * per + gl], zl, preferred_element_type=f32) + jnp.dot(
                tll_ref[sub * per + gl], zl, preferred_element_type=f32
            )
            acc = jnp.where(lane_group == gl, part, acc)
        stacked = jnp.concatenate([incoming] * per, axis=0)
        srow = lax.broadcasted_iota(jnp.int32, stacked.shape, 0) // modes
        slane = lax.broadcasted_iota(jnp.int32, stacked.shape, 1) // group_width
        stacked = jnp.where(srow == slane, stacked, 0.0)
        ih, il = split_bf16(stacked)
        eh = ech_ref[:, lanes]
        el = ecl_ref[:, lanes]
        carried = (
            jnp.dot(eh, ih, preferred_element_type=f32)
            + jnp.dot(eh, il, preferred_element_type=f32)
            + jnp.dot(el, ih, preferred_element_type=f32)
        )
        lo_ref[:, lanes] = (feats[2][0] * (acc + carried)).astype(lo_ref.dtype)


def head_products(messages, before, ft, operator, lookback, modes):
    feats = []
    for branch in (1, 2):
        head = head_slot(operator, branch, modes, lookback)
        rim = rim_slot(operator, branch, modes, lookback)
        taps = ft[(operator * 3 + branch) * (lookback + 1):(operator * 3 + branch + 1) * (lookback + 1)]
        rows = []
        for p in range(lookback):
            total = None
            for j in range(lookback + 1):
                src = messages[:, head + p - j] if p >= j else before[:, rim + lookback + p - j]
                term = taps[j] * src.astype(f32)
                total = term if total is None else total + term
            rows.append(total)
        feats.append(jnp.stack(rows, axis=1))
    return lax.reduce_precision(feats[0] * feats[1], exponent_bits=8, mantissa_bits=7)


def on_device(short_proj, medium_proj, long_proj, feature_taps, short_taps, medium_taps,
              long_rates, long_residues):
    _, length, channels = short_proj.shape
    groups, modes = long_rates.shape
    group_width = channels // groups
    lookback = feature_taps.shape[2] - 1
    reach = medium_taps.shape[1]
    short_count = short_taps.shape[0]
    assert reach <= length and short_count <= 17 and 0 < lookback <= 4 and modes % 8 == 0
    blocks = lax.axis_size("ctx")
    position = lax.axis_index("ctx")
    inline = blocks <= 8
    width = min(BLOCK, channels)
    steps = channels // width
    gpb = width // group_width
    tail = short_count - 1
    state_row, _, _, small_rows, msg_rows = layout(modes, lookback, tail)
    full_rows = msg_rows + length

    ft = feature_taps.astype(f32).reshape(-1, channels)
    st = jnp.repeat(short_taps.astype(f32), group_width, axis=1)
    rates = long_rates
    loop_length = length * blocks
    wrap_scale = -jnp.expm1(-rates * loop_length)
    gains = long_residues * jnp.sqrt(
        -jnp.expm1(-2.0 * rates) * wrap_scale / (1.0 + jnp.exp(-rates * loop_length))
    )
    offsets = jnp.arange(length, dtype=f32)
    to_end = jnp.exp(-rates[:, :, None] * (length - 1.0 - offsets))
    late = jnp.where(offsets >= lookback, to_end, 0.0).reshape(groups * modes, length)
    wsh, wsl = split_glue(late)

    lane_block = lambda rows: pl.BlockSpec((rows, width), lambda j: (0, j))
    taps_block = pl.BlockSpec((3, 3, lookback + 1, width), lambda j: (0, 0, 0, j))
    proj_block = pl.BlockSpec((3, length, width), lambda j: (0, 0, j))
    full, msg = pl.pallas_call(
        functools.partial(pre_kernel, lookback=lookback, modes=modes, group_width=group_width,
                          tail=tail),
        grid=(steps,),
        in_specs=[
            proj_block,
            proj_block,
            proj_block,
            taps_block,
            pl.BlockSpec((gpb * modes, length), lambda j: (j, 0)),
            pl.BlockSpec((gpb * modes, length), lambda j: (j, 0)),
        ],
        out_specs=[lane_block(full_rows), lane_block(small_rows)],
        out_shape=[
            jax.ShapeDtypeStruct((full_rows, channels), bf16),
            jax.ShapeDtypeStruct((small_rows, channels), bf16),
        ],
        scratch_shapes=[pltpu.VMEM((msg_rows, TILE), f32)],
        cost_estimate=pl.CostEstimate(
            flops=length * channels * (30 + 4 * TILE),
            transcendentals=0,
            bytes_accessed=length * channels * 22,
        ),
    )(short_proj, medium_proj, long_proj, feature_taps, wsh, wsl)

    arrived = shifted(full, "ctx", 1)
    first_w = jnp.repeat(
        jnp.transpose(to_end[:, :, :lookback], (2, 1, 0)), group_width, axis=2
    )
    rate_c = jnp.repeat(rates.T, group_width, axis=1)
    wrap_c = jnp.repeat(wrap_scale.T, group_width, axis=1)
    powers = jnp.arange(blocks, dtype=f32)
    coef = jnp.exp(-rate_c[None] * (length * powers)[:, None, None]) / wrap_c[None]
    if inline:
        others = [shifted(msg, "ctx", k) for k in range(2, blocks)]
        extra = [coef, first_w, msg] + others
        extra_specs = [
            pl.BlockSpec((blocks, modes, width), lambda j: (0, 0, j)),
            pl.BlockSpec((lookback, modes, width), lambda j: (0, 0, j)),
        ] + [lane_block(small_rows)] * (blocks - 1)
    else:
        messages = lax.all_gather(msg, "ctx")[(position - jnp.arange(blocks)) % blocks]
        before = jnp.roll(messages, -1, axis=0)
        head_long = head_products(messages, before, ft, 2, lookback, modes)
        states = (
            messages[:, state_row:state_row + modes].astype(f32)
            + messages[:, state_row + modes:state_row + 2 * modes].astype(f32)
            + jnp.sum(first_w[None] * head_long[:, :, None, :], axis=1)
        )
        incoming = jnp.sum(coef * jnp.roll(states, -1, axis=0), axis=0)
        fix = head_products(arrived[None], before[1:2], ft, 1, lookback, modes)[0]
        fix = jnp.pad(fix, ((0, 16 - lookback), (0, 0)))
        extra = [incoming, fix]
        extra_specs = [lane_block(modes), lane_block(16)]

    bm = jnp.concatenate(
        [
            jnp.zeros((groups, length - reach + 1), f32),
            medium_taps.astype(f32)[:, ::-1],
            jnp.zeros((groups, length - 1), f32),
        ],
        axis=1,
    )
    profile = jnp.sum(gains[:, :, None] * jnp.exp(-rates[:, :, None] * offsets), axis=1)
    bl = jnp.concatenate(
        [profile[:, :1], jnp.zeros((groups, length), f32), profile[:, :0:-1]], axis=1
    )
    starts = (gains[None] * jnp.exp(-rates[None] * (offsets + 1.0)[:, None, None])).reshape(
        length, groups * modes
    )
    ech, ecl = split_glue(starts)
    tm, tlh, tll = pl.pallas_call(
        toeplitz_kernel,
        grid=(steps,),
        in_specs=[pl.BlockSpec((gpb, 2 * length), lambda j: (j, 0))] * 2
        + [lane_block(small_rows)],
        out_specs=[
            pl.BlockSpec((gpb, length, 2 * length), lambda j: (j, 0, 0)),
            pl.BlockSpec((gpb, length, length), lambda j: (j, 0, 0)),
            pl.BlockSpec((gpb, length, length), lambda j: (j, 0, 0)),
        ],
        out_shape=[
            jax.ShapeDtypeStruct((groups, length, 2 * length), bf16),
            jax.ShapeDtypeStruct((groups, length, length), bf16),
            jax.ShapeDtypeStruct((groups, length, length), bf16),
        ],
        cost_estimate=pl.CostEstimate(
            flops=groups * length * length * 8,
            transcendentals=0,
            bytes_accessed=groups * length * length * 8,
        ),
    )(bm, bl, msg)

    outs = pl.pallas_call(
        functools.partial(mix_kernel, lookback=lookback, modes=modes, group_width=group_width,
                          inline=inline, blocks=blocks, tail=tail),
        grid=(steps,),
        in_specs=[
            proj_block,
            proj_block,
            proj_block,
            lane_block(full_rows),
            taps_block,
            lane_block(short_count),
            pl.BlockSpec((gpb, length, 2 * length), lambda j: (j, 0, 0)),
            pl.BlockSpec((gpb, length, length), lambda j: (j, 0, 0)),
            pl.BlockSpec((gpb, length, length), lambda j: (j, 0, 0)),
            pl.BlockSpec((length, gpb * modes), lambda j: (0, j)),
            pl.BlockSpec((length, gpb * modes), lambda j: (0, j)),
        ] + extra_specs,
        out_specs=[lane_block(length)] * 3,
        out_shape=[jax.ShapeDtypeStruct((length, channels), bf16)] * 3,
        scratch_shapes=[
            pltpu.VMEM((length, TILE), f32),
            pltpu.VMEM((2 * length, TILE), bf16),
        ],
        cost_estimate=pl.CostEstimate(
            flops=groups * length * TILE * length * 10,
            transcendentals=0,
            bytes_accessed=groups * length * length * 8 + length * channels * 24,
        ),
    )(short_proj, medium_proj, long_proj, arrived, feature_taps, st, tm, tlh, tll, ech, ecl, *extra)
    return tuple(outs)


def solution(mesh):
    return jax.shard_map(
        on_device,
        mesh=mesh,
        in_specs=(
            P(None, ("group", "ctx"), "chan"),
            P(None, ("group", "ctx"), "chan"),
            P(None, ("group", "ctx"), "chan"),
            P(None, None, None, "chan"),
            P(None, "chan"),
            P("chan", None),
            P("chan", None),
            P("chan", None),
        ),
        out_specs=(
            P(("group", "ctx"), "chan"),
            P(("group", "ctx"), "chan"),
            P(("group", "ctx"), "chan"),
        ),
        check_vma=False,
    )
```

```python
import functools

import jax
import jax.numpy as jnp
from jax import lax
from jax.experimental import pallas as pl
from jax.experimental.pallas import tpu as pltpu
from jax.sharding import PartitionSpec as P

f32 = jnp.float32
bf16 = jnp.bfloat16
TILE = 128
BLOCK = 512


def shifted(block, axis, distance):
    size = lax.axis_size(axis)
    route = [((i - distance) % size, i) for i in range(size)]
    return lax.ppermute(block, axis, route)


def split_bf16(x):
    hi = x.astype(bf16)
    return hi, (x - hi.astype(f32)).astype(bf16)


def split_glue(x):
    hi = lax.reduce_precision(x, exponent_bits=8, mantissa_bits=7)
    return hi.astype(bf16), (x - hi).astype(bf16)


KEPT = ((1, 1), (1, 2), (2, 1), (2, 2))
OTHER = ((0, 0), (0, 1), (0, 2), (1, 0), (2, 0))


def round16(x):
    return -(-x // 16) * 16


def layout(modes, lookback, tail=0):
    state_row = 0
    kept_row = 2 * modes
    head_row = kept_row + len(KEPT) * lookback
    small_rows = round16(head_row + len(KEPT) * lookback)
    msg_rows = round16(small_rows + len(OTHER) * lookback + tail)
    return state_row, kept_row, head_row, small_rows, msg_rows


def tail_slot(modes, lookback):
    return layout(modes, lookback)[3] + len(OTHER) * lookback


def rim_slot(operator, branch, modes, lookback):
    _, kept_row, _, small_rows, _ = layout(modes, lookback)
    if (operator, branch) in KEPT:
        return kept_row + KEPT.index((operator, branch)) * lookback
    return small_rows + OTHER.index((operator, branch)) * lookback


def head_slot(operator, branch, modes, lookback):
    return layout(modes, lookback)[2] + KEPT.index((operator, branch)) * lookback


def feature_rows(proj_ref, rim_ref, ft_ref, lanes, operator, branch, index, lookback, modes=0):
    src = proj_ref[index, :, lanes].astype(f32)
    number = operator * 3 + branch
    row = lax.broadcasted_iota(jnp.int32, src.shape, 0)
    result = ft_ref[operator, branch, pl.ds(0, 1), lanes].astype(f32) * src
    for back in range(1, lookback + 1):
        moved = pltpu.roll(src, back, 0)
        for t in range(back if rim_ref is not None else 0):
            rim_row = rim_ref[pl.ds(rim_slot(operator, branch, modes, lookback) + lookback + t - back, 1), lanes]
            moved = jnp.where(row == t, rim_row.astype(f32), moved)
        result = result + ft_ref[operator, branch, pl.ds(back, 1), lanes].astype(f32) * moved
    return result


def toeplitz_kernel(bm_ref, bl_ref, after_ref, tm_ref, tlh_ref, tll_ref):
    per = bm_ref.shape[0]
    rows = tm_ref.shape[1]
    width = bm_ref.shape[1]
    for gl in range(per):
        base = jnp.broadcast_to(bm_ref[pl.ds(gl, 1), :], (rows, width))
        tm_ref[gl] = pltpu.roll(base, 0, 1, stride=1, stride_axis=0).astype(bf16)
        base = jnp.broadcast_to(bl_ref[pl.ds(gl, 1), :], (rows, width))
        full = pltpu.roll(base, 0, 1, stride=1, stride_axis=0)[:, :rows]
        hi, lo = split_bf16(full)
        tlh_ref[gl] = hi
        tll_ref[gl] = lo


def pre_kernel(sp_ref, mp_ref, lp_ref, ft_ref, wsh_ref, wsl_ref, full_ref, msg_ref, msg_scr,
               *, lookback, modes, group_width, tail):
    length = sp_ref.shape[1]
    rows_per = TILE // group_width * modes
    state_row, _, _, small_rows, msg_rows = layout(modes, lookback, tail)
    projs = (sp_ref, mp_ref, lp_ref)
    for sub in range(full_ref.shape[1] // TILE):
        lanes = pl.ds(sub * TILE, TILE)
        msg_scr[...] = jnp.zeros_like(msg_scr)
        for operator in range(3):
            for branch in range(3):
                for r in range(lookback):
                    msg_scr[pl.ds(rim_slot(operator, branch, modes, lookback) + r, 1), :] = projs[operator][
                        branch, pl.ds(length - lookback + r, 1), lanes
                    ].astype(f32)
        for operator in (1, 2):
            for branch in (1, 2):
                for r in range(lookback):
                    at = head_slot(operator, branch, modes, lookback) + r
                    msg_scr[pl.ds(at, 1), :] = projs[operator][branch, pl.ds(r, 1), lanes].astype(f32)
        products = []
        for operator, proj_ref in enumerate(projs):
            k_feat = feature_rows(proj_ref, None, ft_ref, lanes, operator, 1, 1, lookback)
            v_feat = feature_rows(proj_ref, None, ft_ref, lanes, operator, 2, 2, lookback)
            products.append((k_feat * v_feat).astype(bf16))
        zs, zm, zl = products
        full_ref[pl.ds(msg_rows, length), lanes] = zm
        msg_scr[pl.ds(tail_slot(modes, lookback), tail), :] = zs.astype(f32)[length - tail:, :]
        weights = pl.ds(sub * rows_per, rows_per)
        full = jnp.dot(wsh_ref[weights, :], zl, preferred_element_type=f32) + jnp.dot(
            wsl_ref[weights, :], zl, preferred_element_type=f32
        )
        rows = lax.broadcasted_iota(jnp.int32, full.shape, 0) // modes
        lane_group = lax.broadcasted_iota(jnp.int32, full.shape, 1) // group_width
        full = jnp.where(rows == lane_group, full, 0.0)
        state = full[0:modes, :]
        for gl in range(1, rows_per // modes):
            state = state + full[gl * modes:(gl + 1) * modes, :]
        hi, lo = split_bf16(state)
        msg_scr[pl.ds(state_row, modes), :] = hi.astype(f32)
        msg_scr[pl.ds(state_row + modes, modes), :] = lo.astype(f32)
        packed = msg_scr[...].astype(bf16)
        msg_ref[:, lanes] = packed[:small_rows]
        full_ref[pl.ds(0, msg_rows), lanes] = packed


def head_rows(head_ref, before_ref, ft_ref, lanes, operator, lookback, modes):
    feats = []
    for branch in (1, 2):
        head = head_slot(operator, branch, modes, lookback)
        rim = rim_slot(operator, branch, modes, lookback)
        base = (operator * 3 + branch) * (lookback + 1)
        rows = []
        for p in range(lookback):
            total = None
            for j in range(lookback + 1):
                if p >= j:
                    src = head_ref[pl.ds(head + p - j, 1), lanes]
                else:
                    src = before_ref[pl.ds(rim + lookback + p - j, 1), lanes]
                term = ft_ref[operator, branch, pl.ds(j, 1), lanes].astype(f32) * src.astype(f32)
                total = term if total is None else total + term
            rows.append(total)
        feats.append(rows)
    return [(a * b).astype(bf16).astype(f32) for a, b in zip(*feats)]


def mix_kernel(*refs, lookback, modes, group_width, inline, blocks, tail):
    (sp_ref, mp_ref, lp_ref, in_ref, ft_ref, st_ref, tm_ref, tlh_ref, tll_ref,
     ech_ref, ecl_ref) = refs[:11]
    if inline:
        coef_ref, first_ref = refs[11:13]
        by_shift = [refs[13], in_ref] + list(refs[14:12 + blocks])
        rest = refs[12 + blocks:]
    else:
        inc_ref, fix_ref = refs[11:13]
        rest = refs[13:]
    so_ref, mo_ref, lo_ref, y_scr, zext_scr = rest
    state_row, _, _, _, msg_rows = layout(modes, lookback, tail)
    length = so_ref.shape[0]
    per = TILE // group_width
    row = lax.broadcasted_iota(jnp.int32, (length, TILE), 0)
    lane_group = lax.broadcasted_iota(jnp.int32, (length, TILE), 1) // group_width
    first = lax.broadcasted_iota(jnp.int32, (16, TILE), 0)
    for sub in range(so_ref.shape[1] // TILE):
        lanes = pl.ds(sub * TILE, TILE)
        if inline:
            incoming = None
            for k in range(blocks):
                now_ref = by_shift[k]
                head = head_rows(now_ref, by_shift[(k + 1) % blocks], ft_ref, lanes, 2, lookback, modes)
                state = now_ref[pl.ds(state_row, modes), lanes].astype(f32) + now_ref[
                    pl.ds(state_row + modes, modes), lanes
                ].astype(f32)
                for p in range(lookback):
                    state = state + first_ref[p, :, lanes] * head[p]
                term = coef_ref[(k - 1) % blocks, :, lanes] * state
                incoming = term if incoming is None else incoming + term
            fixed = head_rows(by_shift[1 % blocks], by_shift[2 % blocks], ft_ref, lanes, 1,
                              lookback, modes)
            fix = jnp.zeros((16, TILE), f32)
            for p in range(lookback):
                fix = jnp.where(first == p, fixed[p], fix)
        else:
            incoming = inc_ref[:, lanes]
            fix = fix_ref[:, lanes]
        feats = [
            [feature_rows(ref, in_ref, ft_ref, lanes, operator, branch, branch, lookback, modes)
             for branch in range(3)]
            for operator, ref in enumerate((sp_ref, mp_ref, lp_ref))
        ]
        zs, zm, zl = [(f[1] * f[2]).astype(bf16) for f in feats]

        zs = zs.astype(f32)
        y_scr[...] = zs
        y_scr[pl.ds(length - tail, tail), :] = in_ref[
            pl.ds(tail_slot(modes, lookback), tail), lanes
        ].astype(f32)
        wrapped = y_scr[...]
        conv = st_ref[pl.ds(0, 1), lanes] * zs
        for j in range(1, st_ref.shape[0]):
            back = jnp.where(row < j, pltpu.roll(wrapped, j, 0), pltpu.roll(zs, j, 0))
            conv = conv + st_ref[pl.ds(j, 1), lanes] * back
        so_ref[:, lanes] = (feats[0][0] * conv).astype(so_ref.dtype)

        zext_scr[pl.ds(0, length), :] = in_ref[pl.ds(msg_rows, length), lanes]
        zext_scr[pl.ds(0, 16), :] = jnp.where(
            first < lookback, fix, in_ref[pl.ds(msg_rows, 16), lanes].astype(f32)
        ).astype(bf16)
        zext_scr[pl.ds(length, length), :] = zm
        zext = zext_scr[...]
        acc = jnp.zeros((length, TILE), f32)
        for gl in range(per):
            part = jnp.dot(tm_ref[sub * per + gl], zext, preferred_element_type=f32)
            acc = jnp.where(lane_group == gl, part, acc)
        mo_ref[:, lanes] = (feats[1][0] * acc).astype(mo_ref.dtype)

        acc = jnp.zeros((length, TILE), f32)
        for gl in range(per):
            part = jnp.dot(tlh_ref[sub * per + gl], zl, preferred_element_type=f32) + jnp.dot(
                tll_ref[sub * per + gl], zl, preferred_element_type=f32
            )
            acc = jnp.where(lane_group == gl, part, acc)
        stacked = jnp.concatenate([incoming] * per, axis=0)
        srow = lax.broadcasted_iota(jnp.int32, stacked.shape, 0) // modes
        slane = lax.broadcasted_iota(jnp.int32, stacked.shape, 1) // group_width
        stacked = jnp.where(srow == slane, stacked, 0.0)
        ih, il = split_bf16(stacked)
        eh = ech_ref[:, lanes]
        el = ecl_ref[:, lanes]
        carried = (
            jnp.dot(eh, ih, preferred_element_type=f32)
            + jnp.dot(eh, il, preferred_element_type=f32)
            + jnp.dot(el, ih, preferred_element_type=f32)
        )
        lo_ref[:, lanes] = (feats[2][0] * (acc + carried)).astype(lo_ref.dtype)


def head_products(messages, before, ft, operator, lookback, modes):
    feats = []
    for branch in (1, 2):
        head = head_slot(operator, branch, modes, lookback)
        rim = rim_slot(operator, branch, modes, lookback)
        taps = ft[(operator * 3 + branch) * (lookback + 1):(operator * 3 + branch + 1) * (lookback + 1)]
        rows = []
        for p in range(lookback):
            total = None
            for j in range(lookback + 1):
                src = messages[:, head + p - j] if p >= j else before[:, rim + lookback + p - j]
                term = taps[j] * src.astype(f32)
                total = term if total is None else total + term
            rows.append(total)
        feats.append(jnp.stack(rows, axis=1))
    return lax.reduce_precision(feats[0] * feats[1], exponent_bits=8, mantissa_bits=7)


def on_device(short_proj, medium_proj, long_proj, feature_taps, short_taps, medium_taps,
              long_rates, long_residues):
    _, length, channels = short_proj.shape
    groups, modes = long_rates.shape
    group_width = channels // groups
    lookback = feature_taps.shape[2] - 1
    reach = medium_taps.shape[1]
    short_count = short_taps.shape[0]
    assert reach <= length and short_count <= 17 and 0 < lookback <= 4 and modes % 8 == 0
    blocks = lax.axis_size("ctx")
    position = lax.axis_index("ctx")
    inline = blocks <= 8
    width = min(BLOCK, channels)
    steps = channels // width
    gpb = width // group_width
    tail = short_count - 1
    state_row, _, _, small_rows, msg_rows = layout(modes, lookback, tail)
    full_rows = msg_rows + length

    ft = feature_taps.astype(f32).reshape(-1, channels)
    st = jnp.repeat(short_taps.astype(f32), group_width, axis=1)
    rates = long_rates
    loop_length = length * blocks
    wrap_scale = -jnp.expm1(-rates * loop_length)
    gains = long_residues * jnp.sqrt(
        -jnp.expm1(-2.0 * rates) * wrap_scale / (1.0 + jnp.exp(-rates * loop_length))
    )
    offsets = jnp.arange(length, dtype=f32)
    to_end = jnp.exp(-rates[:, :, None] * (length - 1.0 - offsets))
    late = jnp.where(offsets >= lookback, to_end, 0.0).reshape(groups * modes, length)
    wsh, wsl = split_glue(late)

    lane_block = lambda rows: pl.BlockSpec((rows, width), lambda j: (0, j))
    taps_block = pl.BlockSpec((3, 3, lookback + 1, width), lambda j: (0, 0, 0, j))
    proj_block = pl.BlockSpec((3, length, width), lambda j: (0, 0, j))
    p_lane = lambda rows: pl.BlockSpec((rows, channels), lambda j: (0, j))
    p_proj = pl.BlockSpec((3, length, channels), lambda j: (0, 0, j))
    p_taps = pl.BlockSpec((3, 3, lookback + 1, channels), lambda j: (0, 0, 0, j))
    full, msg = pl.pallas_call(
        functools.partial(pre_kernel, lookback=lookback, modes=modes, group_width=group_width,
                          tail=tail),
        grid=(1,),
        in_specs=[
            p_proj,
            p_proj,
            p_proj,
            p_taps,
            pl.BlockSpec((groups * modes, length), lambda j: (j, 0)),
            pl.BlockSpec((groups * modes, length), lambda j: (j, 0)),
        ],
        out_specs=[p_lane(full_rows), p_lane(small_rows)],
        out_shape=[
            jax.ShapeDtypeStruct((full_rows, channels), bf16),
            jax.ShapeDtypeStruct((small_rows, channels), bf16),
        ],
        scratch_shapes=[pltpu.VMEM((msg_rows, TILE), f32)],
        cost_estimate=pl.CostEstimate(
            flops=length * channels * (30 + 4 * TILE),
            transcendentals=0,
            bytes_accessed=length * channels * 22,
        ),
    )(short_proj, medium_proj, long_proj, feature_taps, wsh, wsl)

    arrived = shifted(full, "ctx", 1)
    first_w = jnp.repeat(
        jnp.transpose(to_end[:, :, :lookback], (2, 1, 0)), group_width, axis=2
    )
    rate_c = jnp.repeat(rates.T, group_width, axis=1)
    wrap_c = jnp.repeat(wrap_scale.T, group_width, axis=1)
    powers = jnp.arange(blocks, dtype=f32)
    coef = jnp.exp(-rate_c[None] * (length * powers)[:, None, None]) / wrap_c[None]
    if inline:
        others = [shifted(msg, "ctx", k) for k in range(2, blocks)]
        extra = [coef, first_w, msg] + others
        extra_specs = [
            pl.BlockSpec((blocks, modes, width), lambda j: (0, 0, j)),
            pl.BlockSpec((lookback, modes, width), lambda j: (0, 0, j)),
        ] + [lane_block(small_rows)] * (blocks - 1)
    else:
        messages = lax.all_gather(msg, "ctx")[(position - jnp.arange(blocks)) % blocks]
        before = jnp.roll(messages, -1, axis=0)
        head_long = head_products(messages, before, ft, 2, lookback, modes)
        states = (
            messages[:, state_row:state_row + modes].astype(f32)
            + messages[:, state_row + modes:state_row + 2 * modes].astype(f32)
            + jnp.sum(first_w[None] * head_long[:, :, None, :], axis=1)
        )
        incoming = jnp.sum(coef * jnp.roll(states, -1, axis=0), axis=0)
        fix = head_products(messages[1:2], before[1:2], ft, 1, lookback, modes)[0]
        fix = jnp.pad(fix, ((0, 16 - lookback), (0, 0)))
        extra = [incoming, fix]
        extra_specs = [lane_block(modes), lane_block(16)]

    bm = jnp.concatenate(
        [
            jnp.zeros((groups, length - reach + 1), f32),
            medium_taps.astype(f32)[:, ::-1],
            jnp.zeros((groups, length - 1), f32),
        ],
        axis=1,
    )
    profile = jnp.sum(gains[:, :, None] * jnp.exp(-rates[:, :, None] * offsets), axis=1)
    bl = jnp.concatenate(
        [profile[:, :1], jnp.zeros((groups, length), f32), profile[:, :0:-1]], axis=1
    )
    starts = (gains[None] * jnp.exp(-rates[None] * (offsets + 1.0)[:, None, None])).reshape(
        length, groups * modes
    )
    ech, ecl = split_glue(starts)
    tm, tlh, tll = pl.pallas_call(
        toeplitz_kernel,
        grid=(steps,),
        in_specs=[pl.BlockSpec((gpb, 2 * length), lambda j: (j, 0))] * 2
        + [lane_block(small_rows)],
        out_specs=[
            pl.BlockSpec((gpb, length, 2 * length), lambda j: (j, 0, 0)),
            pl.BlockSpec((gpb, length, length), lambda j: (j, 0, 0)),
            pl.BlockSpec((gpb, length, length), lambda j: (j, 0, 0)),
        ],
        out_shape=[
            jax.ShapeDtypeStruct((groups, length, 2 * length), bf16),
            jax.ShapeDtypeStruct((groups, length, length), bf16),
            jax.ShapeDtypeStruct((groups, length, length), bf16),
        ],
        cost_estimate=pl.CostEstimate(
            flops=groups * length * length * 8,
            transcendentals=0,
            bytes_accessed=groups * length * length * 8,
        ),
    )(bm, bl, msg)

    outs = pl.pallas_call(
        functools.partial(mix_kernel, lookback=lookback, modes=modes, group_width=group_width,
                          inline=inline, blocks=blocks, tail=tail),
        grid=(steps,),
        in_specs=[
            proj_block,
            proj_block,
            proj_block,
            lane_block(full_rows),
            taps_block,
            lane_block(short_count),
            pl.BlockSpec((gpb, length, 2 * length), lambda j: (j, 0, 0)),
            pl.BlockSpec((gpb, length, length), lambda j: (j, 0, 0)),
            pl.BlockSpec((gpb, length, length), lambda j: (j, 0, 0)),
            pl.BlockSpec((length, gpb * modes), lambda j: (0, j)),
            pl.BlockSpec((length, gpb * modes), lambda j: (0, j)),
        ] + extra_specs,
        out_specs=[lane_block(length)] * 3,
        out_shape=[jax.ShapeDtypeStruct((length, channels), bf16)] * 3,
        scratch_shapes=[
            pltpu.VMEM((length, TILE), f32),
            pltpu.VMEM((2 * length, TILE), bf16),
        ],
        cost_estimate=pl.CostEstimate(
            flops=groups * length * TILE * length * 10,
            transcendentals=0,
            bytes_accessed=groups * length * length * 8 + length * channels * 24,
        ),
    )(short_proj, medium_proj, long_proj, arrived, feature_taps, st, tm, tlh, tll, ech, ecl, *extra)
    return tuple(outs)


def solution(mesh):
    return jax.shard_map(
        on_device,
        mesh=mesh,
        in_specs=(
            P(None, ("group", "ctx"), "chan"),
            P(None, ("group", "ctx"), "chan"),
            P(None, ("group", "ctx"), "chan"),
            P(None, None, None, "chan"),
            P(None, "chan"),
            P("chan", None),
            P("chan", None),
            P("chan", None),
        ),
        out_specs=(
            P(("group", "ctx"), "chan"),
            P(("group", "ctx"), "chan"),
            P(("group", "ctx"), "chan"),
        ),
        check_vma=False,
    )
```
